32 devices in a mesh: grp: 2 (over y), seq: 8 (over z, x), outer: 2 (over core).
Axes of the slice: x: 2, y: 2, z: 4, core: 2. Of those that a mesh axis runs over, the one named last changes fastest.
Arguments:
- keys: bfloat16 [4096, 512], P(('grp', 'seq', 'outer')), parts along dimension 0, may hold values from -6 to 6
- values: bfloat16 [4096, 512], P(('grp', 'seq', 'outer')), parts along dimension 0, may hold values from -6 to 6
- queries: bfloat16 [4096, 512], P(('grp', 'seq', 'outer')), parts along dimension 0, may hold values from -6 to 6
- learn_rate: float32 [4096], P(('grp', 'seq', 'outer')), parts along dimension 0, may hold values from 0.0006629126 to 0.006629126
- w_gate: bfloat16 [1024, 512], P('grp'), parts along dimension 0, may hold values from -0.25 to 0.25
- w_up: bfloat16 [1024, 512], P('grp'), parts along dimension 0, may hold values from -0.25 to 0.25
- w_out: bfloat16 [1024, 512], P('grp'), parts along dimension 0, may hold values from -0.25 to 0.25
Outputs:
- output: bfloat16 [4096, 512], P(('grp', 'seq', 'outer')), parts along dimension 0
The draws below stay inside these ranges and needn't reach their ends.
There are 2 independent parts, one for each index of `grp`. The reference program is written for one: setup_inputs(seed, part) draws one part's arguments, and reference() takes and returns one part's arrays. A program takes and returns all parts, laid end to end along the dimension named above; each array names one. Nothing has to cross between parts.
All inputs are finite; a program needn't handle non-finite values.
Results may differ from the reference program's by a relative error of at most 0.0098.
Values may be sent and summed in bfloat16 or wider, within the bound.
No kernel may reach another device: no remote copies, remote signals or barrier semaphores. Data moves between devices by JAX's collectives and lax.ppermute only.
A program may use at most 64 MiB of HBM per device.

```python
import math
import jax
import jax.numpy as jnp
from jax import lax

D = 512
HID = 512
TOKENS = 2048


def raised(values, stream_key, source, target, shards_of, factor):
    owner, partner = [(jnp.arange(values.shape[axis_at]) // (values.shape[axis_at] // shards_of)).reshape([-1 if axis == axis_at else 1 for axis in range(values.ndim)]) for axis_at in (source, target)]
    chosen = jax.random.permutation(stream_key, shards_of)[partner]
    strong = (owner == chosen) | (owner == (partner + shards_of // 2) % shards_of)
    return jnp.where(strong, factor * values, values)


def block_scale(stream_key, extent, split, low, high):
    def one(position, shards_of):
        steps = jax.random.uniform(jax.random.fold_in(jax.random.fold_in(stream_key, 6), position), (shards_of,), jnp.float32, low / len(split), high / len(split))
        return jnp.repeat(jnp.exp(steps), extent[position] // shards_of).reshape((-1,) + (1,) * (len(extent) - position - 1))

    loudness = one(*split[0])
    for cut in split[1:]:
        loudness = loudness * one(*cut)
    return loudness


def normal_values(key, shape, deviation, limit, pieces=(), kind=jnp.bfloat16):
    factor_of = block_scale(key, shape, pieces, -0.22, 0.18) if pieces else 1.0
    entries = jax.random.normal(key, shape, jnp.float32) * deviation * factor_of
    return jnp.minimum(jnp.maximum(entries, -limit), limit).astype(kind)


def noise_with(stream_key, dims, scale, limit, cuts, heavy, dtype=jnp.bfloat16):
    entries = scale * jax.random.normal(stream_key, dims, jnp.float32)
    if cuts:
        entries = entries * block_scale(stream_key, dims, cuts, -0.22, 0.18)
    return jnp.clip(raised(entries, jax.random.fold_in(stream_key, 3), *heavy), -limit, limit).astype(dtype)


def setup_inputs(seed: int = 0, part: int = 0) -> dict:
    key_list = jax.random.split(jax.random.key(seed), 8)
    part_splits = jax.random.split(jax.random.fold_in(key_list[7], part), 8)
    keys = noise_with(part_splits[0], (TOKENS, D), 1.0, 6.0, ((0, 16),), (0, 1, 16, 2.0))
    values = noise_with(part_splits[1], (TOKENS, D), 1.0, 6.0, ((0, 16),), (0, 1, 16, 2.0))
    queries = normal_values(part_splits[2], (TOKENS, D), 1.0, 6.0, ((0, 16),))
    learn_rate = jnp.clip(jnp.exp(math.log(0.006629126) - 2.3025851 * jax.random.uniform(part_splits[3], (TOKENS,), jnp.float32) ** block_scale(part_splits[3], (TOKENS,), ((0, 16),), -0.2, 0.2)), 0.0006629126, 0.006629126)
    w_gate = normal_values(part_splits[4], (D, HID), D ** -0.5, 0.25)
    w_up = normal_values(part_splits[5], (D, HID), D ** -0.5, 0.25)
    w_out = normal_values(part_splits[6], (HID, D), HID ** -0.5, 0.25)
    return dict(keys=keys, values=values, queries=queries, learn_rate=learn_rate, w_gate=w_gate, w_up=w_up, w_out=w_out)


epsilon = 1e-06

def silu_grad(inputs):
    sigma = jax.nn.sigmoid(inputs)
    return sigma * (1.0 + inputs * (1.0 - sigma))

def renorm(weight, grads):
    old = weight.astype(jnp.float32)
    update = old + grads
    factor = jnp.sqrt(lax.optimization_barrier(jnp.mean(old * old, axis=1, keepdims=True)) + epsilon) / jnp.sqrt(lax.optimization_barrier(jnp.mean(update * update, axis=1, keepdims=True)) + epsilon)
    return (update * factor).astype(jnp.bfloat16)

def reference(keys, values, queries, learn_rate, w_gate, w_up, w_out):
    total = keys.shape[0]
    block = min(4096, total)
    number = total // block
    width = keys.shape[1]
    hidden = w_gate.shape[1]
    key_blocks = keys.reshape(number, block, width)
    value_blocks = values.reshape(number, block, width)
    rate_blocks = learn_rate.reshape(number, block)

    def accumulate(totals, blocks):
        key_block, value_block, rate_block = blocks
        gate_pre = jnp.dot(key_block, w_gate, preferred_element_type=jnp.float32)
        up_pre = jnp.dot(key_block, w_up, preferred_element_type=jnp.float32)
        activation = (jax.nn.silu(gate_pre) * up_pre).astype(jnp.bfloat16)
        scaled = (rate_block[:, None] * value_block.astype(jnp.float32)).astype(jnp.bfloat16)
        back_grad = jnp.dot(scaled, w_out.T, preferred_element_type=jnp.float32)
        d_gate = (back_grad * up_pre * silu_grad(gate_pre)).astype(jnp.bfloat16)
        d_up = (back_grad * jax.nn.silu(gate_pre)).astype(jnp.bfloat16)
        grad_gate = totals[0] + jnp.dot(key_block.T, d_gate, preferred_element_type=jnp.float32)
        grad_up = totals[1] + jnp.dot(key_block.T, d_up, preferred_element_type=jnp.float32)
        grad_out = totals[2] + jnp.dot(activation.T, scaled, preferred_element_type=jnp.float32)
        return ((grad_gate, grad_up, grad_out), None)
    start_sums = (jnp.zeros((width, hidden), jnp.float32), jnp.zeros((width, hidden), jnp.float32), jnp.zeros((hidden, width), jnp.float32))
    sums, unused = lax.scan(accumulate, start_sums, (key_blocks, value_blocks, rate_blocks))
    new_gate = renorm(w_gate, sums[0])
    new_up = renorm(w_up, sums[1])
    new_out = renorm(w_out, sums[2])

    def apply_block(query_block):
        q_gate = jnp.dot(query_block, new_gate, preferred_element_type=jnp.float32)
        q_up = jnp.dot(query_block, new_up, preferred_element_type=jnp.float32)
        q_act = (jax.nn.silu(q_gate) * q_up).astype(jnp.bfloat16)
        return jnp.dot(q_act, new_out, preferred_element_type=jnp.float32).astype(jnp.bfloat16)
    result = lax.map(apply_block, queries.reshape(number, block, width))
    return result.reshape(total, width)
```

```python
import jax
import jax.numpy as jnp
from jax import lax
from jax.sharding import PartitionSpec as P

epsilon = 1e-06
GATHER_LIMIT_BYTES = 16 * 1024 * 1024


def silu_grad(inputs):
    sigma = jax.nn.sigmoid(inputs)
    return sigma * (1.0 + inputs * (1.0 - sigma))


def renorm(weight, grads):
    old = weight.astype(jnp.float32)
    update = old + grads
    factor = jnp.sqrt(jnp.mean(old * old, axis=1, keepdims=True) + epsilon) / jnp.sqrt(
        jnp.mean(update * update, axis=1, keepdims=True) + epsilon
    )
    return (update * factor).astype(jnp.bfloat16)


contract_last = (((1,), (1,)), ((), ()))
contract_first = (((0,), (0,)), ((), ()))


def gradients(keys, scaled, w_gate, w_up, w_out):
    gate_pre = jnp.dot(keys, w_gate, preferred_element_type=jnp.float32)
    up_pre = jnp.dot(keys, w_up, preferred_element_type=jnp.float32)
    back_grad = lax.dot_general(scaled, w_out, contract_last, preferred_element_type=jnp.float32)
    activation = (jax.nn.silu(gate_pre) * up_pre).astype(jnp.bfloat16)
    d_gate = (back_grad * up_pre * silu_grad(gate_pre)).astype(jnp.bfloat16)
    d_up = (back_grad * jax.nn.silu(gate_pre)).astype(jnp.bfloat16)
    both_grads = jnp.concatenate([d_gate, d_up], axis=1)
    full_in = lax.dot_general(keys, both_grads, contract_first, preferred_element_type=jnp.float32)
    full_out = lax.dot_general(activation, scaled, contract_first, preferred_element_type=jnp.float32)
    return full_in, full_out


def apply(queries, full_gate, full_up, full_out_w):
    q_gate = jnp.dot(queries, full_gate, preferred_element_type=jnp.float32)
    q_up = jnp.dot(queries, full_up, preferred_element_type=jnp.float32)
    q_act = (jax.nn.silu(q_gate) * q_up).astype(jnp.bfloat16)
    return jnp.dot(q_act, full_out_w, preferred_element_type=jnp.float32).astype(jnp.bfloat16)


def local_gather(keys, values, queries, learn_rate, w_gate, w_up, w_out):
    hidden = w_gate.shape[1]
    shards = lax.axis_size(("seq", "outer"))
    rows = keys.shape[0]
    width = keys.shape[1]
    scaled = (learn_rate[:, None] * values.astype(jnp.float32)).astype(jnp.bfloat16)
    both = jnp.concatenate([keys, scaled], axis=0)
    full = lax.all_gather(both, ("seq", "outer"), axis=0, tiled=True)
    full = full.reshape(shards, 2, rows, width)
    all_keys = full[:, 0].reshape(shards * rows, width)
    all_scaled = full[:, 1].reshape(shards * rows, width)
    full_in, full_out = gradients(all_keys, all_scaled, w_gate, w_up, w_out)
    new_gate = renorm(w_gate, full_in[:, :hidden])
    new_up = renorm(w_up, full_in[:, hidden:])
    new_out = renorm(w_out, full_out)
    return apply(queries, new_gate, new_up, new_out)


def local_scatter(keys, values, queries, learn_rate, w_gate, w_up, w_out):
    hidden = w_gate.shape[1]
    shards = lax.axis_size(("seq", "outer"))
    rows_gate = w_gate.shape[0] // shards
    rows_out = w_out.shape[0] // shards
    position = lax.axis_index(("seq", "outer"))
    scaled = (learn_rate[:, None] * values.astype(jnp.float32)).astype(jnp.bfloat16)
    full_in, full_out = gradients(keys, scaled, w_gate, w_up, w_out)
    grad_in = lax.psum_scatter(full_in, ("seq", "outer"), scatter_dimension=0, tiled=True)
    grad_out = lax.psum_scatter(full_out, ("seq", "outer"), scatter_dimension=0, tiled=True)
    own_gate = lax.dynamic_slice_in_dim(w_gate, position * rows_gate, rows_gate, 0)
    own_up = lax.dynamic_slice_in_dim(w_up, position * rows_gate, rows_gate, 0)
    own_out = lax.dynamic_slice_in_dim(w_out, position * rows_out, rows_out, 0)
    new_gate = renorm(own_gate, grad_in[:, :hidden])
    new_up = renorm(own_up, grad_in[:, hidden:])
    new_out = renorm(own_out, grad_out)
    full_gate, full_up, full_out_w = (
        lax.all_gather(new_gate, ("seq", "outer"), axis=0, tiled=True),
        lax.all_gather(new_up, ("seq", "outer"), axis=0, tiled=True),
        lax.all_gather(new_out, ("seq", "outer"), axis=0, tiled=True),
    )
    return apply(queries, full_gate, full_up, full_out_w)


def solution(mesh):
    placed = (
        P(("grp", "seq", "outer"), None),
        P(("grp", "seq", "outer"), None),
        P(("grp", "seq", "outer"), None),
        P(("grp", "seq", "outer")),
        P("grp", None),
        P("grp", None),
        P("grp", None),
    )
    shards = mesh.shape["seq"] * mesh.shape["outer"]

    def run(keys, values, queries, learn_rate, w_gate, w_up, w_out):
        per_part = keys.shape[0] // mesh.shape["grp"]
        gathered_bytes = 2 * per_part * keys.shape[1] * keys.dtype.itemsize
        body = local_gather if gathered_bytes <= GATHER_LIMIT_BYTES else local_scatter
        return jax.shard_map(
            body,
            mesh=mesh,
            in_specs=placed,
            out_specs=P(("grp", "seq", "outer"), None),
            check_vma=False,
        )(keys, values, queries, learn_rate, w_gate, w_up, w_out)

    del shards
    return run
```

```python
import jax
import jax.numpy as jnp
from jax import lax
from jax.sharding import PartitionSpec as P

epsilon = 1e-06
GATHER_LIMIT_BYTES = 16 * 1024 * 1024


def silu_grad(inputs):
    sigma = jax.nn.sigmoid(inputs)
    return sigma * (1.0 + inputs * (1.0 - sigma))


def renorm(weight, grads):
    old = weight.astype(jnp.float32)
    update = old + grads
    factor = jnp.sqrt(jnp.mean(old * old, axis=1, keepdims=True) + epsilon) / jnp.sqrt(
        jnp.mean(update * update, axis=1, keepdims=True) + epsilon
    )
    return (update * factor).astype(jnp.bfloat16)


contract_last = (((1,), (1,)), ((), ()))
contract_first = (((0,), (0,)), ((), ()))


def gradients(keys, scaled, w_gate, w_up, w_out):
    gate_pre = jnp.dot(keys, w_gate, preferred_element_type=jnp.float32)
    up_pre = jnp.dot(keys, w_up, preferred_element_type=jnp.float32)
    back_grad = lax.dot_general(scaled, w_out, contract_last, preferred_element_type=jnp.float32)
    activation = (jax.nn.silu(gate_pre) * up_pre).astype(jnp.bfloat16)
    d_gate = (back_grad * up_pre * silu_grad(gate_pre)).astype(jnp.bfloat16)
    d_up = (back_grad * jax.nn.silu(gate_pre)).astype(jnp.bfloat16)
    both_grads = jnp.concatenate([d_gate, d_up], axis=1)
    full_in = lax.dot_general(keys, both_grads, contract_first, preferred_element_type=jnp.float32)
    full_out = lax.dot_general(activation, scaled, contract_first, preferred_element_type=jnp.float32)
    return full_in, full_out


def apply(queries, full_gate, full_up, full_out_w):
    q_gate = jnp.dot(queries, full_gate, preferred_element_type=jnp.float32)
    q_up = jnp.dot(queries, full_up, preferred_element_type=jnp.float32)
    q_act = (jax.nn.silu(q_gate) * q_up).astype(jnp.bfloat16)
    return jnp.dot(q_act, full_out_w, preferred_element_type=jnp.float32).astype(jnp.bfloat16)


def local_gather(keys, values, queries, learn_rate, w_gate, w_up, w_out):
    hidden = w_gate.shape[1]
    shards = lax.axis_size(("seq", "outer"))
    rows = keys.shape[0]
    width = keys.shape[1]
    scaled = (learn_rate[:, None] * values.astype(jnp.float32)).astype(jnp.bfloat16)
    both = jnp.concatenate([keys, scaled], axis=0)
    full = lax.all_gather(both, ("seq", "outer"), axis=0, tiled=True)
    full = full.reshape(shards, 2, rows, width)
    all_keys = full[:, 0].reshape(shards * rows, width)
    all_scaled = full[:, 1].reshape(shards * rows, width)
    full_in, full_out = gradients(all_keys, all_scaled, w_gate, w_up, w_out)
    new_gate = renorm(w_gate, full_in[:, :hidden])
    new_up = renorm(w_up, full_in[:, hidden:])
    new_out = renorm(w_out, full_out)
    return apply(queries, new_gate, new_up, new_out)


def local_scatter(keys, values, queries, learn_rate, w_gate, w_up, w_out):
    hidden = w_gate.shape[1]
    shards = lax.axis_size(("seq", "outer"))
    rows_gate = w_gate.shape[0] // shards
    rows_out = w_out.shape[0] // shards
    position = lax.axis_index(("seq", "outer"))
    scaled = (learn_rate[:, None] * values.astype(jnp.float32)).astype(jnp.bfloat16)
    full_in, full_out = gradients(keys, scaled, w_gate, w_up, w_out)
    grad_in = lax.psum_scatter(full_in, ("seq", "outer"), scatter_dimension=0, tiled=True)
    grad_out = lax.psum_scatter(full_out, ("seq", "outer"), scatter_dimension=0, tiled=True)
    own_gate = lax.dynamic_slice_in_dim(w_gate, position * rows_gate, rows_gate, 0)
    own_up = lax.dynamic_slice_in_dim(w_up, position * rows_gate, rows_gate, 0)
    own_out = lax.dynamic_slice_in_dim(w_out, position * rows_out, rows_out, 0)
    new_gate = renorm(own_gate, grad_in[:, :hidden])
    new_up = renorm(own_up, grad_in[:, hidden:])
    new_out = renorm(own_out, grad_out)
    full_gate, full_up, full_out_w = (
        lax.all_gather(new_gate, ("seq", "outer"), axis=0, tiled=True),
        lax.all_gather(new_up, ("seq", "outer"), axis=0, tiled=True),
        lax.all_gather(new_out, ("seq", "outer"), axis=0, tiled=True),
    )
    return apply(queries, full_gate, full_up, full_out_w)


def chip_ring(mesh):
    seq = mesh.shape["seq"]
    try:
        places = [tuple(mesh.devices[0, s, 0].coords) for s in range(seq)]
    except (AttributeError, TypeError):
        return None
    columns = sorted({p[0] for p in places})
    if len(columns) != 2 or len({p[1] for p in places}) != 1:
        return None
    first = sorted((p[2], s) for s, p in enumerate(places) if p[0] == columns[0])
    second = sorted((p[2], s) for s, p in enumerate(places) if p[0] == columns[1])
    return [s for _, s in first] + [s for _, s in reversed(second)]


def add_grads(total, keys_part, scaled_part, w_gate, w_up, w_out):
    full_in, full_out = gradients(keys_part, scaled_part, w_gate, w_up, w_out)
    if total is None:
        return full_in, full_out
    return total[0] + full_in, total[1] + full_out


def make_local_ring(ring):
    chips = len(ring)
    cw_perm = []
    ccw_perm = []
    for p in range(chips):
        for c in range(2):
            cw_perm.append((ring[p] * 2 + c, ring[(p + 1) % chips] * 2 + c))
            ccw_perm.append((ring[p] * 2 + c, ring[(p - 1) % chips] * 2 + c))
    swap = [(i, i ^ 1) for i in range(chips * 2)]
    cw_steps = chips // 2
    ccw_steps = (chips - 1) // 2
    axes = ("seq", "outer")

    def split(chunks):
        rows = chunks[0].shape[0] // 2
        keys_part = jnp.concatenate([ch[:rows] for ch in chunks], axis=0)
        scaled_part = jnp.concatenate([ch[rows:] for ch in chunks], axis=0)
        return keys_part, scaled_part

    def local_ring(keys, values, queries, learn_rate, w_gate, w_up, w_out):
        hidden = w_gate.shape[1]
        scaled = (learn_rate[:, None] * values.astype(jnp.float32)).astype(jnp.bfloat16)
        own = jnp.concatenate([keys, scaled], axis=0)
        sib = lax.ppermute(own, axes, swap)
        total = add_grads(None, *split([own, sib]), w_gate, w_up, w_out)
        cw = own
        ccw = own
        for step in range(1, cw_steps + 1):
            cw = lax.ppermute(cw, axes, cw_perm)
            arrived = [cw]
            if step <= ccw_steps:
                ccw = lax.ppermute(ccw, axes, ccw_perm)
                arrived.append(ccw)
            both = jnp.concatenate(arrived, axis=0)
            sib_both = lax.ppermute(both, axes, swap)
            rows = own.shape[0]
            chunks = [both[j * rows:(j + 1) * rows] for j in range(len(arrived))]
            chunks += [sib_both[j * rows:(j + 1) * rows] for j in range(len(arrived))]
            total = add_grads(total, *split(chunks), w_gate, w_up, w_out)
        full_in, full_out = total
        new_gate = renorm(w_gate, full_in[:, :hidden])
        new_up = renorm(w_up, full_in[:, hidden:])
        new_out = renorm(w_out, full_out)
        return apply(queries, new_gate, new_up, new_out)

    return local_ring


def solution(mesh):
    placed = (
        P(("grp", "seq", "outer"), None),
        P(("grp", "seq", "outer"), None),
        P(("grp", "seq", "outer"), None),
        P(("grp", "seq", "outer")),
        P("grp", None),
        P("grp", None),
        P("grp", None),
    )
    ring = chip_ring(mesh) if mesh.shape["outer"] == 2 else None
    local_ring = make_local_ring(ring) if ring else None

    def run(keys, values, queries, learn_rate, w_gate, w_up, w_out):
        per_part = keys.shape[0] // mesh.shape["grp"]
        gathered_bytes = 2 * per_part * keys.shape[1] * keys.dtype.itemsize
        if gathered_bytes > GATHER_LIMIT_BYTES:
            body = local_scatter
        elif local_ring is not None:
            body = local_ring
        else:
            body = local_gather
        return jax.shard_map(
            body,
            mesh=mesh,
            in_specs=placed,
            out_specs=P(("grp", "seq", "outer"), None),
            check_vma=False,
        )(keys, values, queries, learn_rate, w_gate, w_up, w_out)

    return run
```

```python
import jax
import jax.numpy as jnp
from jax import lax
from jax.sharding import PartitionSpec as P

epsilon = 1e-06
GATHER_LIMIT_BYTES = 16 * 1024 * 1024


def silu_grad(inputs):
    sigma = jax.nn.sigmoid(inputs)
    return sigma * (1.0 + inputs * (1.0 - sigma))


def renorm(weight, grads):
    old = weight.astype(jnp.float32)
    update = old + grads
    factor = jnp.sqrt(jnp.mean(old * old, axis=1, keepdims=True) + epsilon) / jnp.sqrt(
        jnp.mean(update * update, axis=1, keepdims=True) + epsilon
    )
    return (update * factor).astype(jnp.bfloat16)


contract_last = (((1,), (1,)), ((), ()))
contract_first = (((0,), (0,)), ((), ()))


def gradients(keys, scaled, w_gate, w_up, w_out):
    gate_pre = jnp.dot(keys, w_gate, preferred_element_type=jnp.float32)
    up_pre = jnp.dot(keys, w_up, preferred_element_type=jnp.float32)
    back_grad = lax.dot_general(scaled, w_out, contract_last, preferred_element_type=jnp.float32)
    activation = (jax.nn.silu(gate_pre) * up_pre).astype(jnp.bfloat16)
    d_gate = (back_grad * up_pre * silu_grad(gate_pre)).astype(jnp.bfloat16)
    d_up = (back_grad * jax.nn.silu(gate_pre)).astype(jnp.bfloat16)
    both_grads = jnp.concatenate([d_gate, d_up], axis=1)
    full_in = lax.dot_general(keys, both_grads, contract_first, preferred_element_type=jnp.float32)
    full_out = lax.dot_general(activation, scaled, contract_first, preferred_element_type=jnp.float32)
    return full_in, full_out


def apply(queries, full_gate, full_up, full_out_w):
    q_gate = jnp.dot(queries, full_gate, preferred_element_type=jnp.float32)
    q_up = jnp.dot(queries, full_up, preferred_element_type=jnp.float32)
    q_act = (jax.nn.silu(q_gate) * q_up).astype(jnp.bfloat16)
    return jnp.dot(q_act, full_out_w, preferred_element_type=jnp.float32).astype(jnp.bfloat16)


def local_gather(keys, values, queries, learn_rate, w_gate, w_up, w_out):
    hidden = w_gate.shape[1]
    shards = lax.axis_size(("seq", "outer"))
    rows = keys.shape[0]
    width = keys.shape[1]
    scaled = (learn_rate[:, None] * values.astype(jnp.float32)).astype(jnp.bfloat16)
    both = jnp.concatenate([keys, scaled], axis=0)
    full = lax.all_gather(both, ("seq", "outer"), axis=0, tiled=True)
    full = full.reshape(shards, 2, rows, width)
    all_keys = full[:, 0].reshape(shards * rows, width)
    all_scaled = full[:, 1].reshape(shards * rows, width)
    full_in, full_out = gradients(all_keys, all_scaled, w_gate, w_up, w_out)
    new_gate = renorm(w_gate, full_in[:, :hidden])
    new_up = renorm(w_up, full_in[:, hidden:])
    new_out = renorm(w_out, full_out)
    return apply(queries, new_gate, new_up, new_out)


def local_scatter(keys, values, queries, learn_rate, w_gate, w_up, w_out):
    hidden = w_gate.shape[1]
    shards = lax.axis_size(("seq", "outer"))
    rows_gate = w_gate.shape[0] // shards
    rows_out = w_out.shape[0] // shards
    position = lax.axis_index(("seq", "outer"))
    scaled = (learn_rate[:, None] * values.astype(jnp.float32)).astype(jnp.bfloat16)
    full_in, full_out = gradients(keys, scaled, w_gate, w_up, w_out)
    grad_in = lax.psum_scatter(full_in, ("seq", "outer"), scatter_dimension=0, tiled=True)
    grad_out = lax.psum_scatter(full_out, ("seq", "outer"), scatter_dimension=0, tiled=True)
    own_gate = lax.dynamic_slice_in_dim(w_gate, position * rows_gate, rows_gate, 0)
    own_up = lax.dynamic_slice_in_dim(w_up, position * rows_gate, rows_gate, 0)
    own_out = lax.dynamic_slice_in_dim(w_out, position * rows_out, rows_out, 0)
    new_gate = renorm(own_gate, grad_in[:, :hidden])
    new_up = renorm(own_up, grad_in[:, hidden:])
    new_out = renorm(own_out, grad_out)
    full_gate, full_up, full_out_w = (
        lax.all_gather(new_gate, ("seq", "outer"), axis=0, tiled=True),
        lax.all_gather(new_up, ("seq", "outer"), axis=0, tiled=True),
        lax.all_gather(new_out, ("seq", "outer"), axis=0, tiled=True),
    )
    return apply(queries, full_gate, full_up, full_out_w)


def chip_ring(mesh):
    seq = mesh.shape["seq"]
    try:
        places = [tuple(mesh.devices[0, s, 0].coords) for s in range(seq)]
    except (AttributeError, TypeError):
        return None
    columns = sorted({p[0] for p in places})
    if len(columns) != 2 or len({p[1] for p in places}) != 1:
        return None
    first = sorted((p[2], s) for s, p in enumerate(places) if p[0] == columns[0])
    second = sorted((p[2], s) for s, p in enumerate(places) if p[0] == columns[1])
    return [s for _, s in first] + [s for _, s in reversed(second)]


def add_grads(total, keys_part, scaled_part, w_gate, w_up, w_out):
    full_in, full_out = gradients(keys_part, scaled_part, w_gate, w_up, w_out)
    if total is None:
        return full_in, full_out
    return total[0] + full_in, total[1] + full_out


def make_local_ring(ring):
    chips = len(ring)
    cw_perm = []
    ccw_perm = []
    for p in range(chips):
        for c in range(2):
            cw_perm.append((ring[p] * 2 + c, ring[(p + 1) % chips] * 2 + c))
            ccw_perm.append((ring[p] * 2 + c, ring[(p - 1) % chips] * 2 + c))
    swap = [(i, i ^ 1) for i in range(chips * 2)]
    cw_steps = chips // 2
    ccw_steps = (chips - 1) // 2
    axes = ("seq", "outer")

    def split(chunks):
        rows = chunks[0].shape[0] // 2
        keys_part = jnp.concatenate([ch[:rows] for ch in chunks], axis=0)
        scaled_part = jnp.concatenate([ch[rows:] for ch in chunks], axis=0)
        return keys_part, scaled_part

    def local_ring(keys, values, queries, learn_rate, w_gate, w_up, w_out):
        hidden = w_gate.shape[1]
        scaled = (learn_rate[:, None] * values.astype(jnp.float32)).astype(jnp.bfloat16)
        own = jnp.concatenate([keys, scaled], axis=0)
        sib = lax.ppermute(own, axes, swap)
        total = add_grads(None, *split([own, sib]), w_gate, w_up, w_out)
        arrived = [own, own]
        for step in range(1, cw_steps + 1):
            sent = [lax.ppermute(arrived[0], axes, cw_perm)]
            if step <= ccw_steps:
                sent.append(lax.ppermute(arrived[1], axes, ccw_perm))
            arrived = sent
            from_sib = [lax.ppermute(chunk, axes, swap) for chunk in arrived]
            total = add_grads(total, *split(arrived + from_sib), w_gate, w_up, w_out)
        full_in, full_out = total
        new_gate = renorm(w_gate, full_in[:, :hidden])
        new_up = renorm(w_up, full_in[:, hidden:])
        new_out = renorm(w_out, full_out)
        return apply(queries, new_gate, new_up, new_out)

    return local_ring


def solution(mesh):
    placed = (
        P(("grp", "seq", "outer"), None),
        P(("grp", "seq", "outer"), None),
        P(("grp", "seq", "outer"), None),
        P(("grp", "seq", "outer")),
        P("grp", None),
        P("grp", None),
        P("grp", None),
    )
    ring = chip_ring(mesh) if mesh.shape["outer"] == 2 else None
    local_ring = make_local_ring(ring) if ring else None

    def run(keys, values, queries, learn_rate, w_gate, w_up, w_out):
        per_part = keys.shape[0] // mesh.shape["grp"]
        gathered_bytes = 2 * per_part * keys.shape[1] * keys.dtype.itemsize
        if gathered_bytes > GATHER_LIMIT_BYTES:
            body = local_scatter
        elif local_ring is not None:
            body = local_ring
        else:
            body = local_gather
        return jax.shard_map(
            body,
            mesh=mesh,
            in_specs=placed,
            out_specs=P(("grp", "seq", "outer"), None),
            check_vma=False,
        )(keys, values, queries, learn_rate, w_gate, w_up, w_out)

    return run
```

```python
import jax
import jax.numpy as jnp
from jax import lax
from jax.sharding import PartitionSpec as P

epsilon = 1e-06
GATHER_LIMIT_BYTES = 16 * 1024 * 1024


def silu_grad(inputs):
    sigma = jax.nn.sigmoid(inputs)
    return sigma * (1.0 + inputs * (1.0 - sigma))


def renorm(weight, grads):
    old = weight.astype(jnp.float32)
    update = old + grads
    factor = jnp.sqrt(jnp.mean(old * old, axis=1, keepdims=True) + epsilon) / jnp.sqrt(
        jnp.mean(update * update, axis=1, keepdims=True) + epsilon
    )
    return (update * factor).astype(jnp.bfloat16)


contract_last = (((1,), (1,)), ((), ()))
contract_first = (((0,), (0,)), ((), ()))


def gradients(keys, scaled, w_gate, w_up, w_out):
    gate_pre = jnp.dot(keys, w_gate, preferred_element_type=jnp.float32)
    up_pre = jnp.dot(keys, w_up, preferred_element_type=jnp.float32)
    back_grad = lax.dot_general(scaled, w_out, contract_last, preferred_element_type=jnp.float32)
    activation = (jax.nn.silu(gate_pre) * up_pre).astype(jnp.bfloat16)
    d_gate = (back_grad * up_pre * silu_grad(gate_pre)).astype(jnp.bfloat16)
    d_up = (back_grad * jax.nn.silu(gate_pre)).astype(jnp.bfloat16)
    both_grads = jnp.concatenate([d_gate, d_up], axis=1)
    full_in = lax.dot_general(keys, both_grads, contract_first, preferred_element_type=jnp.float32)
    full_out = lax.dot_general(activation, scaled, contract_first, preferred_element_type=jnp.float32)
    return full_in, full_out


def apply(queries, full_gate, full_up, full_out_w):
    q_gate = jnp.dot(queries, full_gate, preferred_element_type=jnp.float32)
    q_up = jnp.dot(queries, full_up, preferred_element_type=jnp.float32)
    q_act = (jax.nn.silu(q_gate) * q_up).astype(jnp.bfloat16)
    return jnp.dot(q_act, full_out_w, preferred_element_type=jnp.float32).astype(jnp.bfloat16)


def local_gather(keys, values, queries, learn_rate, w_gate, w_up, w_out):
    hidden = w_gate.shape[1]
    shards = lax.axis_size(("seq", "outer"))
    rows = keys.shape[0]
    width = keys.shape[1]
    scaled = (learn_rate[:, None] * values.astype(jnp.float32)).astype(jnp.bfloat16)
    both = jnp.concatenate([keys, scaled], axis=0)
    full = lax.all_gather(both, ("seq", "outer"), axis=0, tiled=True)
    full = full.reshape(shards, 2, rows, width)
    all_keys = full[:, 0].reshape(shards * rows, width)
    all_scaled = full[:, 1].reshape(shards * rows, width)
    full_in, full_out = gradients(all_keys, all_scaled, w_gate, w_up, w_out)
    new_gate = renorm(w_gate, full_in[:, :hidden])
    new_up = renorm(w_up, full_in[:, hidden:])
    new_out = renorm(w_out, full_out)
    return apply(queries, new_gate, new_up, new_out)


def local_scatter(keys, values, queries, learn_rate, w_gate, w_up, w_out):
    hidden = w_gate.shape[1]
    shards = lax.axis_size(("seq", "outer"))
    rows_gate = w_gate.shape[0] // shards
    rows_out = w_out.shape[0] // shards
    position = lax.axis_index(("seq", "outer"))
    scaled = (learn_rate[:, None] * values.astype(jnp.float32)).astype(jnp.bfloat16)
    full_in, full_out = gradients(keys, scaled, w_gate, w_up, w_out)
    grad_in = lax.psum_scatter(full_in, ("seq", "outer"), scatter_dimension=0, tiled=True)
    grad_out = lax.psum_scatter(full_out, ("seq", "outer"), scatter_dimension=0, tiled=True)
    own_gate = lax.dynamic_slice_in_dim(w_gate, position * rows_gate, rows_gate, 0)
    own_up = lax.dynamic_slice_in_dim(w_up, position * rows_gate, rows_gate, 0)
    own_out = lax.dynamic_slice_in_dim(w_out, position * rows_out, rows_out, 0)
    new_gate = renorm(own_gate, grad_in[:, :hidden])
    new_up = renorm(own_up, grad_in[:, hidden:])
    new_out = renorm(own_out, grad_out)
    full_gate, full_up, full_out_w = (
        lax.all_gather(new_gate, ("seq", "outer"), axis=0, tiled=True),
        lax.all_gather(new_up, ("seq", "outer"), axis=0, tiled=True),
        lax.all_gather(new_out, ("seq", "outer"), axis=0, tiled=True),
    )
    return apply(queries, full_gate, full_up, full_out_w)


def chip_ring(mesh):
    seq = mesh.shape["seq"]
    try:
        places = [tuple(mesh.devices[0, s, 0].coords) for s in range(seq)]
    except (AttributeError, TypeError):
        return None
    columns = sorted({p[0] for p in places})
    if len(columns) != 2 or len({p[1] for p in places}) != 1:
        return None
    first = sorted((p[2], s) for s, p in enumerate(places) if p[0] == columns[0])
    second = sorted((p[2], s) for s, p in enumerate(places) if p[0] == columns[1])
    return [s for _, s in first] + [s for _, s in reversed(second)]


def add_grads(total, keys_part, scaled_part, w_gate, w_up, w_out):
    full_in, full_out = gradients(keys_part, scaled_part, w_gate, w_up, w_out)
    if total is None:
        return full_in, full_out
    return total[0] + full_in, total[1] + full_out


def make_local_ring(ring):
    chips = len(ring)
    cw_perm = []
    ccw_perm = []
    for p in range(chips):
        for c in range(2):
            cw_perm.append((ring[p] * 2 + c, ring[(p + 1) % chips] * 2 + c))
            ccw_perm.append((ring[p] * 2 + c, ring[(p - 1) % chips] * 2 + c))
    swap = [(i, i ^ 1) for i in range(chips * 2)]
    steps = chips // 2
    axes = ("seq", "outer")

    def split(chunks, half):
        keys_parts = []
        scaled_parts = []
        for ch in chunks:
            for j in range(ch.shape[0] // (2 * half)):
                keys_parts.append(ch[2 * j * half:(2 * j + 1) * half])
                scaled_parts.append(ch[(2 * j + 1) * half:(2 * j + 2) * half])
        return jnp.concatenate(keys_parts, axis=0), jnp.concatenate(scaled_parts, axis=0)

    def local_ring(keys, values, queries, learn_rate, w_gate, w_up, w_out):
        hidden = w_gate.shape[1]
        rows = keys.shape[0]
        halves = 2 if rows % 16 == 0 else 1
        half = rows // halves
        scaled = (learn_rate[:, None] * values.astype(jnp.float32)).astype(jnp.bfloat16)
        pieces = []
        for j in range(halves):
            pieces += [keys[j * half:(j + 1) * half], scaled[j * half:(j + 1) * half]]
        own = jnp.concatenate(pieces, axis=0)
        sib = lax.ppermute(own, axes, swap)
        total = add_grads(None, *split([own, sib], half), w_gate, w_up, w_out)
        arrived = [own, own]
        for step in range(1, steps + 1):
            last = step == steps and chips % 2 == 0
            if last and halves == 2:
                sent = [lax.ppermute(arrived[0][:2 * half], axes, cw_perm),
                        lax.ppermute(arrived[1][2 * half:], axes, ccw_perm)]
            elif last:
                sent = [lax.ppermute(arrived[0], axes, cw_perm)]
            else:
                sent = [lax.ppermute(arrived[0], axes, cw_perm),
                        lax.ppermute(arrived[1], axes, ccw_perm)]
            arrived = sent
            from_sib = [lax.ppermute(chunk, axes, swap) for chunk in arrived]
            total = add_grads(total, *split(arrived + from_sib, half), w_gate, w_up, w_out)
        full_in, full_out = total
        new_gate = renorm(w_gate, full_in[:, :hidden])
        new_up = renorm(w_up, full_in[:, hidden:])
        new_out = renorm(w_out, full_out)
        return apply(queries, new_gate, new_up, new_out)

    return local_ring


def solution(mesh):
    placed = (
        P(("grp", "seq", "outer"), None),
        P(("grp", "seq", "outer"), None),
        P(("grp", "seq", "outer"), None),
        P(("grp", "seq", "outer")),
        P("grp", None),
        P("grp", None),
        P("grp", None),
    )
    ring = chip_ring(mesh) if mesh.shape["outer"] == 2 else None
    local_ring = make_local_ring(ring) if ring else None

    def run(keys, values, queries, learn_rate, w_gate, w_up, w_out):
        per_part = keys.shape[0] // mesh.shape["grp"]
        gathered_bytes = 2 * per_part * keys.shape[1] * keys.dtype.itemsize
        if gathered_bytes > GATHER_LIMIT_BYTES:
            body = local_scatter
        elif local_ring is not None:
            body = local_ring
        else:
            body = local_gather
        return jax.shard_map(
            body,
            mesh=mesh,
            in_specs=placed,
            out_specs=P(("grp", "seq", "outer"), None),
            check_vma=False,
        )(keys, values, queries, learn_rate, w_gate, w_up, w_out)

    return run
```

```python
import jax
import jax.numpy as jnp
from jax import lax
from jax.sharding import PartitionSpec as P

epsilon = 1e-06
GATHER_LIMIT_BYTES = 16 * 1024 * 1024


def silu_grad(inputs):
    sigma = jax.nn.sigmoid(inputs)
    return sigma * (1.0 + inputs * (1.0 - sigma))


def renorm(weight, grads):
    old = weight.astype(jnp.float32)
    update = old + grads
    factor = jnp.sqrt(jnp.mean(old * old, axis=1, keepdims=True) + epsilon) / jnp.sqrt(
        jnp.mean(update * update, axis=1, keepdims=True) + epsilon
    )
    return (update * factor).astype(jnp.bfloat16)


contract_last = (((1,), (1,)), ((), ()))
contract_first = (((0,), (0,)), ((), ()))


def gradients(keys, scaled, w_gate, w_up, w_out):
    gate_pre = jnp.dot(keys, w_gate, preferred_element_type=jnp.float32)
    up_pre = jnp.dot(keys, w_up, preferred_element_type=jnp.float32)
    back_grad = lax.dot_general(scaled, w_out, contract_last, preferred_element_type=jnp.float32)
    activation = (jax.nn.silu(gate_pre) * up_pre).astype(jnp.bfloat16)
    d_gate = (back_grad * up_pre * silu_grad(gate_pre)).astype(jnp.bfloat16)
    d_up = (back_grad * jax.nn.silu(gate_pre)).astype(jnp.bfloat16)
    both_grads = jnp.concatenate([d_gate, d_up], axis=1)
    full_in = lax.dot_general(keys, both_grads, contract_first, preferred_element_type=jnp.float32)
    full_out = lax.dot_general(activation, scaled, contract_first, preferred_element_type=jnp.float32)
    return full_in, full_out


def apply(queries, full_gate, full_up, full_out_w):
    q_gate = jnp.dot(queries, full_gate, preferred_element_type=jnp.float32)
    q_up = jnp.dot(queries, full_up, preferred_element_type=jnp.float32)
    q_act = (jax.nn.silu(q_gate) * q_up).astype(jnp.bfloat16)
    return jnp.dot(q_act, full_out_w, preferred_element_type=jnp.float32).astype(jnp.bfloat16)


def local_gather(keys, values, queries, learn_rate, w_gate, w_up, w_out):
    hidden = w_gate.shape[1]
    shards = lax.axis_size(("seq", "outer"))
    rows = keys.shape[0]
    width = keys.shape[1]
    scaled = (learn_rate[:, None] * values.astype(jnp.float32)).astype(jnp.bfloat16)
    both = jnp.concatenate([keys, scaled], axis=0)
    full = lax.all_gather(both, ("seq", "outer"), axis=0, tiled=True)
    full = full.reshape(shards, 2, rows, width)
    all_keys = full[:, 0].reshape(shards * rows, width)
    all_scaled = full[:, 1].reshape(shards * rows, width)
    full_in, full_out = gradients(all_keys, all_scaled, w_gate, w_up, w_out)
    new_gate = renorm(w_gate, full_in[:, :hidden])
    new_up = renorm(w_up, full_in[:, hidden:])
    new_out = renorm(w_out, full_out)
    return apply(queries, new_gate, new_up, new_out)


def local_scatter(keys, values, queries, learn_rate, w_gate, w_up, w_out):
    hidden = w_gate.shape[1]
    shards = lax.axis_size(("seq", "outer"))
    rows_gate = w_gate.shape[0] // shards
    rows_out = w_out.shape[0] // shards
    position = lax.axis_index(("seq", "outer"))
    scaled = (learn_rate[:, None] * values.astype(jnp.float32)).astype(jnp.bfloat16)
    full_in, full_out = gradients(keys, scaled, w_gate, w_up, w_out)
    grad_in = lax.psum_scatter(full_in, ("seq", "outer"), scatter_dimension=0, tiled=True)
    grad_out = lax.psum_scatter(full_out, ("seq", "outer"), scatter_dimension=0, tiled=True)
    own_gate = lax.dynamic_slice_in_dim(w_gate, position * rows_gate, rows_gate, 0)
    own_up = lax.dynamic_slice_in_dim(w_up, position * rows_gate, rows_gate, 0)
    own_out = lax.dynamic_slice_in_dim(w_out, position * rows_out, rows_out, 0)
    new_gate = renorm(own_gate, grad_in[:, :hidden])
    new_up = renorm(own_up, grad_in[:, hidden:])
    new_out = renorm(own_out, grad_out)
    full_gate, full_up, full_out_w = (
        lax.all_gather(new_gate, ("seq", "outer"), axis=0, tiled=True),
        lax.all_gather(new_up, ("seq", "outer"), axis=0, tiled=True),
        lax.all_gather(new_out, ("seq", "outer"), axis=0, tiled=True),
    )
    return apply(queries, full_gate, full_up, full_out_w)


def chip_ring(mesh):
    seq = mesh.shape["seq"]
    try:
        places = [tuple(mesh.devices[0, s, 0].coords) for s in range(seq)]
    except (AttributeError, TypeError):
        return None
    columns = sorted({p[0] for p in places})
    if len(columns) != 2 or len({p[1] for p in places}) != 1:
        return None
    first = sorted((p[2], s) for s, p in enumerate(places) if p[0] == columns[0])
    second = sorted((p[2], s) for s, p in enumerate(places) if p[0] == columns[1])
    return [s for _, s in first] + [s for _, s in reversed(second)]


def add_grads(total, keys_part, scaled_part, w_gate, w_up, w_out):
    full_in, full_out = gradients(keys_part, scaled_part, w_gate, w_up, w_out)
    if total is None:
        return full_in, full_out
    return total[0] + full_in, total[1] + full_out


def make_local_ring(ring):
    chips = len(ring)
    cw_perm = []
    ccw_perm = []
    for p in range(chips):
        for c in range(2):
            cw_perm.append((ring[p] * 2 + c, ring[(p + 1) % chips] * 2 + c))
            ccw_perm.append((ring[p] * 2 + c, ring[(p - 1) % chips] * 2 + c))
    swap = [(i, i ^ 1) for i in range(chips * 2)]
    steps = chips // 2
    axes = ("seq", "outer")

    def split(chunks, half):
        keys_parts = []
        scaled_parts = []
        for ch in chunks:
            for j in range(ch.shape[0] // (2 * half)):
                keys_parts.append(ch[2 * j * half:(2 * j + 1) * half])
                scaled_parts.append(ch[(2 * j + 1) * half:(2 * j + 2) * half])
        return jnp.concatenate(keys_parts, axis=0), jnp.concatenate(scaled_parts, axis=0)

    def local_ring(keys, values, queries, learn_rate, w_gate, w_up, w_out):
        hidden = w_gate.shape[1]
        rows = keys.shape[0]
        halves = 2 if rows % 16 == 0 else 1
        half = rows // halves
        scaled = (learn_rate[:, None] * values.astype(jnp.float32)).astype(jnp.bfloat16)
        width = keys.shape[1]
        own = jnp.stack(
            [keys.reshape(halves, half, width), scaled.reshape(halves, half, width)], axis=1
        ).reshape(2 * rows, width)
        sib = lax.ppermute(own, axes, swap)
        total = add_grads(None, *split([own, sib], half), w_gate, w_up, w_out)
        arrived = [own, own]
        for step in range(1, steps + 1):
            last = step == steps and chips % 2 == 0
            if last and halves == 2:
                sent = [lax.ppermute(arrived[0][:2 * half], axes, cw_perm),
                        lax.ppermute(arrived[1][2 * half:], axes, ccw_perm)]
            elif last:
                sent = [lax.ppermute(arrived[0], axes, cw_perm)]
            else:
                sent = [lax.ppermute(arrived[0], axes, cw_perm),
                        lax.ppermute(arrived[1], axes, ccw_perm)]
            arrived = sent
            from_sib = [lax.ppermute(chunk, axes, swap) for chunk in arrived]
            total = add_grads(total, *split(arrived + from_sib, half), w_gate, w_up, w_out)
        full_in, full_out = total
        new_gate = renorm(w_gate, full_in[:, :hidden])
        new_up = renorm(w_up, full_in[:, hidden:])
        new_out = renorm(w_out, full_out)
        new_gate, new_up, new_out = lax.optimization_barrier((new_gate, new_up, new_out))
        return apply(queries, new_gate, new_up, new_out)

    return local_ring


def solution(mesh):
    placed = (
        P(("grp", "seq", "outer"), None),
        P(("grp", "seq", "outer"), None),
        P(("grp", "seq", "outer"), None),
        P(("grp", "seq", "outer")),
        P("grp", None),
        P("grp", None),
        P("grp", None),
    )
    ring = chip_ring(mesh) if mesh.shape["outer"] == 2 else None
    local_ring = make_local_ring(ring) if ring else None

    def run(keys, values, queries, learn_rate, w_gate, w_up, w_out):
        per_part = keys.shape[0] // mesh.shape["grp"]
        gathered_bytes = 2 * per_part * keys.shape[1] * keys.dtype.itemsize
        if gathered_bytes > GATHER_LIMIT_BYTES:
            body = local_scatter
        elif local_ring is not None:
            body = local_ring
        else:
            body = local_gather
        return jax.shard_map(
            body,
            mesh=mesh,
            in_specs=placed,
            out_specs=P(("grp", "seq", "outer"), None),
            check_vma=False,
        )(keys, values, queries, learn_rate, w_gate, w_up, w_out)

    return run
```

```python
import jax
import jax.numpy as jnp
from jax import lax
from jax.sharding import PartitionSpec as P

epsilon = 1e-06
GATHER_LIMIT_BYTES = 16 * 1024 * 1024


def silu_grad(inputs):
    sigma = jax.nn.sigmoid(inputs)
    return sigma * (1.0 + inputs * (1.0 - sigma))


def renorm(weight, grads):
    old = weight.astype(jnp.float32)
    update = old + grads
    factor = jnp.sqrt(jnp.mean(old * old, axis=1, keepdims=True) + epsilon) / jnp.sqrt(
        jnp.mean(update * update, axis=1, keepdims=True) + epsilon
    )
    return (update * factor).astype(jnp.bfloat16)


contract_last = (((1,), (1,)), ((), ()))
contract_first = (((0,), (0,)), ((), ()))


def gradients(keys, scaled, w_gate, w_up, w_out):
    gate_pre = jnp.dot(keys, w_gate, preferred_element_type=jnp.float32)
    up_pre = jnp.dot(keys, w_up, preferred_element_type=jnp.float32)
    back_grad = lax.dot_general(scaled, w_out, contract_last, preferred_element_type=jnp.float32)
    activation = (jax.nn.silu(gate_pre) * up_pre).astype(jnp.bfloat16)
    d_gate = (back_grad * up_pre * silu_grad(gate_pre)).astype(jnp.bfloat16)
    d_up = (back_grad * jax.nn.silu(gate_pre)).astype(jnp.bfloat16)
    both_grads = jnp.concatenate([d_gate, d_up], axis=1)
    full_in = lax.dot_general(keys, both_grads, contract_first, preferred_element_type=jnp.float32)
    full_out = lax.dot_general(activation, scaled, contract_first, preferred_element_type=jnp.float32)
    return full_in, full_out


def apply(queries, full_gate, full_up, full_out_w):
    q_gate = jnp.dot(queries, full_gate, preferred_element_type=jnp.float32)
    q_up = jnp.dot(queries, full_up, preferred_element_type=jnp.float32)
    q_act = (jax.nn.silu(q_gate) * q_up).astype(jnp.bfloat16)
    return jnp.dot(q_act, full_out_w, preferred_element_type=jnp.float32).astype(jnp.bfloat16)


def local_gather(keys, values, queries, learn_rate, w_gate, w_up, w_out):
    hidden = w_gate.shape[1]
    shards = lax.axis_size(("seq", "outer"))
    rows = keys.shape[0]
    width = keys.shape[1]
    scaled = (learn_rate[:, None] * values.astype(jnp.float32)).astype(jnp.bfloat16)
    both = jnp.concatenate([keys, scaled], axis=0)
    full = lax.all_gather(both, ("seq", "outer"), axis=0, tiled=True)
    full = full.reshape(shards, 2, rows, width)
    all_keys = full[:, 0].reshape(shards * rows, width)
    all_scaled = full[:, 1].reshape(shards * rows, width)
    full_in, full_out = gradients(all_keys, all_scaled, w_gate, w_up, w_out)
    new_gate = renorm(w_gate, full_in[:, :hidden])
    new_up = renorm(w_up, full_in[:, hidden:])
    new_out = renorm(w_out, full_out)
    return apply(queries, new_gate, new_up, new_out)


def local_scatter(keys, values, queries, learn_rate, w_gate, w_up, w_out):
    hidden = w_gate.shape[1]
    shards = lax.axis_size(("seq", "outer"))
    rows_gate = w_gate.shape[0] // shards
    rows_out = w_out.shape[0] // shards
    position = lax.axis_index(("seq", "outer"))
    scaled = (learn_rate[:, None] * values.astype(jnp.float32)).astype(jnp.bfloat16)
    full_in, full_out = gradients(keys, scaled, w_gate, w_up, w_out)
    grad_in = lax.psum_scatter(full_in, ("seq", "outer"), scatter_dimension=0, tiled=True)
    grad_out = lax.psum_scatter(full_out, ("seq", "outer"), scatter_dimension=0, tiled=True)
    own_gate = lax.dynamic_slice_in_dim(w_gate, position * rows_gate, rows_gate, 0)
    own_up = lax.dynamic_slice_in_dim(w_up, position * rows_gate, rows_gate, 0)
    own_out = lax.dynamic_slice_in_dim(w_out, position * rows_out, rows_out, 0)
    new_gate = renorm(own_gate, grad_in[:, :hidden])
    new_up = renorm(own_up, grad_in[:, hidden:])
    new_out = renorm(own_out, grad_out)
    full_gate, full_up, full_out_w = (
        lax.all_gather(new_gate, ("seq", "outer"), axis=0, tiled=True),
        lax.all_gather(new_up, ("seq", "outer"), axis=0, tiled=True),
        lax.all_gather(new_out, ("seq", "outer"), axis=0, tiled=True),
    )
    return apply(queries, full_gate, full_up, full_out_w)


def chip_ring(mesh):
    seq = mesh.shape["seq"]
    try:
        places = [tuple(mesh.devices[0, s, 0].coords) for s in range(seq)]
    except (AttributeError, TypeError):
        return None
    columns = sorted({p[0] for p in places})
    if len(columns) != 2 or len({p[1] for p in places}) != 1:
        return None
    first = sorted((p[2], s) for s, p in enumerate(places) if p[0] == columns[0])
    second = sorted((p[2], s) for s, p in enumerate(places) if p[0] == columns[1])
    return [s for _, s in first] + [s for _, s in reversed(second)]


def add_grads(total, keys_part, scaled_part, w_gate, w_up, w_out):
    full_in, full_out = gradients(keys_part, scaled_part, w_gate, w_up, w_out)
    if total is None:
        return full_in, full_out
    return total[0] + full_in, total[1] + full_out


def make_local_ring(ring):
    chips = len(ring)
    cw_perm = []
    ccw_perm = []
    for p in range(chips):
        for c in range(2):
            cw_perm.append((ring[p] * 2 + c, ring[(p + 1) % chips] * 2 + c))
            ccw_perm.append((ring[p] * 2 + c, ring[(p - 1) % chips] * 2 + c))
    swap = [(i, i ^ 1) for i in range(chips * 2)]
    steps = chips // 2
    axes = ("seq", "outer")

    def split(chunks, half):
        keys_parts = []
        scaled_parts = []
        for ch in chunks:
            for j in range(ch.shape[0] // (2 * half)):
                keys_parts.append(ch[2 * j * half:(2 * j + 1) * half])
                scaled_parts.append(ch[(2 * j + 1) * half:(2 * j + 2) * half])
        return jnp.concatenate(keys_parts, axis=0), jnp.concatenate(scaled_parts, axis=0)

    def local_ring(keys, values, queries, learn_rate, w_gate, w_up, w_out):
        hidden = w_gate.shape[1]
        rows = keys.shape[0]
        halves = 2 if rows % 16 == 0 else 1
        half = rows // halves
        scaled = (learn_rate[:, None] * values.astype(jnp.float32)).astype(jnp.bfloat16)
        width = keys.shape[1]
        own = jnp.stack(
            [keys.reshape(halves, half, width), scaled.reshape(halves, half, width)], axis=1
        ).reshape(2 * rows, width)
        sib = lax.ppermute(own, axes, swap)
        total = add_grads(None, *split([own, sib], half), w_gate, w_up, w_out)
        arrived = [own, own]
        for step in range(1, steps + 1):
            last = step == steps and chips % 2 == 0
            if last and halves == 2:
                sent = [lax.ppermute(arrived[0][:2 * half], axes, cw_perm),
                        lax.ppermute(arrived[1][2 * half:], axes, ccw_perm)]
            elif last:
                sent = [lax.ppermute(arrived[0], axes, cw_perm)]
            else:
                sent = [lax.ppermute(arrived[0], axes, cw_perm),
                        lax.ppermute(arrived[1], axes, ccw_perm)]
            arrived = sent
            if step == steps:
                total, arrived = lax.optimization_barrier((total, arrived))
            from_sib = [lax.ppermute(chunk, axes, swap) for chunk in arrived]
            total = add_grads(total, *split(arrived + from_sib, half), w_gate, w_up, w_out)
        full_in, full_out = total
        new_gate = renorm(w_gate, full_in[:, :hidden])
        new_up = renorm(w_up, full_in[:, hidden:])
        new_out = renorm(w_out, full_out)
        new_gate, new_up, new_out = lax.optimization_barrier((new_gate, new_up, new_out))
        return apply(queries, new_gate, new_up, new_out)

    return local_ring


def solution(mesh):
    placed = (
        P(("grp", "seq", "outer"), None),
        P(("grp", "seq", "outer"), None),
        P(("grp", "seq", "outer"), None),
        P(("grp", "seq", "outer")),
        P("grp", None),
        P("grp", None),
        P("grp", None),
    )
    ring = chip_ring(mesh) if mesh.shape["outer"] == 2 else None
    local_ring = make_local_ring(ring) if ring else None

    def run(keys, values, queries, learn_rate, w_gate, w_up, w_out):
        per_part = keys.shape[0] // mesh.shape["grp"]
        gathered_bytes = 2 * per_part * keys.shape[1] * keys.dtype.itemsize
        if gathered_bytes > GATHER_LIMIT_BYTES:
            body = local_scatter
        elif local_ring is not None:
            body = local_ring
        else:
            body = local_gather
        return jax.shard_map(
            body,
            mesh=mesh,
            in_specs=placed,
            out_specs=P(("grp", "seq", "outer"), None),
            check_vma=False,
        )(keys, values, queries, learn_rate, w_gate, w_up, w_out)

    return run
```

```python
import jax
import jax.numpy as jnp
from jax import lax
from jax.sharding import PartitionSpec as P

epsilon = 1e-06
GATHER_LIMIT_BYTES = 16 * 1024 * 1024


def silu_grad(inputs):
    sigma = jax.nn.sigmoid(inputs)
    return sigma * (1.0 + inputs * (1.0 - sigma))


def renorm(weight, grads):
    old = weight.astype(jnp.float32)
    update = old + grads
    factor = jnp.sqrt(jnp.mean(old * old, axis=1, keepdims=True) + epsilon) / jnp.sqrt(
        jnp.mean(update * update, axis=1, keepdims=True) + epsilon
    )
    return (update * factor).astype(jnp.bfloat16)


contract_last = (((1,), (1,)), ((), ()))
contract_first = (((0,), (0,)), ((), ()))


def gradients(keys, scaled, w_gate, w_up, w_out):
    gate_pre = jnp.dot(keys, w_gate, preferred_element_type=jnp.float32)
    up_pre = jnp.dot(keys, w_up, preferred_element_type=jnp.float32)
    back_grad = lax.dot_general(scaled, w_out, contract_last, preferred_element_type=jnp.float32)
    activation = (jax.nn.silu(gate_pre) * up_pre).astype(jnp.bfloat16)
    d_gate = (back_grad * up_pre * silu_grad(gate_pre)).astype(jnp.bfloat16)
    d_up = (back_grad * jax.nn.silu(gate_pre)).astype(jnp.bfloat16)
    both_grads = jnp.concatenate([d_gate, d_up], axis=1)
    full_in = lax.dot_general(keys, both_grads, contract_first, preferred_element_type=jnp.float32)
    full_out = lax.dot_general(activation, scaled, contract_first, preferred_element_type=jnp.float32)
    return full_in, full_out


def apply(queries, full_gate, full_up, full_out_w):
    q_gate = jnp.dot(queries, full_gate, preferred_element_type=jnp.float32)
    q_up = jnp.dot(queries, full_up, preferred_element_type=jnp.float32)
    q_act = (jax.nn.silu(q_gate) * q_up).astype(jnp.bfloat16)
    return jnp.dot(q_act, full_out_w, preferred_element_type=jnp.float32).astype(jnp.bfloat16)


def local_gather(keys, values, queries, learn_rate, w_gate, w_up, w_out):
    hidden = w_gate.shape[1]
    shards = lax.axis_size(("seq", "outer"))
    rows = keys.shape[0]
    width = keys.shape[1]
    scaled = (learn_rate[:, None] * values.astype(jnp.float32)).astype(jnp.bfloat16)
    both = jnp.concatenate([keys, scaled], axis=0)
    full = lax.all_gather(both, ("seq", "outer"), axis=0, tiled=True)
    full = full.reshape(shards, 2, rows, width)
    all_keys = full[:, 0].reshape(shards * rows, width)
    all_scaled = full[:, 1].reshape(shards * rows, width)
    full_in, full_out = gradients(all_keys, all_scaled, w_gate, w_up, w_out)
    new_gate = renorm(w_gate, full_in[:, :hidden])
    new_up = renorm(w_up, full_in[:, hidden:])
    new_out = renorm(w_out, full_out)
    return apply(queries, new_gate, new_up, new_out)


def local_scatter(keys, values, queries, learn_rate, w_gate, w_up, w_out):
    hidden = w_gate.shape[1]
    shards = lax.axis_size(("seq", "outer"))
    rows_gate = w_gate.shape[0] // shards
    rows_out = w_out.shape[0] // shards
    position = lax.axis_index(("seq", "outer"))
    scaled = (learn_rate[:, None] * values.astype(jnp.float32)).astype(jnp.bfloat16)
    full_in, full_out = gradients(keys, scaled, w_gate, w_up, w_out)
    grad_in = lax.psum_scatter(full_in, ("seq", "outer"), scatter_dimension=0, tiled=True)
    grad_out = lax.psum_scatter(full_out, ("seq", "outer"), scatter_dimension=0, tiled=True)
    own_gate = lax.dynamic_slice_in_dim(w_gate, position * rows_gate, rows_gate, 0)
    own_up = lax.dynamic_slice_in_dim(w_up, position * rows_gate, rows_gate, 0)
    own_out = lax.dynamic_slice_in_dim(w_out, position * rows_out, rows_out, 0)
    new_gate = renorm(own_gate, grad_in[:, :hidden])
    new_up = renorm(own_up, grad_in[:, hidden:])
    new_out = renorm(own_out, grad_out)
    full_gate, full_up, full_out_w = (
        lax.all_gather(new_gate, ("seq", "outer"), axis=0, tiled=True),
        lax.all_gather(new_up, ("seq", "outer"), axis=0, tiled=True),
        lax.all_gather(new_out, ("seq", "outer"), axis=0, tiled=True),
    )
    return apply(queries, full_gate, full_up, full_out_w)


def chip_ring(mesh):
    seq = mesh.shape["seq"]
    try:
        places = [tuple(mesh.devices[0, s, 0].coords) for s in range(seq)]
    except (AttributeError, TypeError):
        return None
    columns = sorted({p[0] for p in places})
    if len(columns) != 2 or len({p[1] for p in places}) != 1:
        return None
    first = sorted((p[2], s) for s, p in enumerate(places) if p[0] == columns[0])
    second = sorted((p[2], s) for s, p in enumerate(places) if p[0] == columns[1])
    return [s for _, s in first] + [s for _, s in reversed(second)]


def add_grads(total, keys_part, scaled_part, w_gate, w_up, w_out):
    full_in, full_out = gradients(keys_part, scaled_part, w_gate, w_up, w_out)
    if total is None:
        return full_in, full_out
    return total[0] + full_in, total[1] + full_out


def make_local_ring(ring):
    chips = len(ring)
    cw_perm = []
    ccw_perm = []
    cross_perm = []
    for p in range(chips):
        for c in range(2):
            cw_perm.append((ring[p] * 2 + c, ring[(p + 1) % chips] * 2 + c))
            ccw_perm.append((ring[p] * 2 + c, ring[(p - 1) % chips] * 2 + c))
            cross_perm.append((ring[p] * 2 + c, ring[(p - 1) % chips] * 2 + 1 - c))
    swap = [(i, i ^ 1) for i in range(chips * 2)]
    steps = chips // 2
    axes = ("seq", "outer")

    def split(chunks, half):
        keys_parts = []
        scaled_parts = []
        for ch in chunks:
            for j in range(ch.shape[0] // (2 * half)):
                keys_parts.append(ch[2 * j * half:(2 * j + 1) * half])
                scaled_parts.append(ch[(2 * j + 1) * half:(2 * j + 2) * half])
        return jnp.concatenate(keys_parts, axis=0), jnp.concatenate(scaled_parts, axis=0)

    def local_ring(keys, values, queries, learn_rate, w_gate, w_up, w_out):
        hidden = w_gate.shape[1]
        rows = keys.shape[0]
        halves = 2 if rows % 16 == 0 else 1
        half = rows // halves
        scaled = (learn_rate[:, None] * values.astype(jnp.float32)).astype(jnp.bfloat16)
        width = keys.shape[1]
        own = jnp.stack(
            [keys.reshape(halves, half, width), scaled.reshape(halves, half, width)], axis=1
        ).reshape(2 * rows, width)
        sib = lax.ppermute(own, axes, swap)
        total = add_grads(None, *split([own, sib], half), w_gate, w_up, w_out)
        arrived = [own, own]
        for step in range(1, steps + 1):
            if step == steps and chips % 2 == 0:
                arrived = [lax.ppermute(arrived[0], axes, cw_perm),
                           lax.ppermute(arrived[1], axes, cross_perm)]
                total, arrived = lax.optimization_barrier((total, arrived))
                total = add_grads(total, *split(arrived, half), w_gate, w_up, w_out)
                continue
            sent = [lax.ppermute(arrived[0], axes, cw_perm)]
            if step < steps or chips % 2:
                sent.append(lax.ppermute(arrived[1], axes, ccw_perm))
            arrived = sent
            from_sib = [lax.ppermute(chunk, axes, swap) for chunk in arrived]
            total = add_grads(total, *split(arrived + from_sib, half), w_gate, w_up, w_out)
        full_in, full_out = total
        new_gate = renorm(w_gate, full_in[:, :hidden])
        new_up = renorm(w_up, full_in[:, hidden:])
        new_out = renorm(w_out, full_out)
        new_gate, new_up, new_out = lax.optimization_barrier((new_gate, new_up, new_out))
        return apply(queries, new_gate, new_up, new_out)

    return local_ring


def solution(mesh):
    placed = (
        P(("grp", "seq", "outer"), None),
        P(("grp", "seq", "outer"), None),
        P(("grp", "seq", "outer"), None),
        P(("grp", "seq", "outer")),
        P("grp", None),
        P("grp", None),
        P("grp", None),
    )
    ring = chip_ring(mesh) if mesh.shape["outer"] == 2 else None
    local_ring = make_local_ring(ring) if ring else None

    def run(keys, values, queries, learn_rate, w_gate, w_up, w_out):
        per_part = keys.shape[0] // mesh.shape["grp"]
        gathered_bytes = 2 * per_part * keys.shape[1] * keys.dtype.itemsize
        if gathered_bytes > GATHER_LIMIT_BYTES:
            body = local_scatter
        elif local_ring is not None:
            body = local_ring
        else:
            body = local_gather
        return jax.shard_map(
            body,
            mesh=mesh,
            in_specs=placed,
            out_specs=P(("grp", "seq", "outer"), None),
            check_vma=False,
        )(keys, values, queries, learn_rate, w_gate, w_up, w_out)

    return run
```

```python
import jax
import jax.numpy as jnp
from jax import lax
from jax.sharding import PartitionSpec as P

epsilon = 1e-06
GATHER_LIMIT_BYTES = 16 * 1024 * 1024


def silu_grad(inputs):
    sigma = jax.nn.sigmoid(inputs)
    return sigma * (1.0 + inputs * (1.0 - sigma))


def renorm(weight, grads):
    old = weight.astype(jnp.float32)
    update = old + grads
    factor = jnp.sqrt(jnp.mean(old * old, axis=1, keepdims=True) + epsilon) / jnp.sqrt(
        jnp.mean(update * update, axis=1, keepdims=True) + epsilon
    )
    return (update * factor).astype(jnp.bfloat16)


contract_last = (((1,), (1,)), ((), ()))
contract_first = (((0,), (0,)), ((), ()))


def gradients(keys, scaled, w_gate, w_up, w_out):
    gate_pre = jnp.dot(keys, w_gate, preferred_element_type=jnp.float32)
    up_pre = jnp.dot(keys, w_up, preferred_element_type=jnp.float32)
    back_grad = lax.dot_general(scaled, w_out, contract_last, preferred_element_type=jnp.float32)
    activation = (jax.nn.silu(gate_pre) * up_pre).astype(jnp.bfloat16)
    d_gate = (back_grad * up_pre * silu_grad(gate_pre)).astype(jnp.bfloat16)
    d_up = (back_grad * jax.nn.silu(gate_pre)).astype(jnp.bfloat16)
    both_grads = jnp.concatenate([d_gate, d_up], axis=1)
    full_in = lax.dot_general(keys, both_grads, contract_first, preferred_element_type=jnp.float32)
    full_out = lax.dot_general(activation, scaled, contract_first, preferred_element_type=jnp.float32)
    return full_in, full_out


def apply(queries, full_gate, full_up, full_out_w):
    q_gate = jnp.dot(queries, full_gate, preferred_element_type=jnp.float32)
    q_up = jnp.dot(queries, full_up, preferred_element_type=jnp.float32)
    q_act = (jax.nn.silu(q_gate) * q_up).astype(jnp.bfloat16)
    return jnp.dot(q_act, full_out_w, preferred_element_type=jnp.float32).astype(jnp.bfloat16)


def local_gather(keys, values, queries, learn_rate, w_gate, w_up, w_out):
    hidden = w_gate.shape[1]
    shards = lax.axis_size(("seq", "outer"))
    rows = keys.shape[0]
    width = keys.shape[1]
    scaled = (learn_rate[:, None] * values.astype(jnp.float32)).astype(jnp.bfloat16)
    both = jnp.concatenate([keys, scaled], axis=0)
    full = lax.all_gather(both, ("seq", "outer"), axis=0, tiled=True)
    full = full.reshape(shards, 2, rows, width)
    all_keys = full[:, 0].reshape(shards * rows, width)
    all_scaled = full[:, 1].reshape(shards * rows, width)
    full_in, full_out = gradients(all_keys, all_scaled, w_gate, w_up, w_out)
    new_gate = renorm(w_gate, full_in[:, :hidden])
    new_up = renorm(w_up, full_in[:, hidden:])
    new_out = renorm(w_out, full_out)
    return apply(queries, new_gate, new_up, new_out)


def local_scatter(keys, values, queries, learn_rate, w_gate, w_up, w_out):
    hidden = w_gate.shape[1]
    shards = lax.axis_size(("seq", "outer"))
    rows_gate = w_gate.shape[0] // shards
    rows_out = w_out.shape[0] // shards
    position = lax.axis_index(("seq", "outer"))
    scaled = (learn_rate[:, None] * values.astype(jnp.float32)).astype(jnp.bfloat16)
    full_in, full_out = gradients(keys, scaled, w_gate, w_up, w_out)
    grad_in = lax.psum_scatter(full_in, ("seq", "outer"), scatter_dimension=0, tiled=True)
    grad_out = lax.psum_scatter(full_out, ("seq", "outer"), scatter_dimension=0, tiled=True)
    own_gate = lax.dynamic_slice_in_dim(w_gate, position * rows_gate, rows_gate, 0)
    own_up = lax.dynamic_slice_in_dim(w_up, position * rows_gate, rows_gate, 0)
    own_out = lax.dynamic_slice_in_dim(w_out, position * rows_out, rows_out, 0)
    new_gate = renorm(own_gate, grad_in[:, :hidden])
    new_up = renorm(own_up, grad_in[:, hidden:])
    new_out = renorm(own_out, grad_out)
    full_gate, full_up, full_out_w = (
        lax.all_gather(new_gate, ("seq", "outer"), axis=0, tiled=True),
        lax.all_gather(new_up, ("seq", "outer"), axis=0, tiled=True),
        lax.all_gather(new_out, ("seq", "outer"), axis=0, tiled=True),
    )
    return apply(queries, full_gate, full_up, full_out_w)


def chip_ring(mesh):
    seq = mesh.shape["seq"]
    try:
        places = [tuple(mesh.devices[0, s, 0].coords) for s in range(seq)]
    except (AttributeError, TypeError):
        return None
    columns = sorted({p[0] for p in places})
    if len(columns) != 2 or len({p[1] for p in places}) != 1:
        return None
    first = sorted((p[2], s) for s, p in enumerate(places) if p[0] == columns[0])
    second = sorted((p[2], s) for s, p in enumerate(places) if p[0] == columns[1])
    return [s for _, s in first] + [s for _, s in reversed(second)]


def add_grads(total, keys_part, scaled_part, w_gate, w_up, w_out):
    full_in, full_out = gradients(keys_part, scaled_part, w_gate, w_up, w_out)
    if total is None:
        return full_in, full_out
    return total[0] + full_in, total[1] + full_out


def make_local_ring(ring):
    chips = len(ring)
    cw_perm = []
    ccw_perm = []
    for p in range(chips):
        for c in range(2):
            cw_perm.append((ring[p] * 2 + c, ring[(p + 1) % chips] * 2 + c))
            ccw_perm.append((ring[p] * 2 + c, ring[(p - 1) % chips] * 2 + c))
    swap = [(i, i ^ 1) for i in range(chips * 2)]
    steps = chips // 2
    axes = ("seq", "outer")

    def split(chunks, half):
        keys_parts = []
        scaled_parts = []
        for ch in chunks:
            for j in range(ch.shape[0] // (2 * half)):
                keys_parts.append(ch[2 * j * half:(2 * j + 1) * half])
                scaled_parts.append(ch[(2 * j + 1) * half:(2 * j + 2) * half])
        return jnp.concatenate(keys_parts, axis=0), jnp.concatenate(scaled_parts, axis=0)

    def local_ring(keys, values, queries, learn_rate, w_gate, w_up, w_out):
        hidden = w_gate.shape[1]
        rows = keys.shape[0]
        halves = 2 if rows % 16 == 0 else 1
        half = rows // halves
        scaled = (learn_rate[:, None] * values.astype(jnp.float32)).astype(jnp.bfloat16)
        width = keys.shape[1]
        own = jnp.stack(
            [keys.reshape(halves, half, width), scaled.reshape(halves, half, width)], axis=1
        ).reshape(2 * rows, width)
        sib = lax.ppermute(own, axes, swap)
        total = add_grads(None, *split([own, sib], half), w_gate, w_up, w_out)
        subs = [own[j * 2 * half:(j + 1) * 2 * half] for j in range(halves)]
        cws = list(subs)
        ccws = list(subs)
        for step in range(1, steps + 1):
            last = step == steps and chips % 2 == 0
            arrived = []
            for j in range(halves):
                if not last or halves == 1 or j == 0:
                    cws[j] = lax.ppermute(cws[j], axes, cw_perm)
                    arrived.append(cws[j])
                if not last or (halves == 2 and j == 1):
                    ccws[j] = lax.ppermute(ccws[j], axes, ccw_perm)
                    arrived.append(ccws[j])
            if step == steps:
                total, arrived = lax.optimization_barrier((total, arrived))
            from_sib = [lax.ppermute(chunk, axes, swap) for chunk in arrived]
            total = add_grads(total, *split(arrived + from_sib, half), w_gate, w_up, w_out)
        full_in, full_out = total
        new_gate = renorm(w_gate, full_in[:, :hidden])
        new_up = renorm(w_up, full_in[:, hidden:])
        new_out = renorm(w_out, full_out)
        new_gate, new_up, new_out = lax.optimization_barrier((new_gate, new_up, new_out))
        return apply(queries, new_gate, new_up, new_out)

    return local_ring


def solution(mesh):
    placed = (
        P(("grp", "seq", "outer"), None),
        P(("grp", "seq", "outer"), None),
        P(("grp", "seq", "outer"), None),
        P(("grp", "seq", "outer")),
        P("grp", None),
        P("grp", None),
        P("grp", None),
    )
    ring = chip_ring(mesh) if mesh.shape["outer"] == 2 else None
    local_ring = make_local_ring(ring) if ring else None

    def run(keys, values, queries, learn_rate, w_gate, w_up, w_out):
        per_part = keys.shape[0] // mesh.shape["grp"]
        gathered_bytes = 2 * per_part * keys.shape[1] * keys.dtype.itemsize
        if gathered_bytes > GATHER_LIMIT_BYTES:
            body = local_scatter
        elif local_ring is not None:
            body = local_ring
        else:
            body = local_gather
        return jax.shard_map(
            body,
            mesh=mesh,
            in_specs=placed,
            out_specs=P(("grp", "seq", "outer"), None),
            check_vma=False,
        )(keys, values, queries, learn_rate, w_gate, w_up, w_out)

    return run
```

```python
import jax
import jax.numpy as jnp
from jax import lax
from jax.sharding import PartitionSpec as P

epsilon = 1e-06
GATHER_LIMIT_BYTES = 16 * 1024 * 1024


def silu_grad(inputs):
    sigma = jax.nn.sigmoid(inputs)
    return sigma * (1.0 + inputs * (1.0 - sigma))


def renorm(weight, grads):
    old = weight.astype(jnp.float32)
    update = old + grads
    factor = jnp.sqrt(jnp.mean(old * old, axis=1, keepdims=True) + epsilon) / jnp.sqrt(
        jnp.mean(update * update, axis=1, keepdims=True) + epsilon
    )
    return (update * factor).astype(jnp.bfloat16)


contract_last = (((1,), (1,)), ((), ()))
contract_first = (((0,), (0,)), ((), ()))


def gradients(keys, scaled, w_gate, w_up, w_out):
    gate_pre = jnp.dot(keys, w_gate, preferred_element_type=jnp.float32)
    up_pre = jnp.dot(keys, w_up, preferred_element_type=jnp.float32)
    back_grad = lax.dot_general(scaled, w_out, contract_last, preferred_element_type=jnp.float32)
    activation = (jax.nn.silu(gate_pre) * up_pre).astype(jnp.bfloat16)
    d_gate = (back_grad * up_pre * silu_grad(gate_pre)).astype(jnp.bfloat16)
    d_up = (back_grad * jax.nn.silu(gate_pre)).astype(jnp.bfloat16)
    both_grads = jnp.concatenate([d_gate, d_up], axis=1)
    full_in = lax.dot_general(keys, both_grads, contract_first, preferred_element_type=jnp.float32)
    full_out = lax.dot_general(activation, scaled, contract_first, preferred_element_type=jnp.float32)
    return full_in, full_out


def apply(queries, full_gate, full_up, full_out_w):
    hidden = full_gate.shape[1]
    q_both = jnp.dot(queries, jnp.concatenate([full_gate, full_up], axis=1), preferred_element_type=jnp.float32)
    q_gate = q_both[:, :hidden]
    q_up = q_both[:, hidden:]
    q_act = (jax.nn.silu(q_gate) * q_up).astype(jnp.bfloat16)
    return jnp.dot(q_act, full_out_w, preferred_element_type=jnp.float32).astype(jnp.bfloat16)


def local_gather(keys, values, queries, learn_rate, w_gate, w_up, w_out):
    hidden = w_gate.shape[1]
    shards = lax.axis_size(("seq", "outer"))
    rows = keys.shape[0]
    width = keys.shape[1]
    scaled = (learn_rate[:, None] * values.astype(jnp.float32)).astype(jnp.bfloat16)
    both = jnp.concatenate([keys, scaled], axis=0)
    full = lax.all_gather(both, ("seq", "outer"), axis=0, tiled=True)
    full = full.reshape(shards, 2, rows, width)
    all_keys = full[:, 0].reshape(shards * rows, width)
    all_scaled = full[:, 1].reshape(shards * rows, width)
    full_in, full_out = gradients(all_keys, all_scaled, w_gate, w_up, w_out)
    new_gate = renorm(w_gate, full_in[:, :hidden])
    new_up = renorm(w_up, full_in[:, hidden:])
    new_out = renorm(w_out, full_out)
    return apply(queries, new_gate, new_up, new_out)


def local_scatter(keys, values, queries, learn_rate, w_gate, w_up, w_out):
    hidden = w_gate.shape[1]
    shards = lax.axis_size(("seq", "outer"))
    rows_gate = w_gate.shape[0] // shards
    rows_out = w_out.shape[0] // shards
    position = lax.axis_index(("seq", "outer"))
    scaled = (learn_rate[:, None] * values.astype(jnp.float32)).astype(jnp.bfloat16)
    full_in, full_out = gradients(keys, scaled, w_gate, w_up, w_out)
    grad_in = lax.psum_scatter(full_in, ("seq", "outer"), scatter_dimension=0, tiled=True)
    grad_out = lax.psum_scatter(full_out, ("seq", "outer"), scatter_dimension=0, tiled=True)
    own_gate = lax.dynamic_slice_in_dim(w_gate, position * rows_gate, rows_gate, 0)
    own_up = lax.dynamic_slice_in_dim(w_up, position * rows_gate, rows_gate, 0)
    own_out = lax.dynamic_slice_in_dim(w_out, position * rows_out, rows_out, 0)
    new_gate = renorm(own_gate, grad_in[:, :hidden])
    new_up = renorm(own_up, grad_in[:, hidden:])
    new_out = renorm(own_out, grad_out)
    full_gate, full_up, full_out_w = (
        lax.all_gather(new_gate, ("seq", "outer"), axis=0, tiled=True),
        lax.all_gather(new_up, ("seq", "outer"), axis=0, tiled=True),
        lax.all_gather(new_out, ("seq", "outer"), axis=0, tiled=True),
    )
    return apply(queries, full_gate, full_up, full_out_w)


def chip_ring(mesh):
    seq = mesh.shape["seq"]
    try:
        places = [tuple(mesh.devices[0, s, 0].coords) for s in range(seq)]
    except (AttributeError, TypeError):
        return None
    columns = sorted({p[0] for p in places})
    if len(columns) != 2 or len({p[1] for p in places}) != 1:
        return None
    first = sorted((p[2], s) for s, p in enumerate(places) if p[0] == columns[0])
    second = sorted((p[2], s) for s, p in enumerate(places) if p[0] == columns[1])
    return [s for _, s in first] + [s for _, s in reversed(second)]


def add_grads(total, keys_part, scaled_part, w_gate, w_up, w_out):
    full_in, full_out = gradients(keys_part, scaled_part, w_gate, w_up, w_out)
    if total is None:
        return full_in, full_out
    return total[0] + full_in, total[1] + full_out


def make_local_ring(ring):
    chips = len(ring)
    cw_perm = []
    ccw_perm = []
    for p in range(chips):
        for c in range(2):
            cw_perm.append((ring[p] * 2 + c, ring[(p + 1) % chips] * 2 + c))
            ccw_perm.append((ring[p] * 2 + c, ring[(p - 1) % chips] * 2 + c))
    swap = [(i, i ^ 1) for i in range(chips * 2)]
    steps = chips // 2
    axes = ("seq", "outer")

    def split(chunks, half):
        keys_parts = []
        scaled_parts = []
        for ch in chunks:
            for j in range(ch.shape[0] // (2 * half)):
                keys_parts.append(ch[2 * j * half:(2 * j + 1) * half])
                scaled_parts.append(ch[(2 * j + 1) * half:(2 * j + 2) * half])
        return jnp.concatenate(keys_parts, axis=0), jnp.concatenate(scaled_parts, axis=0)

    def local_ring(keys, values, queries, learn_rate, w_gate, w_up, w_out):
        hidden = w_gate.shape[1]
        rows = keys.shape[0]
        halves = 2 if rows % 16 == 0 else 1
        half = rows // halves
        width = keys.shape[1]
        scaled = (learn_rate[:, None] * values.astype(jnp.float32)).astype(jnp.bfloat16)
        own = jnp.stack(
            [keys.reshape(halves, half, width), scaled.reshape(halves, half, width)], axis=1
        ).reshape(2 * rows, width)
        sib = lax.ppermute(own, axes, swap)
        total = add_grads(None, *split([own, sib], half), w_gate, w_up, w_out)
        arrived = [own, own]
        for step in range(1, steps + 1):
            last = step == steps and chips % 2 == 0
            if last and halves == 2:
                sent = [lax.ppermute(arrived[0][:2 * half], axes, cw_perm),
                        lax.ppermute(arrived[1][2 * half:], axes, ccw_perm)]
            elif last:
                sent = [lax.ppermute(arrived[0], axes, cw_perm)]
            else:
                sent = [lax.ppermute(arrived[0], axes, cw_perm),
                        lax.ppermute(arrived[1], axes, ccw_perm)]
            arrived = sent
            if step == steps:
                total, arrived = lax.optimization_barrier((total, arrived))
            from_sib = [lax.ppermute(chunk, axes, swap) for chunk in arrived]
            total = add_grads(total, *split(arrived + from_sib, half), w_gate, w_up, w_out)
        full_in, full_out = total
        new_gate = renorm(w_gate, full_in[:, :hidden])
        new_up = renorm(w_up, full_in[:, hidden:])
        new_out = renorm(w_out, full_out)
        new_gate, new_up, new_out = lax.optimization_barrier((new_gate, new_up, new_out))
        return apply(queries, new_gate, new_up, new_out)

    return local_ring


def solution(mesh):
    placed = (
        P(("grp", "seq", "outer"), None),
        P(("grp", "seq", "outer"), None),
        P(("grp", "seq", "outer"), None),
        P(("grp", "seq", "outer")),
        P("grp", None),
        P("grp", None),
        P("grp", None),
    )
    ring = chip_ring(mesh) if mesh.shape["outer"] == 2 else None
    local_ring = make_local_ring(ring) if ring else None

    def run(keys, values, queries, learn_rate, w_gate, w_up, w_out):
        per_part = keys.shape[0] // mesh.shape["grp"]
        gathered_bytes = 2 * per_part * keys.shape[1] * keys.dtype.itemsize
        if gathered_bytes > GATHER_LIMIT_BYTES:
            body = local_scatter
        elif local_ring is not None:
            body = local_ring
        else:
            body = local_gather
        return jax.shard_map(
            body,
            mesh=mesh,
            in_specs=placed,
            out_specs=P(("grp", "seq", "outer"), None),
            check_vma=False,
        )(keys, values, queries, learn_rate, w_gate, w_up, w_out)

    return run
```

```python
import jax
import jax.numpy as jnp
from jax import lax
from jax.experimental import pallas as pl
from jax.sharding import PartitionSpec as P

epsilon = 1e-06
GATHER_LIMIT_BYTES = 16 * 1024 * 1024


def silu_grad(inputs):
    sigma = jax.nn.sigmoid(inputs)
    return sigma * (1.0 + inputs * (1.0 - sigma))


def renorm(weight, grads):
    old = weight.astype(jnp.float32)
    update = old + grads
    factor = jnp.sqrt(jnp.mean(old * old, axis=1, keepdims=True) + epsilon) / jnp.sqrt(
        jnp.mean(update * update, axis=1, keepdims=True) + epsilon
    )
    return (update * factor).astype(jnp.bfloat16)


contract_last = (((1,), (1,)), ((), ()))
contract_first = (((0,), (0,)), ((), ()))


def gradients(keys, scaled, w_gate, w_up, w_out):
    gate_pre = jnp.dot(keys, w_gate, preferred_element_type=jnp.float32)
    up_pre = jnp.dot(keys, w_up, preferred_element_type=jnp.float32)
    back_grad = lax.dot_general(scaled, w_out, contract_last, preferred_element_type=jnp.float32)
    activation = (jax.nn.silu(gate_pre) * up_pre).astype(jnp.bfloat16)
    d_gate = (back_grad * up_pre * silu_grad(gate_pre)).astype(jnp.bfloat16)
    d_up = (back_grad * jax.nn.silu(gate_pre)).astype(jnp.bfloat16)
    both_grads = jnp.concatenate([d_gate, d_up], axis=1)
    full_in = lax.dot_general(keys, both_grads, contract_first, preferred_element_type=jnp.float32)
    full_out = lax.dot_general(activation, scaled, contract_first, preferred_element_type=jnp.float32)
    return full_in, full_out


def apply(queries, full_gate, full_up, full_out_w):
    hidden = full_gate.shape[1]
    q_both = jnp.dot(queries, jnp.concatenate([full_gate, full_up], axis=1), preferred_element_type=jnp.float32)
    q_gate = q_both[:, :hidden]
    q_up = q_both[:, hidden:]
    q_act = (jax.nn.silu(q_gate) * q_up).astype(jnp.bfloat16)
    return jnp.dot(q_act, full_out_w, preferred_element_type=jnp.float32).astype(jnp.bfloat16)


def _tail_kernel(in_a, in_b, out_a, out_b, wg, wu, wo, q, o):
    hidden = wg.shape[1]
    grad_in = in_a[...] + in_b[...]
    new_gate = renorm(wg[...], grad_in[:, :hidden])
    new_up = renorm(wu[...], grad_in[:, hidden:])
    new_out = renorm(wo[...], out_a[...] + out_b[...])
    o[...] = apply(q[...], new_gate, new_up, new_out)


def tail(total, last, w_gate, w_up, w_out, queries):
    return pl.pallas_call(
        _tail_kernel,
        out_shape=jax.ShapeDtypeStruct((queries.shape[0], w_out.shape[1]), jnp.bfloat16),
    )(total[0], last[0], total[1], last[1], w_gate, w_up, w_out, queries)


def local_gather(keys, values, queries, learn_rate, w_gate, w_up, w_out):
    hidden = w_gate.shape[1]
    shards = lax.axis_size(("seq", "outer"))
    rows = keys.shape[0]
    width = keys.shape[1]
    scaled = (learn_rate[:, None] * values.astype(jnp.float32)).astype(jnp.bfloat16)
    both = jnp.concatenate([keys, scaled], axis=0)
    full = lax.all_gather(both, ("seq", "outer"), axis=0, tiled=True)
    full = full.reshape(shards, 2, rows, width)
    all_keys = full[:, 0].reshape(shards * rows, width)
    all_scaled = full[:, 1].reshape(shards * rows, width)
    full_in, full_out = gradients(all_keys, all_scaled, w_gate, w_up, w_out)
    new_gate = renorm(w_gate, full_in[:, :hidden])
    new_up = renorm(w_up, full_in[:, hidden:])
    new_out = renorm(w_out, full_out)
    return apply(queries, new_gate, new_up, new_out)


def local_scatter(keys, values, queries, learn_rate, w_gate, w_up, w_out):
    hidden = w_gate.shape[1]
    shards = lax.axis_size(("seq", "outer"))
    rows_gate = w_gate.shape[0] // shards
    rows_out = w_out.shape[0] // shards
    position = lax.axis_index(("seq", "outer"))
    scaled = (learn_rate[:, None] * values.astype(jnp.float32)).astype(jnp.bfloat16)
    full_in, full_out = gradients(keys, scaled, w_gate, w_up, w_out)
    grad_in = lax.psum_scatter(full_in, ("seq", "outer"), scatter_dimension=0, tiled=True)
    grad_out = lax.psum_scatter(full_out, ("seq", "outer"), scatter_dimension=0, tiled=True)
    own_gate = lax.dynamic_slice_in_dim(w_gate, position * rows_gate, rows_gate, 0)
    own_up = lax.dynamic_slice_in_dim(w_up, position * rows_gate, rows_gate, 0)
    own_out = lax.dynamic_slice_in_dim(w_out, position * rows_out, rows_out, 0)
    new_gate = renorm(own_gate, grad_in[:, :hidden])
    new_up = renorm(own_up, grad_in[:, hidden:])
    new_out = renorm(own_out, grad_out)
    full_gate, full_up, full_out_w = (
        lax.all_gather(new_gate, ("seq", "outer"), axis=0, tiled=True),
        lax.all_gather(new_up, ("seq", "outer"), axis=0, tiled=True),
        lax.all_gather(new_out, ("seq", "outer"), axis=0, tiled=True),
    )
    return apply(queries, full_gate, full_up, full_out_w)


def chip_ring(mesh):
    seq = mesh.shape["seq"]
    try:
        places = [tuple(mesh.devices[0, s, 0].coords) for s in range(seq)]
    except (AttributeError, TypeError):
        return None
    columns = sorted({p[0] for p in places})
    if len(columns) != 2 or len({p[1] for p in places}) != 1:
        return None
    first = sorted((p[2], s) for s, p in enumerate(places) if p[0] == columns[0])
    second = sorted((p[2], s) for s, p in enumerate(places) if p[0] == columns[1])
    return [s for _, s in first] + [s for _, s in reversed(second)]


def add_grads(total, keys_part, scaled_part, w_gate, w_up, w_out):
    full_in, full_out = gradients(keys_part, scaled_part, w_gate, w_up, w_out)
    if total is None:
        return full_in, full_out
    return total[0] + full_in, total[1] + full_out


def make_local_ring(ring):
    chips = len(ring)
    cw_perm = []
    ccw_perm = []
    for p in range(chips):
        for c in range(2):
            cw_perm.append((ring[p] * 2 + c, ring[(p + 1) % chips] * 2 + c))
            ccw_perm.append((ring[p] * 2 + c, ring[(p - 1) % chips] * 2 + c))
    swap = [(i, i ^ 1) for i in range(chips * 2)]
    steps = chips // 2
    axes = ("seq", "outer")

    def split(chunks, half):
        keys_parts = []
        scaled_parts = []
        for ch in chunks:
            for j in range(ch.shape[0] // (2 * half)):
                keys_parts.append(ch[2 * j * half:(2 * j + 1) * half])
                scaled_parts.append(ch[(2 * j + 1) * half:(2 * j + 2) * half])
        return jnp.concatenate(keys_parts, axis=0), jnp.concatenate(scaled_parts, axis=0)

    def local_ring(keys, values, queries, learn_rate, w_gate, w_up, w_out):
        hidden = w_gate.shape[1]
        rows = keys.shape[0]
        halves = 2 if rows % 16 == 0 else 1
        half = rows // halves
        width = keys.shape[1]
        scaled = (learn_rate[:, None] * values.astype(jnp.float32)).astype(jnp.bfloat16)
        own = jnp.stack(
            [keys.reshape(halves, half, width), scaled.reshape(halves, half, width)], axis=1
        ).reshape(2 * rows, width)
        sib = lax.ppermute(own, axes, swap)
        total = add_grads(None, *split([own, sib], half), w_gate, w_up, w_out)
        arrived = [own, own]
        for step in range(1, steps + 1):
            last = step == steps and chips % 2 == 0
            if last and halves == 2:
                sent = [lax.ppermute(arrived[0][:2 * half], axes, cw_perm),
                        lax.ppermute(arrived[1][2 * half:], axes, ccw_perm)]
            elif last:
                sent = [lax.ppermute(arrived[0], axes, cw_perm)]
            else:
                sent = [lax.ppermute(arrived[0], axes, cw_perm),
                        lax.ppermute(arrived[1], axes, ccw_perm)]
            arrived = sent
            if step == steps:
                total, arrived = lax.optimization_barrier((total, arrived))
            from_sib = [lax.ppermute(chunk, axes, swap) for chunk in arrived]
            if step == steps:
                last = gradients(*split(arrived + from_sib, half), w_gate, w_up, w_out)
                return tail(total, last, w_gate, w_up, w_out, queries)
            total = add_grads(total, *split(arrived + from_sib, half), w_gate, w_up, w_out)
        del hidden

    return local_ring


def solution(mesh):
    placed = (
        P(("grp", "seq", "outer"), None),
        P(("grp", "seq", "outer"), None),
        P(("grp", "seq", "outer"), None),
        P(("grp", "seq", "outer")),
        P("grp", None),
        P("grp", None),
        P("grp", None),
    )
    ring = chip_ring(mesh) if mesh.shape["outer"] == 2 else None
    local_ring = make_local_ring(ring) if ring else None

    def run(keys, values, queries, learn_rate, w_gate, w_up, w_out):
        per_part = keys.shape[0] // mesh.shape["grp"]
        gathered_bytes = 2 * per_part * keys.shape[1] * keys.dtype.itemsize
        if gathered_bytes > GATHER_LIMIT_BYTES:
            body = local_scatter
        elif local_ring is not None:
            body = local_ring
        else:
            body = local_gather
        return jax.shard_map(
            body,
            mesh=mesh,
            in_specs=placed,
            out_specs=P(("grp", "seq", "outer"), None),
            check_vma=False,
        )(keys, values, queries, learn_rate, w_gate, w_up, w_out)

    return run
```

```python
import jax
import jax.numpy as jnp
from jax import lax
from jax.sharding import PartitionSpec as P

epsilon = 1e-06
GATHER_LIMIT_BYTES = 16 * 1024 * 1024


def silu_grad(inputs):
    sigma = jax.nn.sigmoid(inputs)
    return sigma * (1.0 + inputs * (1.0 - sigma))


def renorm(weight, grads):
    old = weight.astype(jnp.float32)
    update = old + grads
    factor = jnp.sqrt(jnp.mean(old * old, axis=1, keepdims=True) + epsilon) / jnp.sqrt(
        jnp.mean(update * update, axis=1, keepdims=True) + epsilon
    )
    return (update * factor).astype(jnp.bfloat16)


contract_last = (((1,), (1,)), ((), ()))
contract_first = (((0,), (0,)), ((), ()))


def gradients(keys, scaled, w_gate, w_up, w_out):
    gate_pre = jnp.dot(keys, w_gate, preferred_element_type=jnp.float32)
    up_pre = jnp.dot(keys, w_up, preferred_element_type=jnp.float32)
    back_grad = lax.dot_general(scaled, w_out, contract_last, preferred_element_type=jnp.float32)
    activation = (jax.nn.silu(gate_pre) * up_pre).astype(jnp.bfloat16)
    d_gate = (back_grad * up_pre * silu_grad(gate_pre)).astype(jnp.bfloat16)
    d_up = (back_grad * jax.nn.silu(gate_pre)).astype(jnp.bfloat16)
    both_grads = jnp.concatenate([d_gate, d_up], axis=1)
    full_in = lax.dot_general(keys, both_grads, contract_first, preferred_element_type=jnp.float32)
    full_out = lax.dot_general(activation, scaled, contract_first, preferred_element_type=jnp.float32)
    return full_in, full_out


def apply(queries, full_gate, full_up, full_out_w):
    q_gate = jnp.dot(queries, full_gate, preferred_element_type=jnp.float32)
    q_up = jnp.dot(queries, full_up, preferred_element_type=jnp.float32)
    q_act = (jax.nn.silu(q_gate) * q_up).astype(jnp.bfloat16)
    return jnp.dot(q_act, full_out_w, preferred_element_type=jnp.float32).astype(jnp.bfloat16)


def local_gather(keys, values, queries, learn_rate, w_gate, w_up, w_out):
    hidden = w_gate.shape[1]
    shards = lax.axis_size(("seq", "outer"))
    rows = keys.shape[0]
    width = keys.shape[1]
    scaled = (learn_rate[:, None] * values.astype(jnp.float32)).astype(jnp.bfloat16)
    both = jnp.concatenate([keys, scaled], axis=0)
    full = lax.all_gather(both, ("seq", "outer"), axis=0, tiled=True)
    full = full.reshape(shards, 2, rows, width)
    all_keys = full[:, 0].reshape(shards * rows, width)
    all_scaled = full[:, 1].reshape(shards * rows, width)
    full_in, full_out = gradients(all_keys, all_scaled, w_gate, w_up, w_out)
    new_gate = renorm(w_gate, full_in[:, :hidden])
    new_up = renorm(w_up, full_in[:, hidden:])
    new_out = renorm(w_out, full_out)
    return apply(queries, new_gate, new_up, new_out)


def local_scatter(keys, values, queries, learn_rate, w_gate, w_up, w_out):
    hidden = w_gate.shape[1]
    shards = lax.axis_size(("seq", "outer"))
    rows_gate = w_gate.shape[0] // shards
    rows_out = w_out.shape[0] // shards
    position = lax.axis_index(("seq", "outer"))
    scaled = (learn_rate[:, None] * values.astype(jnp.float32)).astype(jnp.bfloat16)
    full_in, full_out = gradients(keys, scaled, w_gate, w_up, w_out)
    grad_in = lax.psum_scatter(full_in, ("seq", "outer"), scatter_dimension=0, tiled=True)
    grad_out = lax.psum_scatter(full_out, ("seq", "outer"), scatter_dimension=0, tiled=True)
    own_gate = lax.dynamic_slice_in_dim(w_gate, position * rows_gate, rows_gate, 0)
    own_up = lax.dynamic_slice_in_dim(w_up, position * rows_gate, rows_gate, 0)
    own_out = lax.dynamic_slice_in_dim(w_out, position * rows_out, rows_out, 0)
    new_gate = renorm(own_gate, grad_in[:, :hidden])
    new_up = renorm(own_up, grad_in[:, hidden:])
    new_out = renorm(own_out, grad_out)
    full_gate, full_up, full_out_w = (
        lax.all_gather(new_gate, ("seq", "outer"), axis=0, tiled=True),
        lax.all_gather(new_up, ("seq", "outer"), axis=0, tiled=True),
        lax.all_gather(new_out, ("seq", "outer"), axis=0, tiled=True),
    )
    return apply(queries, full_gate, full_up, full_out_w)


def chip_ring(mesh):
    seq = mesh.shape["seq"]
    try:
        places = [tuple(mesh.devices[0, s, 0].coords) for s in range(seq)]
    except (AttributeError, TypeError):
        return None
    columns = sorted({p[0] for p in places})
    if len(columns) != 2 or len({p[1] for p in places}) != 1:
        return None
    first = sorted((p[2], s) for s, p in enumerate(places) if p[0] == columns[0])
    second = sorted((p[2], s) for s, p in enumerate(places) if p[0] == columns[1])
    return [s for _, s in first] + [s for _, s in reversed(second)]


def add_grads(total, keys_part, scaled_part, w_gate, w_up, w_out):
    full_in, full_out = gradients(keys_part, scaled_part, w_gate, w_up, w_out)
    if total is None:
        return full_in, full_out
    return total[0] + full_in, total[1] + full_out


def make_local_ring(ring):
    chips = len(ring)
    cw_perm = []
    ccw_perm = []
    cw2_perm = []
    ccw2_perm = []
    for p in range(chips):
        for c in range(2):
            cw_perm.append((ring[p] * 2 + c, ring[(p + 1) % chips] * 2 + c))
            ccw_perm.append((ring[p] * 2 + c, ring[(p - 1) % chips] * 2 + c))
            cw2_perm.append((ring[p] * 2 + c, ring[(p + 2) % chips] * 2 + c))
            ccw2_perm.append((ring[p] * 2 + c, ring[(p - 2) % chips] * 2 + c))
    swap = [(i, i ^ 1) for i in range(chips * 2)]
    steps = chips // 2
    axes = ("seq", "outer")

    def split(chunks, half):
        keys_parts = []
        scaled_parts = []
        for ch in chunks:
            for j in range(ch.shape[0] // (2 * half)):
                keys_parts.append(ch[2 * j * half:(2 * j + 1) * half])
                scaled_parts.append(ch[(2 * j + 1) * half:(2 * j + 2) * half])
        return jnp.concatenate(keys_parts, axis=0), jnp.concatenate(scaled_parts, axis=0)

    def local_ring(keys, values, queries, learn_rate, w_gate, w_up, w_out):
        hidden = w_gate.shape[1]
        rows = keys.shape[0]
        halves = 2 if rows % 16 == 0 else 1
        half = rows // halves
        scaled = (learn_rate[:, None] * values.astype(jnp.float32)).astype(jnp.bfloat16)
        width = keys.shape[1]
        own = jnp.stack(
            [keys.reshape(halves, half, width), scaled.reshape(halves, half, width)], axis=1
        ).reshape(2 * rows, width)
        sib = lax.ppermute(own, axes, swap)
        total = add_grads(None, *split([own, sib], half), w_gate, w_up, w_out)
        arrived = [own, own]
        jump = chips % 2 == 0 and chips >= 4 and halves == 2
        last_step = steps - 1 if jump else steps
        for step in range(1, last_step + 1):
            final = step == last_step
            if final and jump:
                sent = [lax.ppermute(arrived[0], axes, cw_perm),
                        lax.ppermute(arrived[1], axes, ccw_perm),
                        lax.ppermute(arrived[0][:2 * half], axes, cw2_perm),
                        lax.ppermute(arrived[1][2 * half:], axes, ccw2_perm)]
            elif final and chips % 2 == 0 and halves == 2:
                sent = [lax.ppermute(arrived[0][:2 * half], axes, cw_perm),
                        lax.ppermute(arrived[1][2 * half:], axes, ccw_perm)]
            elif final and chips % 2 == 0:
                sent = [lax.ppermute(arrived[0], axes, cw_perm)]
            else:
                sent = [lax.ppermute(arrived[0], axes, cw_perm),
                        lax.ppermute(arrived[1], axes, ccw_perm)]
            arrived = sent
            if final:
                total, arrived = lax.optimization_barrier((total, arrived))
            from_sib = [lax.ppermute(chunk, axes, swap) for chunk in arrived]
            total = add_grads(total, *split(arrived + from_sib, half), w_gate, w_up, w_out)
            arrived = arrived[:2]
        full_in, full_out = total
        new_gate = renorm(w_gate, full_in[:, :hidden])
        new_up = renorm(w_up, full_in[:, hidden:])
        new_out = renorm(w_out, full_out)
        new_gate, new_up, new_out = lax.optimization_barrier((new_gate, new_up, new_out))
        return apply(queries, new_gate, new_up, new_out)

    return local_ring


def solution(mesh):
    placed = (
        P(("grp", "seq", "outer"), None),
        P(("grp", "seq", "outer"), None),
        P(("grp", "seq", "outer"), None),
        P(("grp", "seq", "outer")),
        P("grp", None),
        P("grp", None),
        P("grp", None),
    )
    ring = chip_ring(mesh) if mesh.shape["outer"] == 2 else None
    local_ring = make_local_ring(ring) if ring else None

    def run(keys, values, queries, learn_rate, w_gate, w_up, w_out):
        per_part = keys.shape[0] // mesh.shape["grp"]
        gathered_bytes = 2 * per_part * keys.shape[1] * keys.dtype.itemsize
        if gathered_bytes > GATHER_LIMIT_BYTES:
            body = local_scatter
        elif local_ring is not None:
            body = local_ring
        else:
            body = local_gather
        return jax.shard_map(
            body,
            mesh=mesh,
            in_specs=placed,
            out_specs=P(("grp", "seq", "outer"), None),
            check_vma=False,
        )(keys, values, queries, learn_rate, w_gate, w_up, w_out)

    return run
```

```python
import jax
import jax.numpy as jnp
from jax import lax
from jax.sharding import PartitionSpec as P

epsilon = 1e-06
GATHER_LIMIT_BYTES = 16 * 1024 * 1024


def silu_grad(inputs):
    sigma = jax.nn.sigmoid(inputs)
    return sigma * (1.0 + inputs * (1.0 - sigma))


def renorm(weight, grads):
    old = weight.astype(jnp.float32)
    update = old + grads
    factor = jnp.sqrt(jnp.mean(old * old, axis=1, keepdims=True) + epsilon) / jnp.sqrt(
        jnp.mean(update * update, axis=1, keepdims=True) + epsilon
    )
    return (update * factor).astype(jnp.bfloat16)


contract_last = (((1,), (1,)), ((), ()))
contract_first = (((0,), (0,)), ((), ()))


def gradients(keys, scaled, w_gate, w_up, w_out):
    gate_pre = jnp.dot(keys, w_gate, preferred_element_type=jnp.float32)
    up_pre = jnp.dot(keys, w_up, preferred_element_type=jnp.float32)
    back_grad = lax.dot_general(scaled, w_out, contract_last, preferred_element_type=jnp.float32)
    activation = (jax.nn.silu(gate_pre) * up_pre).astype(jnp.bfloat16)
    d_gate = (back_grad * up_pre * silu_grad(gate_pre)).astype(jnp.bfloat16)
    d_up = (back_grad * jax.nn.silu(gate_pre)).astype(jnp.bfloat16)
    both_grads = jnp.concatenate([d_gate, d_up], axis=1)
    full_in = lax.dot_general(keys, both_grads, contract_first, preferred_element_type=jnp.float32)
    full_out = lax.dot_general(activation, scaled, contract_first, preferred_element_type=jnp.float32)
    return full_in, full_out


def apply(queries, full_gate, full_up, full_out_w):
    q_gate = jnp.dot(queries, full_gate, preferred_element_type=jnp.float32)
    q_up = jnp.dot(queries, full_up, preferred_element_type=jnp.float32)
    q_act = (jax.nn.silu(q_gate) * q_up).astype(jnp.bfloat16)
    return jnp.dot(q_act, full_out_w, preferred_element_type=jnp.float32).astype(jnp.bfloat16)


def local_gather(keys, values, queries, learn_rate, w_gate, w_up, w_out):
    hidden = w_gate.shape[1]
    shards = lax.axis_size(("seq", "outer"))
    rows = keys.shape[0]
    width = keys.shape[1]
    scaled = (learn_rate[:, None] * values.astype(jnp.float32)).astype(jnp.bfloat16)
    both = jnp.concatenate([keys, scaled], axis=0)
    full = lax.all_gather(both, ("seq", "outer"), axis=0, tiled=True)
    full = full.reshape(shards, 2, rows, width)
    all_keys = full[:, 0].reshape(shards * rows, width)
    all_scaled = full[:, 1].reshape(shards * rows, width)
    full_in, full_out = gradients(all_keys, all_scaled, w_gate, w_up, w_out)
    new_gate = renorm(w_gate, full_in[:, :hidden])
    new_up = renorm(w_up, full_in[:, hidden:])
    new_out = renorm(w_out, full_out)
    return apply(queries, new_gate, new_up, new_out)


def local_scatter(keys, values, queries, learn_rate, w_gate, w_up, w_out):
    hidden = w_gate.shape[1]
    shards = lax.axis_size(("seq", "outer"))
    rows_gate = w_gate.shape[0] // shards
    rows_out = w_out.shape[0] // shards
    position = lax.axis_index(("seq", "outer"))
    scaled = (learn_rate[:, None] * values.astype(jnp.float32)).astype(jnp.bfloat16)
    full_in, full_out = gradients(keys, scaled, w_gate, w_up, w_out)
    grad_in = lax.psum_scatter(full_in, ("seq", "outer"), scatter_dimension=0, tiled=True)
    grad_out = lax.psum_scatter(full_out, ("seq", "outer"), scatter_dimension=0, tiled=True)
    own_gate = lax.dynamic_slice_in_dim(w_gate, position * rows_gate, rows_gate, 0)
    own_up = lax.dynamic_slice_in_dim(w_up, position * rows_gate, rows_gate, 0)
    own_out = lax.dynamic_slice_in_dim(w_out, position * rows_out, rows_out, 0)
    new_gate = renorm(own_gate, grad_in[:, :hidden])
    new_up = renorm(own_up, grad_in[:, hidden:])
    new_out = renorm(own_out, grad_out)
    full_gate, full_up, full_out_w = (
        lax.all_gather(new_gate, ("seq", "outer"), axis=0, tiled=True),
        lax.all_gather(new_up, ("seq", "outer"), axis=0, tiled=True),
        lax.all_gather(new_out, ("seq", "outer"), axis=0, tiled=True),
    )
    return apply(queries, full_gate, full_up, full_out_w)


def chip_ring(mesh):
    seq = mesh.shape["seq"]
    try:
        places = [tuple(mesh.devices[0, s, 0].coords) for s in range(seq)]
    except (AttributeError, TypeError):
        return None
    columns = sorted({p[0] for p in places})
    if len(columns) != 2 or len({p[1] for p in places}) != 1:
        return None
    first = sorted((p[2], s) for s, p in enumerate(places) if p[0] == columns[0])
    second = sorted((p[2], s) for s, p in enumerate(places) if p[0] == columns[1])
    return [s for _, s in first] + [s for _, s in reversed(second)]


def add_grads(total, keys_part, scaled_part, w_gate, w_up, w_out):
    full_in, full_out = gradients(keys_part, scaled_part, w_gate, w_up, w_out)
    if total is None:
        return full_in, full_out
    return total[0] + full_in, total[1] + full_out


def make_local_ring(ring):
    chips = len(ring)
    cw_perm = []
    ccw_perm = []
    for p in range(chips):
        for c in range(2):
            cw_perm.append((ring[p] * 2 + c, ring[(p + 1) % chips] * 2 + c))
            ccw_perm.append((ring[p] * 2 + c, ring[(p - 1) % chips] * 2 + c))
    swap = [(i, i ^ 1) for i in range(chips * 2)]
    steps = chips // 2
    axes = ("seq", "outer")

    def split(chunks, half):
        keys_parts = []
        scaled_parts = []
        for ch in chunks:
            for j in range(ch.shape[0] // (2 * half)):
                keys_parts.append(ch[2 * j * half:(2 * j + 1) * half])
                scaled_parts.append(ch[(2 * j + 1) * half:(2 * j + 2) * half])
        return jnp.concatenate(keys_parts, axis=0), jnp.concatenate(scaled_parts, axis=0)

    def local_ring(keys, values, queries, learn_rate, w_gate, w_up, w_out):
        hidden = w_gate.shape[1]
        rows = keys.shape[0]
        halves = 2 if rows % 16 == 0 else 1
        half = rows // halves
        scaled = (learn_rate[:, None] * values.astype(jnp.float32)).astype(jnp.bfloat16)
        width = keys.shape[1]
        own = jnp.stack(
            [keys.reshape(halves, half, width), scaled.reshape(halves, half, width)], axis=1
        ).reshape(2 * rows, width)
        sib = lax.ppermute(own, axes, swap)
        total = add_grads(None, *split([own, sib], half), w_gate, w_up, w_out)
        arrived = [own, own]
        for step in range(1, steps + 1):
            last = step == steps and chips % 2 == 0
            if last and halves == 2:
                sent = [lax.ppermute(arrived[0][:2 * half], axes, cw_perm),
                        lax.ppermute(arrived[1][2 * half:], axes, ccw_perm)]
            elif last:
                sent = [lax.ppermute(arrived[0], axes, cw_perm)]
            else:
                sent = [lax.ppermute(arrived[0], axes, cw_perm),
                        lax.ppermute(arrived[1], axes, ccw_perm)]
            arrived = sent
            if step == steps:
                total, arrived = lax.optimization_barrier((total, arrived))
            from_sib = [lax.ppermute(chunk, axes, swap) for chunk in arrived]
            if step == steps:
                total = add_grads(total, *split(arrived, half), w_gate, w_up, w_out)
                total = add_grads(total, *split(from_sib, half), w_gate, w_up, w_out)
            else:
                total = add_grads(total, *split(arrived + from_sib, half), w_gate, w_up, w_out)
        full_in, full_out = total
        new_gate = renorm(w_gate, full_in[:, :hidden])
        new_up = renorm(w_up, full_in[:, hidden:])
        new_out = renorm(w_out, full_out)
        new_gate, new_up, new_out = lax.optimization_barrier((new_gate, new_up, new_out))
        return apply(queries, new_gate, new_up, new_out)

    return local_ring


def solution(mesh):
    placed = (
        P(("grp", "seq", "outer"), None),
        P(("grp", "seq", "outer"), None),
        P(("grp", "seq", "outer"), None),
        P(("grp", "seq", "outer")),
        P("grp", None),
        P("grp", None),
        P("grp", None),
    )
    ring = chip_ring(mesh) if mesh.shape["outer"] == 2 else None
    local_ring = make_local_ring(ring) if ring else None

    def run(keys, values, queries, learn_rate, w_gate, w_up, w_out):
        per_part = keys.shape[0] // mesh.shape["grp"]
        gathered_bytes = 2 * per_part * keys.shape[1] * keys.dtype.itemsize
        if gathered_bytes > GATHER_LIMIT_BYTES:
            body = local_scatter
        elif local_ring is not None:
            body = local_ring
        else:
            body = local_gather
        return jax.shard_map(
            body,
            mesh=mesh,
            in_specs=placed,
            out_specs=P(("grp", "seq", "outer"), None),
            check_vma=False,
        )(keys, values, queries, learn_rate, w_gate, w_up, w_out)

    return run
```

```python
import jax
import jax.numpy as jnp
from jax import lax
from jax.sharding import PartitionSpec as P

epsilon = 1e-06
GATHER_LIMIT_BYTES = 16 * 1024 * 1024


def silu_grad(inputs):
    sigma = jax.nn.sigmoid(inputs)
    return sigma * (1.0 + inputs * (1.0 - sigma))


def renorm(weight, grads):
    old = weight.astype(jnp.float32)
    update = old + grads
    factor = jnp.sqrt(jnp.mean(old * old, axis=1, keepdims=True) + epsilon) / jnp.sqrt(
        jnp.mean(update * update, axis=1, keepdims=True) + epsilon
    )
    return (update * factor).astype(jnp.bfloat16)


def renorm_rows(weight, grads):
    old = weight.astype(jnp.float32)
    update = old + grads
    factor = jnp.sqrt(jnp.mean(old * old, axis=-1, keepdims=True) + epsilon) / jnp.sqrt(
        jnp.mean(update * update, axis=-1, keepdims=True) + epsilon
    )
    return (update * factor).astype(jnp.bfloat16)


contract_last = (((1,), (1,)), ((), ()))
contract_first = (((0,), (0,)), ((), ()))


def gradients(keys, scaled, w_gate, w_up, w_out):
    gate_pre = jnp.dot(keys, w_gate, preferred_element_type=jnp.float32)
    up_pre = jnp.dot(keys, w_up, preferred_element_type=jnp.float32)
    back_grad = lax.dot_general(scaled, w_out, contract_last, preferred_element_type=jnp.float32)
    activation = (jax.nn.silu(gate_pre) * up_pre).astype(jnp.bfloat16)
    d_gate = (back_grad * up_pre * silu_grad(gate_pre)).astype(jnp.bfloat16)
    d_up = (back_grad * jax.nn.silu(gate_pre)).astype(jnp.bfloat16)
    both_grads = jnp.concatenate([d_gate, d_up], axis=1)
    full_in = lax.dot_general(keys, both_grads, contract_first, preferred_element_type=jnp.float32)
    full_out = lax.dot_general(activation, scaled, contract_first, preferred_element_type=jnp.float32)
    return full_in, full_out


def apply(queries, full_gate, full_up, full_out_w):
    q_gate = jnp.dot(queries, full_gate, preferred_element_type=jnp.float32)
    q_up = jnp.dot(queries, full_up, preferred_element_type=jnp.float32)
    q_act = (jax.nn.silu(q_gate) * q_up).astype(jnp.bfloat16)
    return jnp.dot(q_act, full_out_w, preferred_element_type=jnp.float32).astype(jnp.bfloat16)


def local_gather(keys, values, queries, learn_rate, w_gate, w_up, w_out):
    hidden = w_gate.shape[1]
    shards = lax.axis_size(("seq", "outer"))
    rows = keys.shape[0]
    width = keys.shape[1]
    scaled = (learn_rate[:, None] * values.astype(jnp.float32)).astype(jnp.bfloat16)
    both = jnp.concatenate([keys, scaled], axis=0)
    full = lax.all_gather(both, ("seq", "outer"), axis=0, tiled=True)
    full = full.reshape(shards, 2, rows, width)
    all_keys = full[:, 0].reshape(shards * rows, width)
    all_scaled = full[:, 1].reshape(shards * rows, width)
    full_in, full_out = gradients(all_keys, all_scaled, w_gate, w_up, w_out)
    new_gate = renorm(w_gate, full_in[:, :hidden])
    new_up = renorm(w_up, full_in[:, hidden:])
    new_out = renorm(w_out, full_out)
    return apply(queries, new_gate, new_up, new_out)


def local_scatter(keys, values, queries, learn_rate, w_gate, w_up, w_out):
    hidden = w_gate.shape[1]
    shards = lax.axis_size(("seq", "outer"))
    rows_gate = w_gate.shape[0] // shards
    rows_out = w_out.shape[0] // shards
    position = lax.axis_index(("seq", "outer"))
    scaled = (learn_rate[:, None] * values.astype(jnp.float32)).astype(jnp.bfloat16)
    full_in, full_out = gradients(keys, scaled, w_gate, w_up, w_out)
    grad_in = lax.psum_scatter(full_in, ("seq", "outer"), scatter_dimension=0, tiled=True)
    grad_out = lax.psum_scatter(full_out, ("seq", "outer"), scatter_dimension=0, tiled=True)
    own_gate = lax.dynamic_slice_in_dim(w_gate, position * rows_gate, rows_gate, 0)
    own_up = lax.dynamic_slice_in_dim(w_up, position * rows_gate, rows_gate, 0)
    own_out = lax.dynamic_slice_in_dim(w_out, position * rows_out, rows_out, 0)
    new_gate = renorm(own_gate, grad_in[:, :hidden])
    new_up = renorm(own_up, grad_in[:, hidden:])
    new_out = renorm(own_out, grad_out)
    full_gate, full_up, full_out_w = (
        lax.all_gather(new_gate, ("seq", "outer"), axis=0, tiled=True),
        lax.all_gather(new_up, ("seq", "outer"), axis=0, tiled=True),
        lax.all_gather(new_out, ("seq", "outer"), axis=0, tiled=True),
    )
    return apply(queries, full_gate, full_up, full_out_w)


def chip_ring(mesh):
    seq = mesh.shape["seq"]
    try:
        places = [tuple(mesh.devices[0, s, 0].coords) for s in range(seq)]
    except (AttributeError, TypeError):
        return None
    columns = sorted({p[0] for p in places})
    if len(columns) != 2 or len({p[1] for p in places}) != 1:
        return None
    first = sorted((p[2], s) for s, p in enumerate(places) if p[0] == columns[0])
    second = sorted((p[2], s) for s, p in enumerate(places) if p[0] == columns[1])
    return [s for _, s in first] + [s for _, s in reversed(second)]


def add_grads(total, keys_part, scaled_part, w_gate, w_up, w_out):
    full_in, full_out = gradients(keys_part, scaled_part, w_gate, w_up, w_out)
    if total is None:
        return full_in, full_out
    return total[0] + full_in, total[1] + full_out


def make_local_ring(ring):
    chips = len(ring)
    cw_perm = []
    ccw_perm = []
    for p in range(chips):
        for c in range(2):
            cw_perm.append((ring[p] * 2 + c, ring[(p + 1) % chips] * 2 + c))
            ccw_perm.append((ring[p] * 2 + c, ring[(p - 1) % chips] * 2 + c))
    swap = [(i, i ^ 1) for i in range(chips * 2)]
    steps = chips // 2
    axes = ("seq", "outer")

    def split(chunks, half):
        keys_parts = []
        scaled_parts = []
        for ch in chunks:
            for j in range(ch.shape[0] // (2 * half)):
                keys_parts.append(ch[2 * j * half:(2 * j + 1) * half])
                scaled_parts.append(ch[(2 * j + 1) * half:(2 * j + 2) * half])
        return jnp.concatenate(keys_parts, axis=0), jnp.concatenate(scaled_parts, axis=0)

    def local_ring(keys, values, queries, learn_rate, w_gate, w_up, w_out):
        hidden = w_gate.shape[1]
        rows = keys.shape[0]
        halves = 2 if rows % 16 == 0 else 1
        half = rows // halves
        scaled = (learn_rate[:, None] * values.astype(jnp.float32)).astype(jnp.bfloat16)
        width = keys.shape[1]
        own = jnp.stack(
            [keys.reshape(halves, half, width), scaled.reshape(halves, half, width)], axis=1
        ).reshape(2 * rows, width)
        sib = lax.ppermute(own, axes, swap)
        total = add_grads(None, *split([own, sib], half), w_gate, w_up, w_out)
        arrived = [own, own]
        for step in range(1, steps + 1):
            last = step == steps and chips % 2 == 0
            if last and halves == 2:
                sent = [lax.ppermute(arrived[0][:2 * half], axes, cw_perm),
                        lax.ppermute(arrived[1][2 * half:], axes, ccw_perm)]
            elif last:
                sent = [lax.ppermute(arrived[0], axes, cw_perm)]
            else:
                sent = [lax.ppermute(arrived[0], axes, cw_perm),
                        lax.ppermute(arrived[1], axes, ccw_perm)]
            arrived = sent
            if step == steps:
                total, arrived = lax.optimization_barrier((total, arrived))
            from_sib = [lax.ppermute(chunk, axes, swap) for chunk in arrived]
            if step == steps:
                total = add_grads(total, *split(arrived, half), w_gate, w_up, w_out)
                total = add_grads(total, *split(from_sib, half), w_gate, w_up, w_out)
            else:
                total = add_grads(total, *split(arrived + from_sib, half), w_gate, w_up, w_out)
        full_in, full_out = total
        old_all = jnp.stack([w_gate, w_up, w_out], axis=1)
        grads_all = jnp.stack([full_in[:, :hidden], full_in[:, hidden:], full_out], axis=1)
        new_all = lax.optimization_barrier(renorm_rows(old_all, grads_all))
        return apply(queries, new_all[:, 0], new_all[:, 1], new_all[:, 2])

    return local_ring


def solution(mesh):
    placed = (
        P(("grp", "seq", "outer"), None),
        P(("grp", "seq", "outer"), None),
        P(("grp", "seq", "outer"), None),
        P(("grp", "seq", "outer")),
        P("grp", None),
        P("grp", None),
        P("grp", None),
    )
    ring = chip_ring(mesh) if mesh.shape["outer"] == 2 else None
    local_ring = make_local_ring(ring) if ring else None

    def run(keys, values, queries, learn_rate, w_gate, w_up, w_out):
        per_part = keys.shape[0] // mesh.shape["grp"]
        gathered_bytes = 2 * per_part * keys.shape[1] * keys.dtype.itemsize
        if gathered_bytes > GATHER_LIMIT_BYTES:
            body = local_scatter
        elif local_ring is not None:
            body = local_ring
        else:
            body = local_gather
        return jax.shard_map(
            body,
            mesh=mesh,
            in_specs=placed,
            out_specs=P(("grp", "seq", "outer"), None),
            check_vma=False,
        )(keys, values, queries, learn_rate, w_gate, w_up, w_out)

    return run
```

```python
import jax
import jax.numpy as jnp
from jax import lax
from jax.experimental import pallas as pl
from jax.sharding import PartitionSpec as P

epsilon = 1e-06
GATHER_LIMIT_BYTES = 16 * 1024 * 1024


def silu_grad(inputs):
    sigma = jax.nn.sigmoid(inputs)
    return sigma * (1.0 + inputs * (1.0 - sigma))


def renorm(weight, grads):
    old = weight.astype(jnp.float32)
    update = old + grads
    factor = jnp.sqrt(jnp.mean(old * old, axis=1, keepdims=True) + epsilon) / jnp.sqrt(
        jnp.mean(update * update, axis=1, keepdims=True) + epsilon
    )
    return (update * factor).astype(jnp.bfloat16)


contract_last = (((1,), (1,)), ((), ()))
contract_first = (((0,), (0,)), ((), ()))


def gradients(keys, scaled, w_gate, w_up, w_out):
    gate_pre = jnp.dot(keys, w_gate, preferred_element_type=jnp.float32)
    up_pre = jnp.dot(keys, w_up, preferred_element_type=jnp.float32)
    back_grad = lax.dot_general(scaled, w_out, contract_last, preferred_element_type=jnp.float32)
    activation = (jax.nn.silu(gate_pre) * up_pre).astype(jnp.bfloat16)
    d_gate = (back_grad * up_pre * silu_grad(gate_pre)).astype(jnp.bfloat16)
    d_up = (back_grad * jax.nn.silu(gate_pre)).astype(jnp.bfloat16)
    both_grads = jnp.concatenate([d_gate, d_up], axis=1)
    full_in = lax.dot_general(keys, both_grads, contract_first, preferred_element_type=jnp.float32)
    full_out = lax.dot_general(activation, scaled, contract_first, preferred_element_type=jnp.float32)
    return full_in, full_out


def apply(queries, full_gate, full_up, full_out_w):
    q_gate = jnp.dot(queries, full_gate, preferred_element_type=jnp.float32)
    q_up = jnp.dot(queries, full_up, preferred_element_type=jnp.float32)
    q_act = (jax.nn.silu(q_gate) * q_up).astype(jnp.bfloat16)
    return jnp.dot(q_act, full_out_w, preferred_element_type=jnp.float32).astype(jnp.bfloat16)


def _build_kernel(k_ref, v_ref, lr_ref, o_ref):
    rows, width = v_ref.shape
    half = rows // 2
    rate = jnp.transpose(jnp.broadcast_to(lr_ref[...], (width, rows)))
    scaled = (v_ref[...].astype(jnp.float32) * rate).astype(jnp.bfloat16)
    keys = k_ref[...]
    o_ref[0:half] = keys[0:half]
    o_ref[half:2 * half] = scaled[0:half]
    o_ref[2 * half:3 * half] = keys[half:]
    o_ref[3 * half:] = scaled[half:]


def build_block(keys, values, learn_rate):
    rows, width = keys.shape
    return pl.pallas_call(
        _build_kernel,
        out_shape=jax.ShapeDtypeStruct((2 * rows, width), keys.dtype),
    )(keys, values, learn_rate.reshape(1, rows))


def local_gather(keys, values, queries, learn_rate, w_gate, w_up, w_out):
    hidden = w_gate.shape[1]
    shards = lax.axis_size(("seq", "outer"))
    rows = keys.shape[0]
    width = keys.shape[1]
    scaled = (learn_rate[:, None] * values.astype(jnp.float32)).astype(jnp.bfloat16)
    both = jnp.concatenate([keys, scaled], axis=0)
    full = lax.all_gather(both, ("seq", "outer"), axis=0, tiled=True)
    full = full.reshape(shards, 2, rows, width)
    all_keys = full[:, 0].reshape(shards * rows, width)
    all_scaled = full[:, 1].reshape(shards * rows, width)
    full_in, full_out = gradients(all_keys, all_scaled, w_gate, w_up, w_out)
    new_gate = renorm(w_gate, full_in[:, :hidden])
    new_up = renorm(w_up, full_in[:, hidden:])
    new_out = renorm(w_out, full_out)
    return apply(queries, new_gate, new_up, new_out)


def local_scatter(keys, values, queries, learn_rate, w_gate, w_up, w_out):
    hidden = w_gate.shape[1]
    shards = lax.axis_size(("seq", "outer"))
    rows_gate = w_gate.shape[0] // shards
    rows_out = w_out.shape[0] // shards
    position = lax.axis_index(("seq", "outer"))
    scaled = (learn_rate[:, None] * values.astype(jnp.float32)).astype(jnp.bfloat16)
    full_in, full_out = gradients(keys, scaled, w_gate, w_up, w_out)
    grad_in = lax.psum_scatter(full_in, ("seq", "outer"), scatter_dimension=0, tiled=True)
    grad_out = lax.psum_scatter(full_out, ("seq", "outer"), scatter_dimension=0, tiled=True)
    own_gate = lax.dynamic_slice_in_dim(w_gate, position * rows_gate, rows_gate, 0)
    own_up = lax.dynamic_slice_in_dim(w_up, position * rows_gate, rows_gate, 0)
    own_out = lax.dynamic_slice_in_dim(w_out, position * rows_out, rows_out, 0)
    new_gate = renorm(own_gate, grad_in[:, :hidden])
    new_up = renorm(own_up, grad_in[:, hidden:])
    new_out = renorm(own_out, grad_out)
    full_gate, full_up, full_out_w = (
        lax.all_gather(new_gate, ("seq", "outer"), axis=0, tiled=True),
        lax.all_gather(new_up, ("seq", "outer"), axis=0, tiled=True),
        lax.all_gather(new_out, ("seq", "outer"), axis=0, tiled=True),
    )
    return apply(queries, full_gate, full_up, full_out_w)


def chip_ring(mesh):
    seq = mesh.shape["seq"]
    try:
        places = [tuple(mesh.devices[0, s, 0].coords) for s in range(seq)]
    except (AttributeError, TypeError):
        return None
    columns = sorted({p[0] for p in places})
    if len(columns) != 2 or len({p[1] for p in places}) != 1:
        return None
    first = sorted((p[2], s) for s, p in enumerate(places) if p[0] == columns[0])
    second = sorted((p[2], s) for s, p in enumerate(places) if p[0] == columns[1])
    return [s for _, s in first] + [s for _, s in reversed(second)]


def add_grads(total, keys_part, scaled_part, w_gate, w_up, w_out):
    full_in, full_out = gradients(keys_part, scaled_part, w_gate, w_up, w_out)
    if total is None:
        return full_in, full_out
    return total[0] + full_in, total[1] + full_out


def make_local_ring(ring):
    chips = len(ring)
    cw_perm = []
    ccw_perm = []
    for p in range(chips):
        for c in range(2):
            cw_perm.append((ring[p] * 2 + c, ring[(p + 1) % chips] * 2 + c))
            ccw_perm.append((ring[p] * 2 + c, ring[(p - 1) % chips] * 2 + c))
    swap = [(i, i ^ 1) for i in range(chips * 2)]
    steps = chips // 2
    axes = ("seq", "outer")

    def split(chunks, half):
        keys_parts = []
        scaled_parts = []
        for ch in chunks:
            for j in range(ch.shape[0] // (2 * half)):
                keys_parts.append(ch[2 * j * half:(2 * j + 1) * half])
                scaled_parts.append(ch[(2 * j + 1) * half:(2 * j + 2) * half])
        return jnp.concatenate(keys_parts, axis=0), jnp.concatenate(scaled_parts, axis=0)

    def local_ring(keys, values, queries, learn_rate, w_gate, w_up, w_out):
        hidden = w_gate.shape[1]
        rows = keys.shape[0]
        halves = 2 if rows % 16 == 0 else 1
        half = rows // halves
        width = keys.shape[1]
        if halves == 2 and rows % 128 == 0 and width % 128 == 0:
            own = build_block(keys, values, learn_rate)
        else:
            scaled = (learn_rate[:, None] * values.astype(jnp.float32)).astype(jnp.bfloat16)
            own = jnp.stack(
                [keys.reshape(halves, half, width), scaled.reshape(halves, half, width)], axis=1
            ).reshape(2 * rows, width)
        sib = lax.ppermute(own, axes, swap)
        total = add_grads(None, *split([own, sib], half), w_gate, w_up, w_out)
        arrived = [own, own]
        for step in range(1, steps + 1):
            last = step == steps and chips % 2 == 0
            if last and halves == 2:
                sent = [lax.ppermute(arrived[0][:2 * half], axes, cw_perm),
                        lax.ppermute(arrived[1][2 * half:], axes, ccw_perm)]
            elif last:
                sent = [lax.ppermute(arrived[0], axes, cw_perm)]
            else:
                sent = [lax.ppermute(arrived[0], axes, cw_perm),
                        lax.ppermute(arrived[1], axes, ccw_perm)]
            arrived = sent
            if step == steps:
                total, arrived = lax.optimization_barrier((total, arrived))
            from_sib = [lax.ppermute(chunk, axes, swap) for chunk in arrived]
            if step == steps:
                total = add_grads(total, *split(arrived, half), w_gate, w_up, w_out)
                total = add_grads(total, *split(from_sib, half), w_gate, w_up, w_out)
            else:
                total = add_grads(total, *split(arrived + from_sib, half), w_gate, w_up, w_out)
        full_in, full_out = total
        new_gate = renorm(w_gate, full_in[:, :hidden])
        new_up = renorm(w_up, full_in[:, hidden:])
        new_out = renorm(w_out, full_out)
        new_gate, new_up, new_out = lax.optimization_barrier((new_gate, new_up, new_out))
        return apply(queries, new_gate, new_up, new_out)

    return local_ring


def solution(mesh):
    placed = (
        P(("grp", "seq", "outer"), None),
        P(("grp", "seq", "outer"), None),
        P(("grp", "seq", "outer"), None),
        P(("grp", "seq", "outer")),
        P("grp", None),
        P("grp", None),
        P("grp", None),
    )
    ring = chip_ring(mesh) if mesh.shape["outer"] == 2 else None
    local_ring = make_local_ring(ring) if ring else None

    def run(keys, values, queries, learn_rate, w_gate, w_up, w_out):
        per_part = keys.shape[0] // mesh.shape["grp"]
        gathered_bytes = 2 * per_part * keys.shape[1] * keys.dtype.itemsize
        if gathered_bytes > GATHER_LIMIT_BYTES:
            body = local_scatter
        elif local_ring is not None:
            body = local_ring
        else:
            body = local_gather
        return jax.shard_map(
            body,
            mesh=mesh,
            in_specs=placed,
            out_specs=P(("grp", "seq", "outer"), None),
            check_vma=False,
        )(keys, values, queries, learn_rate, w_gate, w_up, w_out)

    return run
```

```python
import jax
import jax.numpy as jnp
from jax import lax
from jax.sharding import PartitionSpec as P

epsilon = 1e-06
GATHER_LIMIT_BYTES = 16 * 1024 * 1024


def silu_grad(inputs):
    sigma = jax.nn.sigmoid(inputs)
    return sigma * (1.0 + inputs * (1.0 - sigma))


def renorm(weight, grads):
    old = weight.astype(jnp.float32)
    update = old + grads
    factor = jnp.sqrt(jnp.mean(old * old, axis=1, keepdims=True) + epsilon) / jnp.sqrt(
        jnp.mean(update * update, axis=1, keepdims=True) + epsilon
    )
    return (update * factor).astype(jnp.bfloat16)


contract_last = (((1,), (1,)), ((), ()))
contract_first = (((0,), (0,)), ((), ()))


def gradients(keys, scaled, w_gate, w_up, w_out):
    gate_pre = jnp.dot(keys, w_gate, preferred_element_type=jnp.float32)
    up_pre = jnp.dot(keys, w_up, preferred_element_type=jnp.float32)
    back_grad = lax.dot_general(scaled, w_out, contract_last, preferred_element_type=jnp.float32)
    activation = (jax.nn.silu(gate_pre) * up_pre).astype(jnp.bfloat16)
    d_gate = (back_grad * up_pre * silu_grad(gate_pre)).astype(jnp.bfloat16)
    d_up = (back_grad * jax.nn.silu(gate_pre)).astype(jnp.bfloat16)
    both_grads = jnp.concatenate([d_gate, d_up], axis=1)
    full_in = lax.dot_general(keys, both_grads, contract_first, preferred_element_type=jnp.float32)
    full_out = lax.dot_general(activation, scaled, contract_first, preferred_element_type=jnp.float32)
    return full_in, full_out


def apply(queries, full_gate, full_up, full_out_w):
    q_gate = jnp.dot(queries, full_gate, preferred_element_type=jnp.float32)
    q_up = jnp.dot(queries, full_up, preferred_element_type=jnp.float32)
    q_act = lax.optimization_barrier((jax.nn.silu(q_gate) * q_up).astype(jnp.bfloat16))
    return jnp.dot(q_act, full_out_w, preferred_element_type=jnp.float32).astype(jnp.bfloat16)


def local_gather(keys, values, queries, learn_rate, w_gate, w_up, w_out):
    hidden = w_gate.shape[1]
    shards = lax.axis_size(("seq", "outer"))
    rows = keys.shape[0]
    width = keys.shape[1]
    scaled = (learn_rate[:, None] * values.astype(jnp.float32)).astype(jnp.bfloat16)
    both = jnp.concatenate([keys, scaled], axis=0)
    full = lax.all_gather(both, ("seq", "outer"), axis=0, tiled=True)
    full = full.reshape(shards, 2, rows, width)
    all_keys = full[:, 0].reshape(shards * rows, width)
    all_scaled = full[:, 1].reshape(shards * rows, width)
    full_in, full_out = gradients(all_keys, all_scaled, w_gate, w_up, w_out)
    new_gate = renorm(w_gate, full_in[:, :hidden])
    new_up = renorm(w_up, full_in[:, hidden:])
    new_out = renorm(w_out, full_out)
    return apply(queries, new_gate, new_up, new_out)


def local_scatter(keys, values, queries, learn_rate, w_gate, w_up, w_out):
    hidden = w_gate.shape[1]
    shards = lax.axis_size(("seq", "outer"))
    rows_gate = w_gate.shape[0] // shards
    rows_out = w_out.shape[0] // shards
    position = lax.axis_index(("seq", "outer"))
    scaled = (learn_rate[:, None] * values.astype(jnp.float32)).astype(jnp.bfloat16)
    full_in, full_out = gradients(keys, scaled, w_gate, w_up, w_out)
    grad_in = lax.psum_scatter(full_in, ("seq", "outer"), scatter_dimension=0, tiled=True)
    grad_out = lax.psum_scatter(full_out, ("seq", "outer"), scatter_dimension=0, tiled=True)
    own_gate = lax.dynamic_slice_in_dim(w_gate, position * rows_gate, rows_gate, 0)
    own_up = lax.dynamic_slice_in_dim(w_up, position * rows_gate, rows_gate, 0)
    own_out = lax.dynamic_slice_in_dim(w_out, position * rows_out, rows_out, 0)
    new_gate = renorm(own_gate, grad_in[:, :hidden])
    new_up = renorm(own_up, grad_in[:, hidden:])
    new_out = renorm(own_out, grad_out)
    full_gate, full_up, full_out_w = (
        lax.all_gather(new_gate, ("seq", "outer"), axis=0, tiled=True),
        lax.all_gather(new_up, ("seq", "outer"), axis=0, tiled=True),
        lax.all_gather(new_out, ("seq", "outer"), axis=0, tiled=True),
    )
    return apply(queries, full_gate, full_up, full_out_w)


def chip_ring(mesh):
    seq = mesh.shape["seq"]
    try:
        places = [tuple(mesh.devices[0, s, 0].coords) for s in range(seq)]
    except (AttributeError, TypeError):
        return None
    columns = sorted({p[0] for p in places})
    if len(columns) != 2 or len({p[1] for p in places}) != 1:
        return None
    first = sorted((p[2], s) for s, p in enumerate(places) if p[0] == columns[0])
    second = sorted((p[2], s) for s, p in enumerate(places) if p[0] == columns[1])
    return [s for _, s in first] + [s for _, s in reversed(second)]


def add_grads(total, keys_part, scaled_part, w_gate, w_up, w_out):
    full_in, full_out = gradients(keys_part, scaled_part, w_gate, w_up, w_out)
    if total is None:
        return full_in, full_out
    return total[0] + full_in, total[1] + full_out


def make_local_ring(ring):
    chips = len(ring)
    cw_perm = []
    ccw_perm = []
    for p in range(chips):
        for c in range(2):
            cw_perm.append((ring[p] * 2 + c, ring[(p + 1) % chips] * 2 + c))
            ccw_perm.append((ring[p] * 2 + c, ring[(p - 1) % chips] * 2 + c))
    swap = [(i, i ^ 1) for i in range(chips * 2)]
    steps = chips // 2
    axes = ("seq", "outer")

    def split(chunks, half):
        keys_parts = []
        scaled_parts = []
        for ch in chunks:
            for j in range(ch.shape[0] // (2 * half)):
                keys_parts.append(ch[2 * j * half:(2 * j + 1) * half])
                scaled_parts.append(ch[(2 * j + 1) * half:(2 * j + 2) * half])
        return jnp.concatenate(keys_parts, axis=0), jnp.concatenate(scaled_parts, axis=0)

    def local_ring(keys, values, queries, learn_rate, w_gate, w_up, w_out):
        hidden = w_gate.shape[1]
        rows = keys.shape[0]
        halves = 2 if rows % 16 == 0 else 1
        half = rows // halves
        scaled = (learn_rate[:, None] * values.astype(jnp.float32)).astype(jnp.bfloat16)
        width = keys.shape[1]
        own = jnp.stack(
            [keys.reshape(halves, half, width), scaled.reshape(halves, half, width)], axis=1
        ).reshape(2 * rows, width)
        sib = lax.ppermute(own, axes, swap)
        total = add_grads(None, *split([own, sib], half), w_gate, w_up, w_out)
        arrived = [own, own]
        for step in range(1, steps + 1):
            last = step == steps and chips % 2 == 0
            if last and halves == 2:
                sent = [lax.ppermute(arrived[0][:2 * half], axes, cw_perm),
                        lax.ppermute(arrived[1][2 * half:], axes, ccw_perm)]
            elif last:
                sent = [lax.ppermute(arrived[0], axes, cw_perm)]
            else:
                sent = [lax.ppermute(arrived[0], axes, cw_perm),
                        lax.ppermute(arrived[1], axes, ccw_perm)]
            arrived = sent
            if step == steps:
                total, arrived = lax.optimization_barrier((total, arrived))
            from_sib = [lax.ppermute(chunk, axes, swap) for chunk in arrived]
            if step == steps:
                total = add_grads(total, *split(arrived, half), w_gate, w_up, w_out)
                total = add_grads(total, *split(from_sib, half), w_gate, w_up, w_out)
            else:
                total = add_grads(total, *split(arrived + from_sib, half), w_gate, w_up, w_out)
        full_in, full_out = total
        new_gate = renorm(w_gate, full_in[:, :hidden])
        new_up = renorm(w_up, full_in[:, hidden:])
        new_out = renorm(w_out, full_out)
        new_gate, new_up, new_out = lax.optimization_barrier((new_gate, new_up, new_out))
        return apply(queries, new_gate, new_up, new_out)

    return local_ring


def solution(mesh):
    placed = (
        P(("grp", "seq", "outer"), None),
        P(("grp", "seq", "outer"), None),
        P(("grp", "seq", "outer"), None),
        P(("grp", "seq", "outer")),
        P("grp", None),
        P("grp", None),
        P("grp", None),
    )
    ring = chip_ring(mesh) if mesh.shape["outer"] == 2 else None
    local_ring = make_local_ring(ring) if ring else None

    def run(keys, values, queries, learn_rate, w_gate, w_up, w_out):
        per_part = keys.shape[0] // mesh.shape["grp"]
        gathered_bytes = 2 * per_part * keys.shape[1] * keys.dtype.itemsize
        if gathered_bytes > GATHER_LIMIT_BYTES:
            body = local_scatter
        elif local_ring is not None:
            body = local_ring
        else:
            body = local_gather
        return jax.shard_map(
            body,
            mesh=mesh,
            in_specs=placed,
            out_specs=P(("grp", "seq", "outer"), None),
            check_vma=False,
        )(keys, values, queries, learn_rate, w_gate, w_up, w_out)

    return run
```

```python
import jax
import jax.numpy as jnp
from jax import lax
from jax.sharding import PartitionSpec as P

epsilon = 1e-06
GATHER_LIMIT_BYTES = 16 * 1024 * 1024


def silu_grad(inputs):
    sigma = jax.nn.sigmoid(inputs)
    return sigma * (1.0 + inputs * (1.0 - sigma))


def renorm(weight, grads):
    old = weight.astype(jnp.float32)
    update = old + grads
    factor = jnp.sqrt(jnp.mean(old * old, axis=1, keepdims=True) + epsilon) / jnp.sqrt(
        jnp.mean(update * update, axis=1, keepdims=True) + epsilon
    )
    return (update * factor).astype(jnp.bfloat16)


contract_last = (((1,), (1,)), ((), ()))
contract_first = (((0,), (0,)), ((), ()))


def gradients(keys, scaled, w_gate, w_up, w_out):
    gate_pre = jnp.dot(keys, w_gate, preferred_element_type=jnp.float32)
    up_pre = jnp.dot(keys, w_up, preferred_element_type=jnp.float32)
    back_grad = lax.dot_general(scaled, w_out, contract_last, preferred_element_type=jnp.float32)
    activation = (jax.nn.silu(gate_pre) * up_pre).astype(jnp.bfloat16)
    d_gate = (back_grad * up_pre * silu_grad(gate_pre)).astype(jnp.bfloat16)
    d_up = (back_grad * jax.nn.silu(gate_pre)).astype(jnp.bfloat16)
    both_grads = jnp.concatenate([d_gate, d_up], axis=1)
    full_in = lax.dot_general(keys, both_grads, contract_first, preferred_element_type=jnp.float32)
    full_out = lax.dot_general(activation, scaled, contract_first, preferred_element_type=jnp.float32)
    return full_in, full_out


def apply(queries, full_gate, full_up, full_out_w):
    q_gate = jnp.dot(queries, full_gate, preferred_element_type=jnp.float32)
    q_up = jnp.dot(queries, full_up, preferred_element_type=jnp.float32)
    q_act = (jax.nn.silu(q_gate) * q_up).astype(jnp.bfloat16)
    return jnp.dot(q_act, full_out_w, preferred_element_type=jnp.float32).astype(jnp.bfloat16)


def local_gather(keys, values, queries, learn_rate, w_gate, w_up, w_out):
    hidden = w_gate.shape[1]
    shards = lax.axis_size(("seq", "outer"))
    rows = keys.shape[0]
    width = keys.shape[1]
    scaled = (learn_rate[:, None] * values.astype(jnp.float32)).astype(jnp.bfloat16)
    both = jnp.concatenate([keys, scaled], axis=0)
    full = lax.all_gather(both, ("seq", "outer"), axis=0, tiled=True)
    full = full.reshape(shards, 2, rows, width)
    all_keys = full[:, 0].reshape(shards * rows, width)
    all_scaled = full[:, 1].reshape(shards * rows, width)
    full_in, full_out = gradients(all_keys, all_scaled, w_gate, w_up, w_out)
    new_gate = renorm(w_gate, full_in[:, :hidden])
    new_up = renorm(w_up, full_in[:, hidden:])
    new_out = renorm(w_out, full_out)
    return apply(queries, new_gate, new_up, new_out)


def local_scatter(keys, values, queries, learn_rate, w_gate, w_up, w_out):
    hidden = w_gate.shape[1]
    shards = lax.axis_size(("seq", "outer"))
    rows_gate = w_gate.shape[0] // shards
    rows_out = w_out.shape[0] // shards
    position = lax.axis_index(("seq", "outer"))
    scaled = (learn_rate[:, None] * values.astype(jnp.float32)).astype(jnp.bfloat16)
    full_in, full_out = gradients(keys, scaled, w_gate, w_up, w_out)
    grad_in = lax.psum_scatter(full_in, ("seq", "outer"), scatter_dimension=0, tiled=True)
    grad_out = lax.psum_scatter(full_out, ("seq", "outer"), scatter_dimension=0, tiled=True)
    own_gate = lax.dynamic_slice_in_dim(w_gate, position * rows_gate, rows_gate, 0)
    own_up = lax.dynamic_slice_in_dim(w_up, position * rows_gate, rows_gate, 0)
    own_out = lax.dynamic_slice_in_dim(w_out, position * rows_out, rows_out, 0)
    new_gate = renorm(own_gate, grad_in[:, :hidden])
    new_up = renorm(own_up, grad_in[:, hidden:])
    new_out = renorm(own_out, grad_out)
    full_gate, full_up, full_out_w = (
        lax.all_gather(new_gate, ("seq", "outer"), axis=0, tiled=True),
        lax.all_gather(new_up, ("seq", "outer"), axis=0, tiled=True),
        lax.all_gather(new_out, ("seq", "outer"), axis=0, tiled=True),
    )
    return apply(queries, full_gate, full_up, full_out_w)


def chip_ring(mesh):
    seq = mesh.shape["seq"]
    try:
        places = [tuple(mesh.devices[0, s, 0].coords) for s in range(seq)]
    except (AttributeError, TypeError):
        return None
    columns = sorted({p[0] for p in places})
    if len(columns) != 2 or len({p[1] for p in places}) != 1:
        return None
    first = sorted((p[2], s) for s, p in enumerate(places) if p[0] == columns[0])
    second = sorted((p[2], s) for s, p in enumerate(places) if p[0] == columns[1])
    return [s for _, s in first] + [s for _, s in reversed(second)]


def add_grads(total, keys_part, scaled_part, w_gate, w_up, w_out):
    full_in, full_out = gradients(keys_part, scaled_part, w_gate, w_up, w_out)
    if total is None:
        return full_in, full_out
    return total[0] + full_in, total[1] + full_out


def make_local_ring(ring):
    chips = len(ring)
    cw_perm = []
    ccw_perm = []
    for p in range(chips):
        for c in range(2):
            cw_perm.append((ring[p] * 2 + c, ring[(p + 1) % chips] * 2 + c))
            ccw_perm.append((ring[p] * 2 + c, ring[(p - 1) % chips] * 2 + c))
    swap = [(i, i ^ 1) for i in range(chips * 2)]
    steps = chips // 2
    axes = ("seq", "outer")

    def split(chunks, half):
        keys_parts = []
        scaled_parts = []
        for ch in chunks:
            for j in range(ch.shape[0] // (2 * half)):
                keys_parts.append(ch[2 * j * half:(2 * j + 1) * half])
                scaled_parts.append(ch[(2 * j + 1) * half:(2 * j + 2) * half])
        return jnp.concatenate(keys_parts, axis=0), jnp.concatenate(scaled_parts, axis=0)

    def local_ring(keys, values, queries, learn_rate, w_gate_all, w_up_all, w_out_all):
        hidden = w_gate_all.shape[1]
        part = hidden // 2
        core = lax.axis_index("outer")
        w_gate = lax.dynamic_slice_in_dim(w_gate_all, core * part, part, axis=1)
        w_up = lax.dynamic_slice_in_dim(w_up_all, core * part, part, axis=1)
        w_out = lax.dynamic_slice_in_dim(w_out_all, core * part, part, axis=0)
        q_sib = lax.ppermute(queries, axes, swap)
        rows = keys.shape[0]
        halves = 2 if rows % 16 == 0 else 1
        half = rows // halves
        scaled = (learn_rate[:, None] * values.astype(jnp.float32)).astype(jnp.bfloat16)
        width = keys.shape[1]
        own = jnp.stack(
            [keys.reshape(halves, half, width), scaled.reshape(halves, half, width)], axis=1
        ).reshape(2 * rows, width)
        sib = lax.ppermute(own, axes, swap)
        total = add_grads(None, *split([own, sib], half), w_gate, w_up, w_out)
        arrived = [own, own]
        for step in range(1, steps + 1):
            last = step == steps and chips % 2 == 0
            if last and halves == 2:
                sent = [lax.ppermute(arrived[0][:2 * half], axes, cw_perm),
                        lax.ppermute(arrived[1][2 * half:], axes, ccw_perm)]
            elif last:
                sent = [lax.ppermute(arrived[0], axes, cw_perm)]
            else:
                sent = [lax.ppermute(arrived[0], axes, cw_perm),
                        lax.ppermute(arrived[1], axes, ccw_perm)]
            arrived = sent
            if step == steps:
                total, arrived = lax.optimization_barrier((total, arrived))
            from_sib = [lax.ppermute(chunk, axes, swap) for chunk in arrived]
            if step == steps:
                total = add_grads(total, *split(arrived, half), w_gate, w_up, w_out)
                total = add_grads(total, *split(from_sib, half), w_gate, w_up, w_out)
            else:
                total = add_grads(total, *split(arrived + from_sib, half), w_gate, w_up, w_out)
        full_in, full_out = total
        up_gate = w_gate.astype(jnp.float32) + full_in[:, :part]
        up_up = w_up.astype(jnp.float32) + full_in[:, part:]
        sums = jnp.stack([jnp.sum(up_gate * up_gate, axis=1), jnp.sum(up_up * up_up, axis=1)])
        sums = sums + lax.ppermute(sums, axes, swap)

        def scale(weight_all, update, row_sums):
            old = weight_all.astype(jnp.float32)
            factor = jnp.sqrt(jnp.mean(old * old, axis=1, keepdims=True) + epsilon) / jnp.sqrt(
                row_sums[:, None] / hidden + epsilon
            )
            return (update * factor).astype(jnp.bfloat16)

        new_gate = scale(w_gate_all, up_gate, sums[0])
        new_up = scale(w_up_all, up_up, sums[1])
        new_out = renorm(w_out, full_out)
        new_gate, new_up, new_out = lax.optimization_barrier((new_gate, new_up, new_out))
        rows = queries.shape[0]
        both_queries = jnp.concatenate([queries, q_sib], axis=0)
        q_gate = jnp.dot(both_queries, new_gate, preferred_element_type=jnp.float32)
        q_up = jnp.dot(both_queries, new_up, preferred_element_type=jnp.float32)
        q_act = (jax.nn.silu(q_gate) * q_up).astype(jnp.bfloat16)
        partial = jnp.dot(q_act, new_out, preferred_element_type=jnp.float32)
        from_sib = lax.ppermute(partial[rows:], axes, swap)
        return (partial[:rows] + from_sib).astype(jnp.bfloat16)

    return local_ring


def solution(mesh):
    placed = (
        P(("grp", "seq", "outer"), None),
        P(("grp", "seq", "outer"), None),
        P(("grp", "seq", "outer"), None),
        P(("grp", "seq", "outer")),
        P("grp", None),
        P("grp", None),
        P("grp", None),
    )
    ring = chip_ring(mesh) if mesh.shape["outer"] == 2 else None
    local_ring = make_local_ring(ring) if ring else None

    def run(keys, values, queries, learn_rate, w_gate, w_up, w_out):
        per_part = keys.shape[0] // mesh.shape["grp"]
        gathered_bytes = 2 * per_part * keys.shape[1] * keys.dtype.itemsize
        if gathered_bytes > GATHER_LIMIT_BYTES:
            body = local_scatter
        elif local_ring is not None and w_gate.shape[1] % 256 == 0:
            body = local_ring
        else:
            body = local_gather
        return jax.shard_map(
            body,
            mesh=mesh,
            in_specs=placed,
            out_specs=P(("grp", "seq", "outer"), None),
            check_vma=False,
        )(keys, values, queries, learn_rate, w_gate, w_up, w_out)

    return run
```

```python
import jax
import jax.numpy as jnp
from jax import lax
from jax.sharding import PartitionSpec as P

epsilon = 1e-06
GATHER_LIMIT_BYTES = 16 * 1024 * 1024


def silu_grad(inputs):
    sigma = jax.nn.sigmoid(inputs)
    return sigma * (1.0 + inputs * (1.0 - sigma))


def renorm(weight, grads):
    old = weight.astype(jnp.float32)
    update = old + grads
    factor = jnp.sqrt(jnp.mean(old * old, axis=1, keepdims=True) + epsilon) / jnp.sqrt(
        jnp.mean(update * update, axis=1, keepdims=True) + epsilon
    )
    return (update * factor).astype(jnp.bfloat16)


contract_last = (((1,), (1,)), ((), ()))
contract_first = (((0,), (0,)), ((), ()))


def gradients(keys, scaled, w_gate, w_up, w_out):
    gate_pre = jnp.dot(keys, w_gate, preferred_element_type=jnp.float32)
    up_pre = jnp.dot(keys, w_up, preferred_element_type=jnp.float32)
    back_grad = lax.dot_general(scaled, w_out, contract_last, preferred_element_type=jnp.float32)
    activation = (jax.nn.silu(gate_pre) * up_pre).astype(jnp.bfloat16)
    d_gate = (back_grad * up_pre * silu_grad(gate_pre)).astype(jnp.bfloat16)
    d_up = (back_grad * jax.nn.silu(gate_pre)).astype(jnp.bfloat16)
    both_grads = jnp.concatenate([d_gate, d_up], axis=1)
    full_in = lax.dot_general(keys, both_grads, contract_first, preferred_element_type=jnp.float32)
    full_out = lax.dot_general(activation, scaled, contract_first, preferred_element_type=jnp.float32)
    return full_in, full_out


def apply(queries, full_gate, full_up, full_out_w):
    q_gate = jnp.dot(queries, full_gate, preferred_element_type=jnp.float32)
    q_up = jnp.dot(queries, full_up, preferred_element_type=jnp.float32)
    q_act = (jax.nn.silu(q_gate) * q_up).astype(jnp.bfloat16)
    return jnp.dot(q_act, full_out_w, preferred_element_type=jnp.float32).astype(jnp.bfloat16)


def local_gather(keys, values, queries, learn_rate, w_gate, w_up, w_out):
    hidden = w_gate.shape[1]
    shards = lax.axis_size(("seq", "outer"))
    rows = keys.shape[0]
    width = keys.shape[1]
    scaled = (learn_rate[:, None] * values.astype(jnp.float32)).astype(jnp.bfloat16)
    both = jnp.concatenate([keys, scaled], axis=0)
    full = lax.all_gather(both, ("seq", "outer"), axis=0, tiled=True)
    full = full.reshape(shards, 2, rows, width)
    all_keys = full[:, 0].reshape(shards * rows, width)
    all_scaled = full[:, 1].reshape(shards * rows, width)
    full_in, full_out = gradients(all_keys, all_scaled, w_gate, w_up, w_out)
    new_gate = renorm(w_gate, full_in[:, :hidden])
    new_up = renorm(w_up, full_in[:, hidden:])
    new_out = renorm(w_out, full_out)
    return apply(queries, new_gate, new_up, new_out)


def local_scatter(keys, values, queries, learn_rate, w_gate, w_up, w_out):
    hidden = w_gate.shape[1]
    shards = lax.axis_size(("seq", "outer"))
    rows_gate = w_gate.shape[0] // shards
    rows_out = w_out.shape[0] // shards
    position = lax.axis_index(("seq", "outer"))
    scaled = (learn_rate[:, None] * values.astype(jnp.float32)).astype(jnp.bfloat16)
    full_in, full_out = gradients(keys, scaled, w_gate, w_up, w_out)
    grad_in = lax.psum_scatter(full_in, ("seq", "outer"), scatter_dimension=0, tiled=True)
    grad_out = lax.psum_scatter(full_out, ("seq", "outer"), scatter_dimension=0, tiled=True)
    own_gate = lax.dynamic_slice_in_dim(w_gate, position * rows_gate, rows_gate, 0)
    own_up = lax.dynamic_slice_in_dim(w_up, position * rows_gate, rows_gate, 0)
    own_out = lax.dynamic_slice_in_dim(w_out, position * rows_out, rows_out, 0)
    new_gate = renorm(own_gate, grad_in[:, :hidden])
    new_up = renorm(own_up, grad_in[:, hidden:])
    new_out = renorm(own_out, grad_out)
    full_gate, full_up, full_out_w = (
        lax.all_gather(new_gate, ("seq", "outer"), axis=0, tiled=True),
        lax.all_gather(new_up, ("seq", "outer"), axis=0, tiled=True),
        lax.all_gather(new_out, ("seq", "outer"), axis=0, tiled=True),
    )
    return apply(queries, full_gate, full_up, full_out_w)


def chip_ring(mesh):
    seq = mesh.shape["seq"]
    try:
        places = [tuple(mesh.devices[0, s, 0].coords) for s in range(seq)]
    except (AttributeError, TypeError):
        return None
    columns = sorted({p[0] for p in places})
    if len(columns) != 2 or len({p[1] for p in places}) != 1:
        return None
    first = sorted((p[2], s) for s, p in enumerate(places) if p[0] == columns[0])
    second = sorted((p[2], s) for s, p in enumerate(places) if p[0] == columns[1])
    return [s for _, s in first] + [s for _, s in reversed(second)]


def add_grads(total, keys_part, scaled_part, w_gate, w_up, w_out):
    full_in, full_out = gradients(keys_part, scaled_part, w_gate, w_up, w_out)
    if total is None:
        return full_in, full_out
    return total[0] + full_in, total[1] + full_out


def make_local_ring(ring):
    chips = len(ring)
    cw_perm = []
    ccw_perm = []
    for p in range(chips):
        for c in range(2):
            cw_perm.append((ring[p] * 2 + c, ring[(p + 1) % chips] * 2 + c))
            ccw_perm.append((ring[p] * 2 + c, ring[(p - 1) % chips] * 2 + c))
    swap = [(i, i ^ 1) for i in range(chips * 2)]
    steps = chips // 2
    axes = ("seq", "outer")

    def split(chunks, half):
        keys_parts = []
        scaled_parts = []
        for ch in chunks:
            for j in range(ch.shape[0] // (2 * half)):
                keys_parts.append(ch[2 * j * half:(2 * j + 1) * half])
                scaled_parts.append(ch[(2 * j + 1) * half:(2 * j + 2) * half])
        return jnp.concatenate(keys_parts, axis=0), jnp.concatenate(scaled_parts, axis=0)

    def local_ring(keys, values, queries, learn_rate, w_gate_all, w_up_all, w_out_all):
        hidden = w_gate_all.shape[1]
        part = hidden // 2
        core = lax.axis_index("outer")
        w_gate = lax.dynamic_slice_in_dim(w_gate_all, core * part, part, axis=1)
        w_up = lax.dynamic_slice_in_dim(w_up_all, core * part, part, axis=1)
        w_out = lax.dynamic_slice_in_dim(w_out_all, core * part, part, axis=0)
        q_sib = lax.ppermute(queries, axes, swap)
        rows = keys.shape[0]
        halves = 2 if rows % 16 == 0 else 1
        half = rows // halves
        scaled = (learn_rate[:, None] * values.astype(jnp.float32)).astype(jnp.bfloat16)
        width = keys.shape[1]
        own = jnp.stack(
            [keys.reshape(halves, half, width), scaled.reshape(halves, half, width)], axis=1
        ).reshape(2 * rows, width)
        sib = lax.ppermute(own, axes, swap)
        total = add_grads(None, *split([own, sib], half), w_gate, w_up, w_out)
        arrived = [own, own]
        for step in range(1, steps + 1):
            last = step == steps and chips % 2 == 0
            if last and halves == 2:
                sent = [lax.ppermute(arrived[0][:2 * half], axes, cw_perm),
                        lax.ppermute(arrived[1][2 * half:], axes, ccw_perm)]
            elif last:
                sent = [lax.ppermute(arrived[0], axes, cw_perm)]
            else:
                sent = [lax.ppermute(arrived[0], axes, cw_perm),
                        lax.ppermute(arrived[1], axes, ccw_perm)]
            arrived = sent
            if step == steps:
                total, arrived = lax.optimization_barrier((total, arrived))
            from_sib = [lax.ppermute(chunk, axes, swap) for chunk in arrived]
            if step == steps:
                total = add_grads(total, *split(arrived, half), w_gate, w_up, w_out)
                total = add_grads(total, *split(from_sib, half), w_gate, w_up, w_out)
            else:
                total = add_grads(total, *split(arrived + from_sib, half), w_gate, w_up, w_out)
        full_in, full_out = total
        up_gate = w_gate.astype(jnp.float32) + full_in[:, :part]
        up_up = w_up.astype(jnp.float32) + full_in[:, part:]
        sums = jnp.stack([jnp.sum(up_gate * up_gate, axis=1), jnp.sum(up_up * up_up, axis=1)])
        sums = sums + lax.ppermute(sums, axes, swap)

        def scale(weight_all, update, row_sums):
            old = weight_all.astype(jnp.float32)
            factor = jnp.sqrt(jnp.mean(old * old, axis=1, keepdims=True) + epsilon) / jnp.sqrt(
                row_sums[:, None] / hidden + epsilon
            )
            return (update * factor).astype(jnp.bfloat16)

        new_gate = scale(w_gate_all, up_gate, sums[0])
        new_up = scale(w_up_all, up_up, sums[1])
        new_out = renorm(w_out, full_out)
        new_gate, new_up, new_out = lax.optimization_barrier((new_gate, new_up, new_out))
        rows = queries.shape[0]
        sib_out = lax.ppermute(new_out, axes, swap)
        both_queries = jnp.concatenate([queries, q_sib], axis=0)
        q_gate = jnp.dot(both_queries, new_gate, preferred_element_type=jnp.float32)
        q_up = jnp.dot(both_queries, new_up, preferred_element_type=jnp.float32)
        q_act = (jax.nn.silu(q_gate) * q_up).astype(jnp.bfloat16)
        sib_act = lax.ppermute(q_act[rows:], axes, swap)
        result = jnp.dot(q_act[:rows], new_out, preferred_element_type=jnp.float32) + jnp.dot(
            sib_act, sib_out, preferred_element_type=jnp.float32
        )
        return result.astype(jnp.bfloat16)

    return local_ring


def solution(mesh):
    placed = (
        P(("grp", "seq", "outer"), None),
        P(("grp", "seq", "outer"), None),
        P(("grp", "seq", "outer"), None),
        P(("grp", "seq", "outer")),
        P("grp", None),
        P("grp", None),
        P("grp", None),
    )
    ring = chip_ring(mesh) if mesh.shape["outer"] == 2 else None
    local_ring = make_local_ring(ring) if ring else None

    def run(keys, values, queries, learn_rate, w_gate, w_up, w_out):
        per_part = keys.shape[0] // mesh.shape["grp"]
        gathered_bytes = 2 * per_part * keys.shape[1] * keys.dtype.itemsize
        if gathered_bytes > GATHER_LIMIT_BYTES:
            body = local_scatter
        elif local_ring is not None and w_gate.shape[1] % 256 == 0:
            body = local_ring
        else:
            body = local_gather
        return jax.shard_map(
            body,
            mesh=mesh,
            in_specs=placed,
            out_specs=P(("grp", "seq", "outer"), None),
            check_vma=False,
        )(keys, values, queries, learn_rate, w_gate, w_up, w_out)

    return run
```

```python
import jax
import jax.numpy as jnp
from jax import lax
from jax.sharding import PartitionSpec as P

epsilon = 1e-06
GATHER_LIMIT_BYTES = 16 * 1024 * 1024


def silu_grad(inputs):
    sigma = jax.nn.sigmoid(inputs)
    return sigma * (1.0 + inputs * (1.0 - sigma))


def renorm(weight, grads):
    old = weight.astype(jnp.float32)
    update = old + grads
    factor = jnp.sqrt(jnp.mean(old * old, axis=1, keepdims=True) + epsilon) / jnp.sqrt(
        jnp.mean(update * update, axis=1, keepdims=True) + epsilon
    )
    return (update * factor).astype(jnp.bfloat16)


contract_last = (((1,), (1,)), ((), ()))
contract_first = (((0,), (0,)), ((), ()))


def gradients(keys, scaled, w_gate, w_up, w_out):
    hidden = w_gate.shape[1]
    both_pre = jnp.dot(keys, jnp.concatenate([w_gate, w_up], axis=1), preferred_element_type=jnp.float32)
    gate_pre = both_pre[:, :hidden]
    up_pre = both_pre[:, hidden:]
    back_grad = lax.dot_general(scaled, w_out, contract_last, preferred_element_type=jnp.float32)
    activation = (jax.nn.silu(gate_pre) * up_pre).astype(jnp.bfloat16)
    d_gate = (back_grad * up_pre * silu_grad(gate_pre)).astype(jnp.bfloat16)
    d_up = (back_grad * jax.nn.silu(gate_pre)).astype(jnp.bfloat16)
    both_grads = jnp.concatenate([d_gate, d_up], axis=1)
    full_in = lax.dot_general(keys, both_grads, contract_first, preferred_element_type=jnp.float32)
    full_out = lax.dot_general(activation, scaled, contract_first, preferred_element_type=jnp.float32)
    return full_in, full_out


def apply(queries, full_gate, full_up, full_out_w):
    q_gate = jnp.dot(queries, full_gate, preferred_element_type=jnp.float32)
    q_up = jnp.dot(queries, full_up, preferred_element_type=jnp.float32)
    q_act = (jax.nn.silu(q_gate) * q_up).astype(jnp.bfloat16)
    return jnp.dot(q_act, full_out_w, preferred_element_type=jnp.float32).astype(jnp.bfloat16)


def local_gather(keys, values, queries, learn_rate, w_gate, w_up, w_out):
    hidden = w_gate.shape[1]
    shards = lax.axis_size(("seq", "outer"))
    rows = keys.shape[0]
    width = keys.shape[1]
    scaled = (learn_rate[:, None] * values.astype(jnp.float32)).astype(jnp.bfloat16)
    both = jnp.concatenate([keys, scaled], axis=0)
    full = lax.all_gather(both, ("seq", "outer"), axis=0, tiled=True)
    full = full.reshape(shards, 2, rows, width)
    all_keys = full[:, 0].reshape(shards * rows, width)
    all_scaled = full[:, 1].reshape(shards * rows, width)
    full_in, full_out = gradients(all_keys, all_scaled, w_gate, w_up, w_out)
    new_gate = renorm(w_gate, full_in[:, :hidden])
    new_up = renorm(w_up, full_in[:, hidden:])
    new_out = renorm(w_out, full_out)
    return apply(queries, new_gate, new_up, new_out)


def local_scatter(keys, values, queries, learn_rate, w_gate, w_up, w_out):
    hidden = w_gate.shape[1]
    shards = lax.axis_size(("seq", "outer"))
    rows_gate = w_gate.shape[0] // shards
    rows_out = w_out.shape[0] // shards
    position = lax.axis_index(("seq", "outer"))
    scaled = (learn_rate[:, None] * values.astype(jnp.float32)).astype(jnp.bfloat16)
    full_in, full_out = gradients(keys, scaled, w_gate, w_up, w_out)
    grad_in = lax.psum_scatter(full_in, ("seq", "outer"), scatter_dimension=0, tiled=True)
    grad_out = lax.psum_scatter(full_out, ("seq", "outer"), scatter_dimension=0, tiled=True)
    own_gate = lax.dynamic_slice_in_dim(w_gate, position * rows_gate, rows_gate, 0)
    own_up = lax.dynamic_slice_in_dim(w_up, position * rows_gate, rows_gate, 0)
    own_out = lax.dynamic_slice_in_dim(w_out, position * rows_out, rows_out, 0)
    new_gate = renorm(own_gate, grad_in[:, :hidden])
    new_up = renorm(own_up, grad_in[:, hidden:])
    new_out = renorm(own_out, grad_out)
    full_gate, full_up, full_out_w = (
        lax.all_gather(new_gate, ("seq", "outer"), axis=0, tiled=True),
        lax.all_gather(new_up, ("seq", "outer"), axis=0, tiled=True),
        lax.all_gather(new_out, ("seq", "outer"), axis=0, tiled=True),
    )
    return apply(queries, full_gate, full_up, full_out_w)


def chip_ring(mesh):
    seq = mesh.shape["seq"]
    try:
        places = [tuple(mesh.devices[0, s, 0].coords) for s in range(seq)]
    except (AttributeError, TypeError):
        return None
    columns = sorted({p[0] for p in places})
    if len(columns) != 2 or len({p[1] for p in places}) != 1:
        return None
    first = sorted((p[2], s) for s, p in enumerate(places) if p[0] == columns[0])
    second = sorted((p[2], s) for s, p in enumerate(places) if p[0] == columns[1])
    return [s for _, s in first] + [s for _, s in reversed(second)]


def add_grads(total, keys_part, scaled_part, w_gate, w_up, w_out):
    full_in, full_out = gradients(keys_part, scaled_part, w_gate, w_up, w_out)
    if total is None:
        return full_in, full_out
    return total[0] + full_in, total[1] + full_out


def make_local_ring(ring):
    chips = len(ring)
    cw_perm = []
    ccw_perm = []
    for p in range(chips):
        for c in range(2):
            cw_perm.append((ring[p] * 2 + c, ring[(p + 1) % chips] * 2 + c))
            ccw_perm.append((ring[p] * 2 + c, ring[(p - 1) % chips] * 2 + c))
    swap = [(i, i ^ 1) for i in range(chips * 2)]
    steps = chips // 2
    axes = ("seq", "outer")

    def split(chunks, half):
        keys_parts = []
        scaled_parts = []
        for ch in chunks:
            for j in range(ch.shape[0] // (2 * half)):
                keys_parts.append(ch[2 * j * half:(2 * j + 1) * half])
                scaled_parts.append(ch[(2 * j + 1) * half:(2 * j + 2) * half])
        return jnp.concatenate(keys_parts, axis=0), jnp.concatenate(scaled_parts, axis=0)

    def local_ring(keys, values, queries, learn_rate, w_gate, w_up, w_out):
        hidden = w_gate.shape[1]
        rows = keys.shape[0]
        halves = 2 if rows % 16 == 0 else 1
        half = rows // halves
        scaled = (learn_rate[:, None] * values.astype(jnp.float32)).astype(jnp.bfloat16)
        width = keys.shape[1]
        own = jnp.stack(
            [keys.reshape(halves, half, width), scaled.reshape(halves, half, width)], axis=1
        ).reshape(2 * rows, width)
        sib = lax.ppermute(own, axes, swap)
        total = add_grads(None, *split([own, sib], half), w_gate, w_up, w_out)
        arrived = [own, own]
        for step in range(1, steps + 1):
            last = step == steps and chips % 2 == 0
            if last and halves == 2:
                sent = [lax.ppermute(arrived[0][:2 * half], axes, cw_perm),
                        lax.ppermute(arrived[1][2 * half:], axes, ccw_perm)]
            elif last:
                sent = [lax.ppermute(arrived[0], axes, cw_perm)]
            else:
                sent = [lax.ppermute(arrived[0], axes, cw_perm),
                        lax.ppermute(arrived[1], axes, ccw_perm)]
            arrived = sent
            if step == steps:
                total, arrived = lax.optimization_barrier((total, arrived))
            from_sib = [lax.ppermute(chunk, axes, swap) for chunk in arrived]
            if step == steps:
                total = add_grads(total, *split(arrived, half), w_gate, w_up, w_out)
                total = add_grads(total, *split(from_sib, half), w_gate, w_up, w_out)
            else:
                total = add_grads(total, *split(arrived + from_sib, half), w_gate, w_up, w_out)
        full_in, full_out = total
        new_gate = renorm(w_gate, full_in[:, :hidden])
        new_up = renorm(w_up, full_in[:, hidden:])
        new_out = renorm(w_out, full_out)
        new_gate, new_up, new_out = lax.optimization_barrier((new_gate, new_up, new_out))
        return apply(queries, new_gate, new_up, new_out)

    return local_ring


def solution(mesh):
    placed = (
        P(("grp", "seq", "outer"), None),
        P(("grp", "seq", "outer"), None),
        P(("grp", "seq", "outer"), None),
        P(("grp", "seq", "outer")),
        P("grp", None),
        P("grp", None),
        P("grp", None),
    )
    ring = chip_ring(mesh) if mesh.shape["outer"] == 2 else None
    local_ring = make_local_ring(ring) if ring else None

    def run(keys, values, queries, learn_rate, w_gate, w_up, w_out):
        per_part = keys.shape[0] // mesh.shape["grp"]
        gathered_bytes = 2 * per_part * keys.shape[1] * keys.dtype.itemsize
        if gathered_bytes > GATHER_LIMIT_BYTES:
            body = local_scatter
        elif local_ring is not None:
            body = local_ring
        else:
            body = local_gather
        return jax.shard_map(
            body,
            mesh=mesh,
            in_specs=placed,
            out_specs=P(("grp", "seq", "outer"), None),
            check_vma=False,
        )(keys, values, queries, learn_rate, w_gate, w_up, w_out)

    return run
```

```python
import jax
import jax.numpy as jnp
from jax import lax
from jax.sharding import PartitionSpec as P

epsilon = 1e-06
GATHER_LIMIT_BYTES = 16 * 1024 * 1024


def silu_grad(inputs):
    sigma = jax.nn.sigmoid(inputs)
    return sigma * (1.0 + inputs * (1.0 - sigma))


def renorm(weight, grads):
    old = weight.astype(jnp.float32)
    update = old + grads
    factor = jnp.sqrt(jnp.mean(old * old, axis=1, keepdims=True) + epsilon) / jnp.sqrt(
        jnp.mean(update * update, axis=1, keepdims=True) + epsilon
    )
    return (update * factor).astype(jnp.bfloat16)


contract_last = (((1,), (1,)), ((), ()))
contract_first = (((0,), (0,)), ((), ()))


def gradients(keys, scaled, w_gate, w_up, w_out):
    gate_pre = jnp.dot(keys, w_gate, preferred_element_type=jnp.float32)
    up_pre = jnp.dot(keys, w_up, preferred_element_type=jnp.float32)
    back_grad = lax.dot_general(scaled, w_out, contract_last, preferred_element_type=jnp.float32)
    activation = (jax.nn.silu(gate_pre) * up_pre).astype(jnp.bfloat16)
    d_gate = (back_grad * up_pre * silu_grad(gate_pre)).astype(jnp.bfloat16)
    d_up = (back_grad * jax.nn.silu(gate_pre)).astype(jnp.bfloat16)
    both_grads = jnp.concatenate([d_gate, d_up], axis=1)
    full_in = lax.dot_general(keys, both_grads, contract_first, preferred_element_type=jnp.float32)
    full_out = lax.dot_general(activation, scaled, contract_first, preferred_element_type=jnp.float32)
    return full_in, full_out


def apply(queries, full_gate, full_up, full_out_w):
    q_gate = jnp.dot(queries, full_gate, preferred_element_type=jnp.float32)
    q_up = jnp.dot(queries, full_up, preferred_element_type=jnp.float32)
    q_act = (jax.nn.silu(q_gate) * q_up).astype(jnp.bfloat16)
    return jnp.dot(q_act, full_out_w, preferred_element_type=jnp.float32).astype(jnp.bfloat16)


def local_gather(keys, values, queries, learn_rate, w_gate, w_up, w_out):
    hidden = w_gate.shape[1]
    shards = lax.axis_size(("seq", "outer"))
    rows = keys.shape[0]
    width = keys.shape[1]
    scaled = (learn_rate[:, None] * values.astype(jnp.float32)).astype(jnp.bfloat16)
    both = jnp.concatenate([keys, scaled], axis=0)
    full = lax.all_gather(both, ("seq", "outer"), axis=0, tiled=True)
    full = full.reshape(shards, 2, rows, width)
    all_keys = full[:, 0].reshape(shards * rows, width)
    all_scaled = full[:, 1].reshape(shards * rows, width)
    full_in, full_out = gradients(all_keys, all_scaled, w_gate, w_up, w_out)
    new_gate = renorm(w_gate, full_in[:, :hidden])
    new_up = renorm(w_up, full_in[:, hidden:])
    new_out = renorm(w_out, full_out)
    return apply(queries, new_gate, new_up, new_out)


def local_scatter(keys, values, queries, learn_rate, w_gate, w_up, w_out):
    hidden = w_gate.shape[1]
    shards = lax.axis_size(("seq", "outer"))
    rows_gate = w_gate.shape[0] // shards
    rows_out = w_out.shape[0] // shards
    position = lax.axis_index(("seq", "outer"))
    scaled = (learn_rate[:, None] * values.astype(jnp.float32)).astype(jnp.bfloat16)
    full_in, full_out = gradients(keys, scaled, w_gate, w_up, w_out)
    grad_in = lax.psum_scatter(full_in, ("seq", "outer"), scatter_dimension=0, tiled=True)
    grad_out = lax.psum_scatter(full_out, ("seq", "outer"), scatter_dimension=0, tiled=True)
    own_gate = lax.dynamic_slice_in_dim(w_gate, position * rows_gate, rows_gate, 0)
    own_up = lax.dynamic_slice_in_dim(w_up, position * rows_gate, rows_gate, 0)
    own_out = lax.dynamic_slice_in_dim(w_out, position * rows_out, rows_out, 0)
    new_gate = renorm(own_gate, grad_in[:, :hidden])
    new_up = renorm(own_up, grad_in[:, hidden:])
    new_out = renorm(own_out, grad_out)
    full_gate, full_up, full_out_w = (
        lax.all_gather(new_gate, ("seq", "outer"), axis=0, tiled=True),
        lax.all_gather(new_up, ("seq", "outer"), axis=0, tiled=True),
        lax.all_gather(new_out, ("seq", "outer"), axis=0, tiled=True),
    )
    return apply(queries, full_gate, full_up, full_out_w)


def chip_ring(mesh):
    seq = mesh.shape["seq"]
    try:
        places = [tuple(mesh.devices[0, s, 0].coords) for s in range(seq)]
    except (AttributeError, TypeError):
        return None
    columns = sorted({p[0] for p in places})
    if len(columns) != 2 or len({p[1] for p in places}) != 1:
        return None
    first = sorted((p[2], s) for s, p in enumerate(places) if p[0] == columns[0])
    second = sorted((p[2], s) for s, p in enumerate(places) if p[0] == columns[1])
    return [s for _, s in first] + [s for _, s in reversed(second)]


def add_grads(total, keys_part, scaled_part, w_gate, w_up, w_out):
    full_in, full_out = gradients(keys_part, scaled_part, w_gate, w_up, w_out)
    if total is None:
        return full_in, full_out
    return total[0] + full_in, total[1] + full_out


def make_local_ring(ring):
    chips = len(ring)
    cw_perm = []
    ccw_perm = []
    for p in range(chips):
        for c in range(2):
            cw_perm.append((ring[p] * 2 + c, ring[(p + 1) % chips] * 2 + c))
            ccw_perm.append((ring[p] * 2 + c, ring[(p - 1) % chips] * 2 + c))
    swap = [(i, i ^ 1) for i in range(chips * 2)]
    steps = chips // 2
    axes = ("seq", "outer")

    def split(chunks, half):
        keys_parts = []
        scaled_parts = []
        for ch in chunks:
            for j in range(ch.shape[0] // (2 * half)):
                keys_parts.append(ch[2 * j * half:(2 * j + 1) * half])
                scaled_parts.append(ch[(2 * j + 1) * half:(2 * j + 2) * half])
        return jnp.concatenate(keys_parts, axis=0), jnp.concatenate(scaled_parts, axis=0)

    def local_ring(keys, values, queries, learn_rate, w_gate, w_up, w_out):
        hidden = w_gate.shape[1]
        rows = keys.shape[0]
        halves = 2 if rows % 16 == 0 else 1
        half = rows // halves
        scaled = (learn_rate[:, None] * values.astype(jnp.float32)).astype(jnp.bfloat16)
        width = keys.shape[1]
        own = jnp.stack(
            [keys.reshape(halves, half, width), scaled.reshape(halves, half, width)], axis=1
        ).reshape(2 * rows, width)
        sib = lax.ppermute(own, axes, swap)
        total = add_grads(None, *split([own, sib], half), w_gate, w_up, w_out)
        arrived = [own, own]
        for step in range(1, steps + 1):
            last = step == steps and chips % 2 == 0
            if last and halves == 2:
                sent = [lax.ppermute(arrived[0][:2 * half], axes, cw_perm),
                        lax.ppermute(arrived[1][2 * half:], axes, ccw_perm)]
            elif last:
                sent = [lax.ppermute(arrived[0], axes, cw_perm)]
            else:
                sent = [lax.ppermute(arrived[0], axes, cw_perm),
                        lax.ppermute(arrived[1], axes, ccw_perm)]
            arrived = sent
            if step == steps:
                total, arrived = lax.optimization_barrier((total, arrived))
            from_sib = [lax.ppermute(chunk, axes, swap) for chunk in arrived]
            if step >= steps - 1:
                total = add_grads(total, *split(arrived, half), w_gate, w_up, w_out)
                total = add_grads(total, *split(from_sib, half), w_gate, w_up, w_out)
            else:
                total = add_grads(total, *split(arrived + from_sib, half), w_gate, w_up, w_out)
        full_in, full_out = total
        new_gate = renorm(w_gate, full_in[:, :hidden])
        new_up = renorm(w_up, full_in[:, hidden:])
        new_out = renorm(w_out, full_out)
        new_gate, new_up, new_out = lax.optimization_barrier((new_gate, new_up, new_out))
        return apply(queries, new_gate, new_up, new_out)

    return local_ring


def solution(mesh):
    placed = (
        P(("grp", "seq", "outer"), None),
        P(("grp", "seq", "outer"), None),
        P(("grp", "seq", "outer"), None),
        P(("grp", "seq", "outer")),
        P("grp", None),
        P("grp", None),
        P("grp", None),
    )
    ring = chip_ring(mesh) if mesh.shape["outer"] == 2 else None
    local_ring = make_local_ring(ring) if ring else None

    def run(keys, values, queries, learn_rate, w_gate, w_up, w_out):
        per_part = keys.shape[0] // mesh.shape["grp"]
        gathered_bytes = 2 * per_part * keys.shape[1] * keys.dtype.itemsize
        if gathered_bytes > GATHER_LIMIT_BYTES:
            body = local_scatter
        elif local_ring is not None:
            body = local_ring
        else:
            body = local_gather
        return jax.shard_map(
            body,
            mesh=mesh,
            in_specs=placed,
            out_specs=P(("grp", "seq", "outer"), None),
            check_vma=False,
        )(keys, values, queries, learn_rate, w_gate, w_up, w_out)

    return run
```

```python
import jax
import jax.numpy as jnp
from jax import lax
from jax.sharding import PartitionSpec as P

epsilon = 1e-06
GATHER_LIMIT_BYTES = 16 * 1024 * 1024


def silu_grad(inputs):
    sigma = jax.nn.sigmoid(inputs)
    return sigma * (1.0 + inputs * (1.0 - sigma))


def renorm(weight, grads):
    old = weight.astype(jnp.float32)
    update = old + grads
    factor = jnp.sqrt(jnp.mean(old * old, axis=1, keepdims=True) + epsilon) / jnp.sqrt(
        jnp.mean(update * update, axis=1, keepdims=True) + epsilon
    )
    return (update * factor).astype(jnp.bfloat16)


contract_last = (((1,), (1,)), ((), ()))
contract_first = (((0,), (0,)), ((), ()))


def gradients(keys, scaled, w_gate, w_up, w_out):
    gate_pre = jnp.dot(keys, w_gate, preferred_element_type=jnp.float32)
    up_pre = jnp.dot(keys, w_up, preferred_element_type=jnp.float32)
    back_grad = lax.dot_general(scaled, w_out, contract_last, preferred_element_type=jnp.float32)
    activation = (jax.nn.silu(gate_pre) * up_pre).astype(jnp.bfloat16)
    d_gate = (back_grad * up_pre * silu_grad(gate_pre)).astype(jnp.bfloat16)
    d_up = (back_grad * jax.nn.silu(gate_pre)).astype(jnp.bfloat16)
    both_grads = jnp.concatenate([d_gate, d_up], axis=1)
    full_in = lax.dot_general(keys, both_grads, contract_first, preferred_element_type=jnp.float32)
    full_out = lax.dot_general(activation, scaled, contract_first, preferred_element_type=jnp.float32)
    return full_in, full_out


def apply(queries, full_gate, full_up, full_out_w):
    q_gate = jnp.dot(queries, full_gate, preferred_element_type=jnp.float32)
    q_up = jnp.dot(queries, full_up, preferred_element_type=jnp.float32)
    q_act = (jax.nn.silu(q_gate) * q_up).astype(jnp.bfloat16)
    return jnp.dot(q_act, full_out_w, preferred_element_type=jnp.float32).astype(jnp.bfloat16)


def local_gather(keys, values, queries, learn_rate, w_gate, w_up, w_out):
    hidden = w_gate.shape[1]
    shards = lax.axis_size(("seq", "outer"))
    rows = keys.shape[0]
    width = keys.shape[1]
    scaled = (learn_rate[:, None] * values.astype(jnp.float32)).astype(jnp.bfloat16)
    both = jnp.concatenate([keys, scaled], axis=0)
    full = lax.all_gather(both, ("seq", "outer"), axis=0, tiled=True)
    full = full.reshape(shards, 2, rows, width)
    all_keys = full[:, 0].reshape(shards * rows, width)
    all_scaled = full[:, 1].reshape(shards * rows, width)
    full_in, full_out = gradients(all_keys, all_scaled, w_gate, w_up, w_out)
    new_gate = renorm(w_gate, full_in[:, :hidden])
    new_up = renorm(w_up, full_in[:, hidden:])
    new_out = renorm(w_out, full_out)
    return apply(queries, new_gate, new_up, new_out)


def local_scatter(keys, values, queries, learn_rate, w_gate, w_up, w_out):
    hidden = w_gate.shape[1]
    shards = lax.axis_size(("seq", "outer"))
    rows_gate = w_gate.shape[0] // shards
    rows_out = w_out.shape[0] // shards
    position = lax.axis_index(("seq", "outer"))
    scaled = (learn_rate[:, None] * values.astype(jnp.float32)).astype(jnp.bfloat16)
    full_in, full_out = gradients(keys, scaled, w_gate, w_up, w_out)
    grad_in = lax.psum_scatter(full_in, ("seq", "outer"), scatter_dimension=0, tiled=True)
    grad_out = lax.psum_scatter(full_out, ("seq", "outer"), scatter_dimension=0, tiled=True)
    own_gate = lax.dynamic_slice_in_dim(w_gate, position * rows_gate, rows_gate, 0)
    own_up = lax.dynamic_slice_in_dim(w_up, position * rows_gate, rows_gate, 0)
    own_out = lax.dynamic_slice_in_dim(w_out, position * rows_out, rows_out, 0)
    new_gate = renorm(own_gate, grad_in[:, :hidden])
    new_up = renorm(own_up, grad_in[:, hidden:])
    new_out = renorm(own_out, grad_out)
    full_gate, full_up, full_out_w = (
        lax.all_gather(new_gate, ("seq", "outer"), axis=0, tiled=True),
        lax.all_gather(new_up, ("seq", "outer"), axis=0, tiled=True),
        lax.all_gather(new_out, ("seq", "outer"), axis=0, tiled=True),
    )
    return apply(queries, full_gate, full_up, full_out_w)


def chip_ring(mesh):
    seq = mesh.shape["seq"]
    try:
        places = [tuple(mesh.devices[0, s, 0].coords) for s in range(seq)]
    except (AttributeError, TypeError):
        return None
    columns = sorted({p[0] for p in places})
    if len(columns) != 2 or len({p[1] for p in places}) != 1:
        return None
    first = sorted((p[2], s) for s, p in enumerate(places) if p[0] == columns[0])
    second = sorted((p[2], s) for s, p in enumerate(places) if p[0] == columns[1])
    return [s for _, s in first] + [s for _, s in reversed(second)]


def add_grads(total, keys_part, scaled_part, w_gate, w_up, w_out):
    full_in, full_out = gradients(keys_part, scaled_part, w_gate, w_up, w_out)
    if total is None:
        return full_in, full_out
    return total[0] + full_in, total[1] + full_out


def make_local_ring(ring):
    chips = len(ring)
    cw_perm = []
    ccw_perm = []
    for p in range(chips):
        for c in range(2):
            cw_perm.append((ring[p] * 2 + c, ring[(p + 1) % chips] * 2 + c))
            ccw_perm.append((ring[p] * 2 + c, ring[(p - 1) % chips] * 2 + c))
    swap = [(i, i ^ 1) for i in range(chips * 2)]
    steps = chips // 2
    axes = ("seq", "outer")

    def split(chunks, half):
        keys_parts = []
        scaled_parts = []
        for ch in chunks:
            for j in range(ch.shape[0] // (2 * half)):
                keys_parts.append(ch[2 * j * half:(2 * j + 1) * half])
                scaled_parts.append(ch[(2 * j + 1) * half:(2 * j + 2) * half])
        return jnp.concatenate(keys_parts, axis=0), jnp.concatenate(scaled_parts, axis=0)

    def local_ring(keys, values, queries, learn_rate, w_gate, w_up, w_out):
        hidden = w_gate.shape[1]
        rows = keys.shape[0]
        halves = 2 if rows % 16 == 0 else 1
        half = rows // halves
        scaled = (learn_rate[:, None] * values.astype(jnp.float32)).astype(jnp.bfloat16)
        width = keys.shape[1]
        own = jnp.stack(
            [keys.reshape(halves, half, width), scaled.reshape(halves, half, width)], axis=1
        ).reshape(2 * rows, width)
        sib = lax.ppermute(own, axes, swap)
        total = add_grads(None, *split([own, sib], half), w_gate, w_up, w_out)
        arrived = [own, own]
        pending = None
        for step in range(1, steps + 1):
            last = step == steps and chips % 2 == 0
            if last and halves == 2:
                sent = [lax.ppermute(arrived[0][:2 * half], axes, cw_perm),
                        lax.ppermute(arrived[1][2 * half:], axes, ccw_perm)]
            elif last:
                sent = [lax.ppermute(arrived[0], axes, cw_perm)]
            else:
                sent = [lax.ppermute(arrived[0], axes, cw_perm),
                        lax.ppermute(arrived[1], axes, ccw_perm)]
            arrived = sent
            if step == steps and pending is not None:
                pending, arrived = lax.optimization_barrier((pending, arrived))
            from_sib = [lax.ppermute(chunk, axes, swap) for chunk in arrived]
            if step == steps:
                total = add_grads(total, *split(arrived, half), w_gate, w_up, w_out)
                total = add_grads(total, *split(from_sib, half), w_gate, w_up, w_out)
            elif step == steps - 1:
                pending = gradients(*split(arrived + from_sib, half), w_gate, w_up, w_out)
            else:
                total = add_grads(total, *split(arrived + from_sib, half), w_gate, w_up, w_out)
        if pending is not None:
            total = (total[0] + pending[0], total[1] + pending[1])
        full_in, full_out = total
        new_gate = renorm(w_gate, full_in[:, :hidden])
        new_up = renorm(w_up, full_in[:, hidden:])
        new_out = renorm(w_out, full_out)
        new_gate, new_up, new_out = lax.optimization_barrier((new_gate, new_up, new_out))
        return apply(queries, new_gate, new_up, new_out)

    return local_ring


def solution(mesh):
    placed = (
        P(("grp", "seq", "outer"), None),
        P(("grp", "seq", "outer"), None),
        P(("grp", "seq", "outer"), None),
        P(("grp", "seq", "outer")),
        P("grp", None),
        P("grp", None),
        P("grp", None),
    )
    ring = chip_ring(mesh) if mesh.shape["outer"] == 2 else None
    local_ring = make_local_ring(ring) if ring else None

    def run(keys, values, queries, learn_rate, w_gate, w_up, w_out):
        per_part = keys.shape[0] // mesh.shape["grp"]
        gathered_bytes = 2 * per_part * keys.shape[1] * keys.dtype.itemsize
        if gathered_bytes > GATHER_LIMIT_BYTES:
            body = local_scatter
        elif local_ring is not None:
            body = local_ring
        else:
            body = local_gather
        return jax.shard_map(
            body,
            mesh=mesh,
            in_specs=placed,
            out_specs=P(("grp", "seq", "outer"), None),
            check_vma=False,
        )(keys, values, queries, learn_rate, w_gate, w_up, w_out)

    return run
```

```python
import jax
import jax.numpy as jnp
from jax import lax
from jax.sharding import PartitionSpec as P

epsilon = 1e-06
GATHER_LIMIT_BYTES = 16 * 1024 * 1024


def silu_grad(inputs):
    sigma = jax.nn.sigmoid(inputs)
    return sigma * (1.0 + inputs * (1.0 - sigma))


def renorm(weight, grads):
    old = weight.astype(jnp.float32)
    update = old + grads
    factor = jnp.sqrt(jnp.mean(old * old, axis=1, keepdims=True) + epsilon) / jnp.sqrt(
        jnp.mean(update * update, axis=1, keepdims=True) + epsilon
    )
    return (update * factor).astype(jnp.bfloat16)


contract_last = (((1,), (1,)), ((), ()))
contract_first = (((0,), (0,)), ((), ()))


def gradients(keys, scaled, w_gate, w_up, w_out):
    gate_pre = jnp.dot(keys, w_gate, preferred_element_type=jnp.float32)
    up_pre = jnp.dot(keys, w_up, preferred_element_type=jnp.float32)
    back_grad = lax.dot_general(scaled, w_out, contract_last, preferred_element_type=jnp.float32)
    activation = (jax.nn.silu(gate_pre) * up_pre).astype(jnp.bfloat16)
    d_gate = (back_grad * up_pre * silu_grad(gate_pre)).astype(jnp.bfloat16)
    d_up = (back_grad * jax.nn.silu(gate_pre)).astype(jnp.bfloat16)
    both_grads = jnp.concatenate([d_gate, d_up], axis=1)
    full_in = lax.dot_general(keys, both_grads, contract_first, preferred_element_type=jnp.float32)
    full_out = lax.dot_general(activation, scaled, contract_first, preferred_element_type=jnp.float32)
    return full_in, full_out


def apply(queries, full_gate, full_up, full_out_w):
    q_gate = jnp.dot(queries, full_gate, preferred_element_type=jnp.float32)
    q_up = jnp.dot(queries, full_up, preferred_element_type=jnp.float32)
    q_act = (jax.nn.silu(q_gate) * q_up).astype(jnp.bfloat16)
    return jnp.dot(q_act, full_out_w, preferred_element_type=jnp.float32).astype(jnp.bfloat16)


def local_gather(keys, values, queries, learn_rate, w_gate, w_up, w_out):
    hidden = w_gate.shape[1]
    shards = lax.axis_size(("seq", "outer"))
    rows = keys.shape[0]
    width = keys.shape[1]
    scaled = (learn_rate[:, None] * values.astype(jnp.float32)).astype(jnp.bfloat16)
    both = jnp.concatenate([keys, scaled], axis=0)
    full = lax.all_gather(both, ("seq", "outer"), axis=0, tiled=True)
    full = full.reshape(shards, 2, rows, width)
    all_keys = full[:, 0].reshape(shards * rows, width)
    all_scaled = full[:, 1].reshape(shards * rows, width)
    full_in, full_out = gradients(all_keys, all_scaled, w_gate, w_up, w_out)
    new_gate = renorm(w_gate, full_in[:, :hidden])
    new_up = renorm(w_up, full_in[:, hidden:])
    new_out = renorm(w_out, full_out)
    return apply(queries, new_gate, new_up, new_out)


def local_scatter(keys, values, queries, learn_rate, w_gate, w_up, w_out):
    hidden = w_gate.shape[1]
    shards = lax.axis_size(("seq", "outer"))
    rows_gate = w_gate.shape[0] // shards
    rows_out = w_out.shape[0] // shards
    position = lax.axis_index(("seq", "outer"))
    scaled = (learn_rate[:, None] * values.astype(jnp.float32)).astype(jnp.bfloat16)
    full_in, full_out = gradients(keys, scaled, w_gate, w_up, w_out)
    grad_in = lax.psum_scatter(full_in, ("seq", "outer"), scatter_dimension=0, tiled=True)
    grad_out = lax.psum_scatter(full_out, ("seq", "outer"), scatter_dimension=0, tiled=True)
    own_gate = lax.dynamic_slice_in_dim(w_gate, position * rows_gate, rows_gate, 0)
    own_up = lax.dynamic_slice_in_dim(w_up, position * rows_gate, rows_gate, 0)
    own_out = lax.dynamic_slice_in_dim(w_out, position * rows_out, rows_out, 0)
    new_gate = renorm(own_gate, grad_in[:, :hidden])
    new_up = renorm(own_up, grad_in[:, hidden:])
    new_out = renorm(own_out, grad_out)
    full_gate, full_up, full_out_w = (
        lax.all_gather(new_gate, ("seq", "outer"), axis=0, tiled=True),
        lax.all_gather(new_up, ("seq", "outer"), axis=0, tiled=True),
        lax.all_gather(new_out, ("seq", "outer"), axis=0, tiled=True),
    )
    return apply(queries, full_gate, full_up, full_out_w)


def chip_ring(mesh):
    seq = mesh.shape["seq"]
    try:
        places = [tuple(mesh.devices[0, s, 0].coords) for s in range(seq)]
    except (AttributeError, TypeError):
        return None
    columns = sorted({p[0] for p in places})
    if len(columns) != 2 or len({p[1] for p in places}) != 1:
        return None
    first = sorted((p[2], s) for s, p in enumerate(places) if p[0] == columns[0])
    second = sorted((p[2], s) for s, p in enumerate(places) if p[0] == columns[1])
    order = [s for _, s in first] + [s for _, s in reversed(second)]
    return order[:1] + order[:0:-1]


def add_grads(total, keys_part, scaled_part, w_gate, w_up, w_out):
    full_in, full_out = gradients(keys_part, scaled_part, w_gate, w_up, w_out)
    if total is None:
        return full_in, full_out
    return total[0] + full_in, total[1] + full_out


def make_local_ring(ring):
    chips = len(ring)
    cw_perm = []
    ccw_perm = []
    for p in range(chips):
        for c in range(2):
            cw_perm.append((ring[p] * 2 + c, ring[(p + 1) % chips] * 2 + c))
            ccw_perm.append((ring[p] * 2 + c, ring[(p - 1) % chips] * 2 + c))
    swap = [(i, i ^ 1) for i in range(chips * 2)]
    steps = chips // 2
    axes = ("seq", "outer")

    def split(chunks, half):
        keys_parts = []
        scaled_parts = []
        for ch in chunks:
            for j in range(ch.shape[0] // (2 * half)):
                keys_parts.append(ch[2 * j * half:(2 * j + 1) * half])
                scaled_parts.append(ch[(2 * j + 1) * half:(2 * j + 2) * half])
        return jnp.concatenate(keys_parts, axis=0), jnp.concatenate(scaled_parts, axis=0)

    def local_ring(keys, values, queries, learn_rate, w_gate, w_up, w_out):
        hidden = w_gate.shape[1]
        rows = keys.shape[0]
        halves = 2 if rows % 16 == 0 else 1
        half = rows // halves
        scaled = (learn_rate[:, None] * values.astype(jnp.float32)).astype(jnp.bfloat16)
        width = keys.shape[1]
        own = jnp.stack(
            [keys.reshape(halves, half, width), scaled.reshape(halves, half, width)], axis=1
        ).reshape(2 * rows, width)
        sib = lax.ppermute(own, axes, swap)
        total = add_grads(None, *split([own, sib], half), w_gate, w_up, w_out)
        arrived = [own, own]
        for step in range(1, steps + 1):
            last = step == steps and chips % 2 == 0
            if last and halves == 2:
                sent = [lax.ppermute(arrived[0][:2 * half], axes, cw_perm),
                        lax.ppermute(arrived[1][2 * half:], axes, ccw_perm)]
            elif last:
                sent = [lax.ppermute(arrived[0], axes, cw_perm)]
            else:
                sent = [lax.ppermute(arrived[0], axes, cw_perm),
                        lax.ppermute(arrived[1], axes, ccw_perm)]
            arrived = sent
            if step == steps:
                total, arrived = lax.optimization_barrier((total, arrived))
            from_sib = [lax.ppermute(chunk, axes, swap) for chunk in arrived]
            if step == steps:
                total = add_grads(total, *split(arrived, half), w_gate, w_up, w_out)
                total = add_grads(total, *split(from_sib, half), w_gate, w_up, w_out)
            else:
                total = add_grads(total, *split(arrived + from_sib, half), w_gate, w_up, w_out)
        full_in, full_out = total
        new_gate = renorm(w_gate, full_in[:, :hidden])
        new_up = renorm(w_up, full_in[:, hidden:])
        new_out = renorm(w_out, full_out)
        new_gate, new_up, new_out = lax.optimization_barrier((new_gate, new_up, new_out))
        return apply(queries, new_gate, new_up, new_out)

    return local_ring


def solution(mesh):
    placed = (
        P(("grp", "seq", "outer"), None),
        P(("grp", "seq", "outer"), None),
        P(("grp", "seq", "outer"), None),
        P(("grp", "seq", "outer")),
        P("grp", None),
        P("grp", None),
        P("grp", None),
    )
    ring = chip_ring(mesh) if mesh.shape["outer"] == 2 else None
    local_ring = make_local_ring(ring) if ring else None

    def run(keys, values, queries, learn_rate, w_gate, w_up, w_out):
        per_part = keys.shape[0] // mesh.shape["grp"]
        gathered_bytes = 2 * per_part * keys.shape[1] * keys.dtype.itemsize
        if gathered_bytes > GATHER_LIMIT_BYTES:
            body = local_scatter
        elif local_ring is not None:
            body = local_ring
        else:
            body = local_gather
        return jax.shard_map(
            body,
            mesh=mesh,
            in_specs=placed,
            out_specs=P(("grp", "seq", "outer"), None),
            check_vma=False,
        )(keys, values, queries, learn_rate, w_gate, w_up, w_out)

    return run
```
